128 devices in a mesh: ctx: 32 (over y, x, core), head: 4 (over z).
Axes of the slice: x: 4, y: 4, z: 4, core: 2. Of those that a mesh axis runs over, the one named last changes fastest.
Arguments:
- queries: bfloat16 [8192, 4, 8, 128], P('ctx', 'head'), may hold values from -6 to 6
- keys: bfloat16 [8192, 8, 128], P('ctx'), may hold values from -6 to 6
- values: bfloat16 [8192, 8, 128], P('ctx'), may hold values from -6 to 6
- dout: bfloat16 [8192, 4, 8, 128], P('ctx', 'head'), may hold values from -24 to 24
- signs: int32 [2, 128, 32], replicated, may hold values from 0 to 1
Outputs:
- dq: bfloat16 [8192, 4, 8, 128], P('ctx', 'head')
- dk: bfloat16 [8192, 8, 128], P('ctx', 'head')
- dv: bfloat16 [8192, 8, 128], P('ctx', 'head')
The draws below stay inside these ranges and needn't reach their ends.
All inputs are finite; a program needn't handle non-finite values.
Results may differ from the reference program's by a relative error of at most 0.0075.
Values may be sent and summed in bfloat16 or wider, within the bound.
No kernel may reach another device: no remote copies, remote signals or barrier semaphores. Data moves between devices by JAX's collectives and lax.ppermute only.
A program may use at most 128 MiB of HBM per device.

```python
import jax
import jax.numpy as jnp
from jax import lax

HD = 128
KVH = 8
GROUP = 4
SKETCH = 32
FEAT = 1024
TOK_DEV = 256
TOKENS = 8192


def set_ends(result, stream_key, smallest, top_value):
    dims = result.shape
    place = [jax.random.randint(jax.random.fold_in(stream_key, axis), (), 0, dims[axis]) for axis in range(len(dims))]
    result = result.at[tuple(place)].set(smallest)
    longest = dims.index(max(dims))
    place[longest] = (place[longest] + 1) % dims[longest]
    return result.at[tuple(place)].set(top_value)


def block_scale(stream_key, shape, split, smallest, largest):
    def one(axis_at, blocks):
        heights = jax.random.uniform(jax.random.fold_in(jax.random.fold_in(stream_key, 6), axis_at), (blocks,), jnp.float32, smallest / len(split), largest / len(split))
        return jnp.repeat(jnp.exp(heights), shape[axis_at] // blocks).reshape((-1,) + (1,) * (len(shape) - axis_at - 1))

    gain = one(*split[0])
    for cut in split[1:]:
        gain = gain * one(*cut)
    return gain


def bell_draw(stream_key, shape, scale, reach, cuts=(), dtype=jnp.bfloat16):
    result = jax.random.normal(stream_key, shape, jnp.float32) * scale
    if len(cuts) > 0:
        result = block_scale(stream_key, shape, cuts, -0.22, 0.18) * result
    return jnp.clip(result, min=-reach, max=reach).astype(dtype)


def setup_inputs(seed: int = 0) -> dict:
    streams_of = jax.random.split(jax.random.key(seed), 6)
    queries = bell_draw(streams_of[0], (TOKENS, GROUP, KVH, HD), 1.0, 6.0, ((0, 32), (1, 4)))
    keys = bell_draw(streams_of[1], (TOKENS, KVH, HD), 1.0, 6.0, ((0, 32),))
    values = bell_draw(streams_of[2], (TOKENS, KVH, HD), 1.0, 6.0, ((0, 32),))
    dout = bell_draw(streams_of[3], (TOKENS, GROUP, KVH, HD), 4.0, 24.0, ((0, 32), (1, 4)))
    signs = set_ends(jax.random.randint(streams_of[4], (2, HD, SKETCH), 0, 2), jax.random.fold_in(streams_of[4], 1), 0, 1).astype(jnp.int32)
    return dict(queries=queries, keys=keys, values=values, dout=dout, signs=signs)


highest = lax.Precision.HIGHEST


def matmul(pattern, first, second):
    return jnp.einsum(pattern, first.astype(jnp.float32), second.astype(jnp.float32), precision=highest)


def sketch_parts(tokens, projector, pattern):
    inverse = tokens.shape[-1] ** -0.5
    sketch_one = matmul(pattern, tokens, projector[0]) * inverse
    sketch_two = matmul(pattern, tokens, projector[1]) * inverse
    return sketch_one, sketch_two


def features(sketch_one, sketch_two):
    width = sketch_one.shape[-1]
    sketch = sketch_one * sketch_two
    outer = sketch[..., :, None] * sketch[..., None, :] * (1.0 / width)
    return outer.reshape(sketch.shape[:-1] + (width * width,)).astype(jnp.bfloat16)


def feature_back(cotangent, sketch_one, sketch_two, proj_wide):
    width = sketch_one.shape[-1]
    sketch = sketch_one * sketch_two
    square = cotangent.reshape(cotangent.shape[:-1] + (width, width))
    dsketch = (jnp.einsum('...ab,...b->...a', square, sketch, precision=highest) + jnp.einsum('...ab,...a->...b', square, sketch, precision=highest)) * (1.0 / width)
    back_one = jnp.einsum('...f,df->...d', dsketch * sketch_two, proj_wide[0], precision=highest)
    back_two = jnp.einsum('...f,df->...d', dsketch * sketch_one, proj_wide[1], precision=highest)
    return (back_one + back_two) * proj_wide.shape[1] ** -0.5


def head_step(inputs):
    key_feat, value_head, state_in, total_in, query_feat, grad_out = inputs
    length = key_feat.shape[0]
    causal = lax.broadcasted_iota(jnp.int32, (length, length), 0) >= lax.broadcasted_iota(jnp.int32, (length, length), 1)

    def member(query_one, grad_one):
        scores = jnp.where(causal, matmul('if,jf->ij', query_one, key_feat), 0.0)
        weights = scores.astype(jnp.bfloat16)
        query_wide = query_one.astype(jnp.float32)
        numerator = matmul('ij,jd->id', weights, value_head) + jnp.dot(query_wide, state_in, precision=highest)
        denominator = 1.0 + jnp.sum(scores, 1) + jnp.dot(query_wide, total_in, precision=highest)
        output_rows = numerator / denominator[:, None]
        grad_rows = grad_one.astype(jnp.float32) / denominator[:, None]
        grad_low = grad_rows.astype(jnp.bfloat16)
        correction = -jnp.sum(grad_rows * output_rows, 1)
        dscores = jnp.where(causal, matmul('id,jd->ij', grad_low, value_head) + correction[:, None], 0.0).astype(jnp.bfloat16)
        grad_qfeat = matmul('ij,jf->if', dscores, key_feat) + jnp.dot(grad_rows, state_in.T, precision=highest) + correction[:, None] * total_in[None, :]
        grad_kfeat = matmul('ij,if->jf', dscores, query_one)
        grad_value = matmul('ij,id->jd', weights, grad_low)
        suffix_part = matmul('if,id->fd', query_one, grad_low)
        suffix_sum = jnp.dot(correction, query_wide, precision=highest)
        return grad_qfeat, grad_kfeat, grad_value, suffix_part, suffix_sum

    results = jax.vmap(member)(query_feat, grad_out)
    return results[0], jnp.sum(results[1], 0), jnp.sum(results[2], 0), results[3], results[4]


def add_states(running_sum, block_term):
    updated = (running_sum[0] + block_term[0], running_sum[1] + block_term[1])
    return updated, running_sum


def reference(queries, keys, values, dout, signs):
    projector = (2 * signs - 1).astype(jnp.bfloat16)
    proj_wide = projector.astype(jnp.float32)
    blocks = TOKENS // TOK_DEV
    query_blocks = queries.reshape(blocks, TOK_DEV, GROUP, KVH, HD)
    key_blocks = keys.reshape(blocks, TOK_DEV, KVH, HD)
    value_blocks = values.reshape(blocks, TOK_DEV, KVH, HD)
    grad_blocks = dout.reshape(blocks, TOK_DEV, GROUP, KVH, HD)

    def block_totals(block_pair):
        key_blk, value_blk = block_pair
        sketch_one, sketch_two = sketch_parts(key_blk, projector, 'thd,df->htf')
        key_feat = features(sketch_one, sketch_two)
        value_heads = value_blk.transpose(1, 0, 2)
        return matmul('htf,htd->hfd', key_feat, value_heads), jnp.sum(key_feat.astype(jnp.float32), 1)

    totals = lax.map(block_totals, (key_blocks, value_blocks))
    start_states = (jnp.zeros((KVH, FEAT, HD), jnp.float32), jnp.zeros((KVH, FEAT), jnp.float32))
    final_state, prefix = lax.scan(add_states, start_states, totals)

    def forward_block(block_items):
        query_blk, key_blk, value_blk, grad_blk, state_in, total_in = block_items
        key_one, key_two = sketch_parts(key_blk, projector, 'thd,df->htf')
        key_feat = features(key_one, key_two)
        query_one, query_two = sketch_parts(query_blk, projector, 'tmhd,df->hmtf')
        query_feat = features(query_one, query_two)
        value_heads = value_blk.transpose(1, 0, 2)
        grad_heads = grad_blk.transpose(2, 1, 0, 3)
        grad_qfeat, grad_kfeat, grad_value, suffix_part, suffix_sum = lax.map(head_step, (key_feat, value_heads, state_in, total_in, query_feat, grad_heads))
        query_grad = feature_back(grad_qfeat, query_one, query_two, proj_wide)
        return query_grad.transpose(2, 1, 0, 3).astype(jnp.bfloat16), grad_kfeat, grad_value, suffix_part, suffix_sum

    dq_blocks, grad_kfeat, grad_value, suffix_part, suffix_sum = lax.map(forward_block, (query_blocks, key_blocks, value_blocks, grad_blocks, prefix[0], prefix[1]))
    start_suffix = (jnp.zeros((KVH, GROUP, FEAT, HD), jnp.float32), jnp.zeros((KVH, GROUP, FEAT), jnp.float32))
    final_suffix, suffix = lax.scan(add_states, start_suffix, (suffix_part, suffix_sum), reverse=True)

    def backward_block(block_items):
        key_blk, value_blk, grad_kblk, grad_vblk, suffix_state, suffix_total = block_items
        key_one, key_two = sketch_parts(key_blk, projector, 'thd,df->htf')
        key_feat = features(key_one, key_two)
        value_heads = value_blk.transpose(1, 0, 2)
        merged_state = jnp.sum(suffix_state, 1)
        merged_total = jnp.sum(suffix_total, 1)
        kfeat_total = grad_kblk + jnp.einsum('htd,hfd->htf', value_heads.astype(jnp.float32), merged_state, precision=highest) + merged_total[:, None, :]
        value_total = grad_vblk + jnp.einsum('htf,hfd->htd', key_feat.astype(jnp.float32), merged_state, precision=highest)
        key_grad = feature_back(kfeat_total, key_one, key_two, proj_wide)
        return key_grad.transpose(1, 0, 2).astype(jnp.bfloat16), value_total.transpose(1, 0, 2).astype(jnp.bfloat16)

    dk_blocks, dv_blocks = lax.map(backward_block, (key_blocks, value_blocks, grad_kfeat, grad_value, suffix[0], suffix[1]))
    return (dq_blocks.reshape(TOKENS, GROUP, KVH, HD), dk_blocks.reshape(TOKENS, KVH, HD), dv_blocks.reshape(TOKENS, KVH, HD))
```

```python
import jax
import jax.numpy as jnp
from jax import lax
from jax.sharding import PartitionSpec as P

highest = lax.Precision.HIGHEST
f32 = jnp.float32
bf16 = jnp.bfloat16


def split2(x):
    hi = x.astype(bf16)
    lo = (x - hi.astype(f32)).astype(bf16)
    return hi, lo


def dot_split(pattern, exact, wide):
    hi, lo = split2(wide)
    return jnp.einsum(pattern, exact, hi, preferred_element_type=f32) + jnp.einsum(
        pattern, exact, lo, preferred_element_type=f32
    )


def dot_split3(pattern, first, second):
    fh, fl = split2(first)
    sh, sl = split2(second)
    return (
        jnp.einsum(pattern, fh, sh, preferred_element_type=f32)
        + jnp.einsum(pattern, fh, sl, preferred_element_type=f32)
        + jnp.einsum(pattern, fl, sh, preferred_element_type=f32)
    )


def ctx_scan(state, total, reverse):
    n = lax.axis_size("ctx")
    heads, feat, width = state.shape
    total_rows = feat // width
    rows = feat + total_rows
    per_head = n // heads
    unit = per_head * 8
    padded = -(-rows // unit) * unit
    comb = jnp.concatenate(
        [
            state,
            total.reshape(heads, total_rows, width),
            jnp.zeros((heads, padded - rows, width), f32),
        ],
        axis=1,
    )
    chunks = comb.reshape(n, padded // per_head, width)
    got = lax.all_to_all(chunks, "ctx", 0, 0, tiled=True)
    src = lax.broadcasted_iota(jnp.int32, (n, n), 1)
    dst = lax.broadcasted_iota(jnp.int32, (n, n), 0)
    mask = (src > dst if reverse else src < dst).astype(f32)
    summed = jnp.einsum("ij,jrc->irc", mask, got, precision=highest)
    back = lax.all_to_all(summed, "ctx", 0, 0, tiled=True)
    comb_out = back.reshape(heads, padded, width)
    return comb_out[:, :feat], comb_out[:, feat:rows].reshape(heads, feat)


def sketch_parts(tokens, projector, pattern):
    inverse = tokens.shape[-1] ** (-0.5)
    sketch_one = jnp.einsum(pattern, tokens, projector[0], preferred_element_type=f32) * inverse
    sketch_two = jnp.einsum(pattern, tokens, projector[1], preferred_element_type=f32) * inverse
    return (sketch_one, sketch_two)


def features(sketch_one, sketch_two):
    width = sketch_one.shape[-1]
    sketch = sketch_one * sketch_two
    outer = sketch[..., :, None] * sketch[..., None, :] * (1.0 / width)
    return outer.reshape(sketch.shape[:-1] + (width * width,)).astype(bf16)


def feature_back(cotangent, sketch_one, sketch_two, proj_wide):
    width = sketch_one.shape[-1]
    sketch = sketch_one * sketch_two
    square = cotangent.reshape(cotangent.shape[:-1] + (width, width))
    dsketch = (
        jnp.einsum("...ab,...b->...a", square, sketch, precision=highest)
        + jnp.einsum("...ab,...a->...b", square, sketch, precision=highest)
    ) * (1.0 / width)
    back_one = jnp.einsum("...f,df->...d", dsketch * sketch_two, proj_wide[0], precision=highest)
    back_two = jnp.einsum("...f,df->...d", dsketch * sketch_one, proj_wide[1], precision=highest)
    return (back_one + back_two) * proj_wide.shape[1] ** (-0.5)


def body(queries, keys, values, dout, signs):
    projector = (2 * signs - 1).astype(bf16)
    proj_wide = projector.astype(f32)
    heads_all = keys.shape[1]
    owned = heads_all // lax.axis_size("head")
    offset = lax.axis_index("head") * owned
    key_part = lax.dynamic_slice_in_dim(keys, offset, owned, 1)
    value_part = lax.dynamic_slice_in_dim(values, offset, owned, 1)
    query_part = lax.all_to_all(queries, "head", split_axis=2, concat_axis=1, tiled=True)
    grad_part = lax.all_to_all(dout, "head", split_axis=2, concat_axis=1, tiled=True)
    key_one, key_two = sketch_parts(key_part, projector, "thd,df->htf")
    key_feat = features(key_one, key_two)
    value_heads = value_part.transpose(1, 0, 2)
    block_state = jnp.einsum("htf,htd->hfd", key_feat, value_heads, preferred_element_type=f32)
    block_total = jnp.sum(key_feat, 1, dtype=f32)
    state_in, total_in = ctx_scan(block_state, block_total, False)

    query_one, query_two = sketch_parts(query_part, projector, "tmhd,df->hmtf")
    query_feat = features(query_one, query_two)
    grad_heads = grad_part.transpose(2, 1, 0, 3).astype(f32)
    length = key_feat.shape[1]
    causal = lax.broadcasted_iota(jnp.int32, (length, length), 0) >= lax.broadcasted_iota(
        jnp.int32, (length, length), 1
    )
    scores = jnp.where(
        causal, jnp.einsum("hmif,hjf->hmij", query_feat, key_feat, preferred_element_type=f32), 0.0
    )
    weights = scores.astype(bf16)
    numerator = jnp.einsum(
        "hmij,hjd->hmid", weights, value_heads, preferred_element_type=f32
    ) + dot_split("hmif,hfd->hmid", query_feat, state_in)
    denominator = 1.0 + jnp.sum(scores, -1) + dot_split("hmif,hf->hmi", query_feat, total_in)
    output_rows = numerator / denominator[..., None]
    grad_rows = grad_heads / denominator[..., None]
    grad_low = grad_rows.astype(bf16)
    correction = -jnp.sum(grad_rows * output_rows, -1)
    suffix_part = jnp.einsum("hmif,hmid->hfd", query_feat, grad_low, preferred_element_type=f32)
    suffix_sum = dot_split("hmif,hmi->hf", query_feat, correction)
    merged_state, merged_total = ctx_scan(suffix_part, suffix_sum, True)

    dscores = jnp.where(
        causal,
        jnp.einsum("hmid,hjd->hmij", grad_low, value_heads, preferred_element_type=f32)
        + correction[..., None],
        0.0,
    ).astype(bf16)
    grad_qfeat = (
        jnp.einsum("hmij,hjf->hmif", dscores, key_feat, preferred_element_type=f32)
        + dot_split3("hmid,hfd->hmif", grad_rows, state_in)
        + correction[..., None] * total_in[:, None, None, :]
    )
    query_grad = feature_back(grad_qfeat, query_one, query_two, proj_wide)
    query_low = query_grad.transpose(2, 1, 0, 3).astype(bf16)
    query_out = lax.all_to_all(query_low, "head", split_axis=1, concat_axis=2, tiled=True)

    grad_kfeat = jnp.einsum("hmij,hmif->hjf", dscores, query_feat, preferred_element_type=f32)
    grad_value = jnp.einsum("hmij,hmid->hjd", weights, grad_low, preferred_element_type=f32)
    kfeat_total = (
        grad_kfeat
        + dot_split("htd,hfd->htf", value_heads, merged_state)
        + merged_total[:, None, :]
    )
    value_total = grad_value + dot_split("htf,hfd->htd", key_feat, merged_state)
    key_sum = feature_back(kfeat_total, key_one, key_two, proj_wide)
    key_out = key_sum.transpose(1, 0, 2).astype(bf16)
    value_out = value_total.transpose(1, 0, 2).astype(bf16)
    return (query_out, key_out, value_out)


def solution(mesh):
    in_specs = (
        P("ctx", "head", None, None),
        P("ctx", None, None),
        P("ctx", None, None),
        P("ctx", "head", None, None),
        P(),
    )
    out_specs = (P("ctx", "head", None, None), P("ctx", "head", None), P("ctx", "head", None))
    return jax.shard_map(body, mesh=mesh, in_specs=in_specs, out_specs=out_specs, check_vma=False)
```

```python
import jax
import jax.numpy as jnp
import numpy as np
from jax import lax
from jax.sharding import PartitionSpec as P

highest = lax.Precision.HIGHEST
f32 = jnp.float32
bf16 = jnp.bfloat16


def triangle(width):
    rows, cols = np.triu_indices(width)
    take_a = np.eye(width, dtype=np.float32)[:, rows]
    take_b = np.eye(width, dtype=np.float32)[:, cols]
    weight = np.where(rows == cols, 1.0, 2.0).astype(np.float32)
    off = (rows != cols).astype(np.float32)
    return take_a, take_b, weight, off


def split_parts(x, count):
    parts = []
    rest = x
    for _ in range(count - 1):
        hi = lax.reduce_precision(rest, exponent_bits=8, mantissa_bits=7)
        parts.append(hi.astype(bf16))
        rest = rest - hi
    parts.append(rest.astype(bf16))
    return parts


def dot_parts(pattern, wide, other, count, wide_first=True):
    total = None
    for part in split_parts(wide, count):
        args = (part, other) if wide_first else (other, part)
        term = jnp.einsum(pattern, *args, preferred_element_type=f32)
        total = term if total is None else total + term
    return total


def dot_split(pattern, exact, wide):
    return dot_parts(pattern, wide, exact, 2, wide_first=False)


def dot_split3(pattern, first, second):
    fh, fl = split_parts(first, 2)
    sh, sl = split_parts(second, 2)
    return (
        jnp.einsum(pattern, fh, sh, preferred_element_type=f32)
        + jnp.einsum(pattern, fh, sl, preferred_element_type=f32)
        + jnp.einsum(pattern, fl, sh, preferred_element_type=f32)
    )


def take_exact(x, select):
    return dot_parts("...a,ak->...k", x, select, 3)


def ctx_scan(state, total, reverse):
    n = lax.axis_size("ctx")
    heads, feat, width = state.shape
    total_rows = -(-feat // width)
    flat = jnp.concatenate(
        [
            state.reshape(heads * feat, width),
            jnp.pad(total, ((0, 0), (0, total_rows * width - feat))).reshape(
                heads * total_rows, width
            ),
        ],
        axis=0,
    )
    rows = flat.shape[0]
    per = -(-rows // (n * 8)) * 8
    flat = jnp.pad(flat, ((0, n * per - rows), (0, 0)))
    got = lax.all_to_all(flat.reshape(n, per, width), "ctx", 0, 0, tiled=True)
    src = lax.broadcasted_iota(jnp.int32, (n, n), 1)
    dst = lax.broadcasted_iota(jnp.int32, (n, n), 0)
    mask = (src > dst if reverse else src < dst).astype(f32)
    summed = jnp.einsum("ij,jrc->irc", mask, got, precision=highest)
    back = lax.all_to_all(summed, "ctx", 0, 0, tiled=True).reshape(n * per, width)
    state_out = back[: heads * feat].reshape(heads, feat, width)
    total_out = back[heads * feat : heads * (feat + total_rows)].reshape(heads, total_rows * width)
    return state_out, total_out[:, :feat]


def sketch_parts(tokens, projector, pattern):
    inverse = tokens.shape[-1] ** (-0.5)
    sketch_one = jnp.einsum(pattern, tokens, projector[0], preferred_element_type=f32) * inverse
    sketch_two = jnp.einsum(pattern, tokens, projector[1], preferred_element_type=f32) * inverse
    return (sketch_one, sketch_two)


def tri_features(sketch_one, sketch_two, take_a, take_b):
    width = sketch_one.shape[-1]
    sketch = sketch_one * sketch_two
    first = take_exact(sketch, take_a)
    second = take_exact(sketch, take_b)
    return (first * second * (1.0 / width)).astype(bf16)


def tri_feature_back(cotangent, sketch_one, sketch_two, proj_wide, take_a, take_b, off):
    width = sketch_one.shape[-1]
    sketch = sketch_one * sketch_two
    first = take_exact(sketch, take_a)
    second = take_exact(sketch, take_b)
    spread = jnp.concatenate([cotangent * second, cotangent * first * off], axis=-1)
    gather = jnp.concatenate([take_a.T, take_b.T], axis=0).astype(bf16)
    dsketch = dot_parts("...k,ka->...a", spread, gather, 2) * (2.0 / width)
    back_one = jnp.einsum("...f,df->...d", dsketch * sketch_two, proj_wide[0], precision=highest)
    back_two = jnp.einsum("...f,df->...d", dsketch * sketch_one, proj_wide[1], precision=highest)
    return (back_one + back_two) * proj_wide.shape[1] ** (-0.5)


def body(queries, keys, values, dout, signs):
    projector = (2 * signs - 1).astype(bf16)
    proj_wide = projector.astype(f32)
    width = signs.shape[-1]
    take_a_np, take_b_np, weight_np, off_np = triangle(width)
    take_a = jnp.asarray(take_a_np, bf16)
    take_b = jnp.asarray(take_b_np, bf16)
    weight = jnp.asarray(weight_np, bf16)
    off = jnp.asarray(off_np, f32)
    heads_all = keys.shape[1]
    owned = heads_all // lax.axis_size("head")
    offset = lax.axis_index("head") * owned
    key_part = lax.dynamic_slice_in_dim(keys, offset, owned, 1)
    value_part = lax.dynamic_slice_in_dim(values, offset, owned, 1)
    both = lax.all_to_all(
        jnp.stack([queries, dout]), "head", split_axis=3, concat_axis=2, tiled=True
    )
    query_part, grad_part = both[0], both[1]
    key_one, key_two = sketch_parts(key_part, projector, "thd,df->htf")
    key_feat = tri_features(key_one, key_two, take_a, take_b)
    key_wfeat = key_feat * weight
    value_heads = value_part.transpose(1, 0, 2)
    block_state = jnp.einsum("htf,htd->hfd", key_feat, value_heads, preferred_element_type=f32)
    block_total = jnp.sum(key_feat, 1, dtype=f32)
    state_in, total_in = ctx_scan(block_state, block_total, False)

    query_one, query_two = sketch_parts(query_part, projector, "tmhd,df->hmtf")
    query_feat = tri_features(query_one, query_two, take_a, take_b)
    query_wfeat = query_feat * weight
    grad_heads = grad_part.transpose(2, 1, 0, 3).astype(f32)
    length = key_feat.shape[1]
    causal = lax.broadcasted_iota(jnp.int32, (length, length), 0) >= lax.broadcasted_iota(
        jnp.int32, (length, length), 1
    )
    scores = jnp.where(
        causal,
        jnp.einsum("hmif,hjf->hmij", query_wfeat, key_feat, preferred_element_type=f32),
        0.0,
    )
    weights = scores.astype(bf16)
    numerator = jnp.einsum(
        "hmij,hjd->hmid", weights, value_heads, preferred_element_type=f32
    ) + dot_split("hmif,hfd->hmid", query_wfeat, state_in)
    denominator = 1.0 + jnp.sum(scores, -1) + dot_split("hmif,hf->hmi", query_wfeat, total_in)
    output_rows = numerator / denominator[..., None]
    grad_rows = grad_heads / denominator[..., None]
    grad_low = grad_rows.astype(bf16)
    correction = -jnp.sum(grad_rows * output_rows, -1)
    suffix_part = jnp.einsum("hmif,hmid->hfd", query_feat, grad_low, preferred_element_type=f32)
    suffix_sum = dot_split("hmif,hmi->hf", query_feat, correction)
    merged_state, merged_total = ctx_scan(suffix_part, suffix_sum, True)

    dscores = jnp.where(
        causal,
        jnp.einsum("hmid,hjd->hmij", grad_low, value_heads, preferred_element_type=f32)
        + correction[..., None],
        0.0,
    ).astype(bf16)
    grad_qfeat = (
        jnp.einsum("hmij,hjf->hmif", dscores, key_feat, preferred_element_type=f32)
        + dot_split3("hmid,hfd->hmif", grad_rows, state_in)
        + correction[..., None] * total_in[:, None, None, :]
    )
    query_grad = tri_feature_back(
        grad_qfeat, query_one, query_two, proj_wide, take_a, take_b, off
    )
    query_low = query_grad.transpose(2, 1, 0, 3).astype(bf16)
    query_out = lax.all_to_all(query_low, "head", split_axis=1, concat_axis=2, tiled=True)

    grad_kfeat = jnp.einsum("hmij,hmif->hjf", dscores, query_feat, preferred_element_type=f32)
    grad_value = jnp.einsum("hmij,hmid->hjd", weights, grad_low, preferred_element_type=f32)
    kfeat_total = (
        grad_kfeat
        + dot_split("htd,hfd->htf", value_heads, merged_state)
        + merged_total[:, None, :]
    )
    value_total = grad_value + dot_split("htf,hfd->htd", key_wfeat, merged_state)
    key_sum = tri_feature_back(kfeat_total, key_one, key_two, proj_wide, take_a, take_b, off)
    key_out = key_sum.transpose(1, 0, 2).astype(bf16)
    value_out = value_total.transpose(1, 0, 2).astype(bf16)
    return (query_out, key_out, value_out)


def solution(mesh):
    in_specs = (
        P("ctx", "head", None, None),
        P("ctx", None, None),
        P("ctx", None, None),
        P("ctx", "head", None, None),
        P(),
    )
    out_specs = (P("ctx", "head", None, None), P("ctx", "head", None), P("ctx", "head", None))
    return jax.shard_map(body, mesh=mesh, in_specs=in_specs, out_specs=out_specs, check_vma=False)
```

```python
import jax
import jax.numpy as jnp
import numpy as np
from jax import lax
from jax.sharding import PartitionSpec as P

highest = lax.Precision.HIGHEST
f32 = jnp.float32
bf16 = jnp.bfloat16


def triangle(width):
    rows, cols = np.triu_indices(width)
    take_a = np.eye(width, dtype=np.float32)[:, rows]
    take_b = np.eye(width, dtype=np.float32)[:, cols]
    weight = np.where(rows == cols, 1.0, 2.0).astype(np.float32)
    off = (rows != cols).astype(np.float32)
    return take_a, take_b, weight, off


def split_parts(x, count):
    parts = []
    rest = x
    for _ in range(count - 1):
        hi = lax.reduce_precision(rest, exponent_bits=8, mantissa_bits=7)
        parts.append(hi.astype(bf16))
        rest = rest - hi
    parts.append(rest.astype(bf16))
    return parts


def dot_parts(pattern, wide, other, count, wide_first=True):
    total = None
    for part in split_parts(wide, count):
        args = (part, other) if wide_first else (other, part)
        term = jnp.einsum(pattern, *args, preferred_element_type=f32)
        total = term if total is None else total + term
    return total


def dot_split(pattern, exact, wide):
    return dot_parts(pattern, wide, exact, 2, wide_first=False)


def dot_split3(pattern, first, second):
    fh, fl = split_parts(first, 2)
    sh, sl = split_parts(second, 2)
    return (
        jnp.einsum(pattern, fh, sh, preferred_element_type=f32)
        + jnp.einsum(pattern, fh, sl, preferred_element_type=f32)
        + jnp.einsum(pattern, fl, sh, preferred_element_type=f32)
    )


def take_exact(x, select):
    return dot_parts("...a,ak->...k", x, select, 3)


def ctx_scan(state, total, reverse):
    n = lax.axis_size("ctx")
    heads, feat, width = state.shape
    total_rows = -(-feat // width)
    flat = jnp.concatenate(
        [
            state.reshape(heads * feat, width),
            jnp.pad(total, ((0, 0), (0, total_rows * width - feat))).reshape(
                heads * total_rows, width
            ),
        ],
        axis=0,
    )
    rows = flat.shape[0]
    per = -(-rows // (n * 8)) * 8
    flat = jnp.pad(flat, ((0, n * per - rows), (0, 0)))
    got = lax.all_to_all(flat.reshape(n, per, width), "ctx", 0, 0, tiled=True)
    src = lax.broadcasted_iota(jnp.int32, (n, n), 1)
    dst = lax.broadcasted_iota(jnp.int32, (n, n), 0)
    mask = (src > dst if reverse else src < dst).astype(f32)
    summed = jnp.einsum("ij,jrc->irc", mask, got, precision=highest)
    back = lax.all_to_all(summed, "ctx", 0, 0, tiled=True).reshape(n * per, width)
    state_out = back[: heads * feat].reshape(heads, feat, width)
    total_out = back[heads * feat : heads * (feat + total_rows)].reshape(heads, total_rows * width)
    return state_out, total_out[:, :feat]


def head_exchange(stacked, owned):
    count = lax.axis_size("head")
    me = lax.axis_index("head")
    pieces = []
    for k in range(count):
        target = (me + k) % count
        piece = lax.dynamic_slice_in_dim(stacked, target * owned, owned, axis=3)
        if k:
            piece = lax.ppermute(piece, "head", [(j, (j + k) % count) for j in range(count)])
        pieces.append(piece)
    return jnp.concatenate(pieces, axis=2)


def head_return(grads, heads_all):
    count = lax.axis_size("head")
    me = lax.axis_index("head")
    owned = grads.shape[2]
    out = jnp.zeros((grads.shape[0], 1, heads_all, grads.shape[3]), grads.dtype)
    for k in range(count):
        piece = grads[:, k : k + 1]
        if k:
            piece = lax.ppermute(piece, "head", [(j, (j - k) % count) for j in range(count)])
        out = lax.dynamic_update_slice_in_dim(out, piece, ((me + k) % count) * owned, axis=2)
    return out


def sketch_parts(tokens, projector, pattern):
    inverse = tokens.shape[-1] ** (-0.5)
    sketch_one = jnp.einsum(pattern, tokens, projector[0], preferred_element_type=f32) * inverse
    sketch_two = jnp.einsum(pattern, tokens, projector[1], preferred_element_type=f32) * inverse
    return (sketch_one, sketch_two)


def tri_features(sketch_one, sketch_two, take_a, take_b):
    width = sketch_one.shape[-1]
    sketch = sketch_one * sketch_two
    first = take_exact(sketch, take_a)
    second = take_exact(sketch, take_b)
    return (first * second * (1.0 / width)).astype(bf16)


def tri_feature_back(cotangent, sketch_one, sketch_two, proj_wide, take_a, take_b, off):
    width = sketch_one.shape[-1]
    sketch = sketch_one * sketch_two
    first = take_exact(sketch, take_a)
    second = take_exact(sketch, take_b)
    spread = jnp.concatenate([cotangent * second, cotangent * first * off], axis=-1)
    gather = jnp.concatenate([take_a.T, take_b.T], axis=0).astype(bf16)
    dsketch = dot_parts("...k,ka->...a", spread, gather, 2) * (2.0 / width)
    back_one = jnp.einsum("...f,df->...d", dsketch * sketch_two, proj_wide[0], precision=highest)
    back_two = jnp.einsum("...f,df->...d", dsketch * sketch_one, proj_wide[1], precision=highest)
    return (back_one + back_two) * proj_wide.shape[1] ** (-0.5)


def body(queries, keys, values, dout, signs):
    projector = (2 * signs - 1).astype(bf16)
    proj_wide = projector.astype(f32)
    width = signs.shape[-1]
    take_a_np, take_b_np, weight_np, off_np = triangle(width)
    take_a = jnp.asarray(take_a_np, bf16)
    take_b = jnp.asarray(take_b_np, bf16)
    weight = jnp.asarray(weight_np, bf16)
    off = jnp.asarray(off_np, f32)
    heads_all = keys.shape[1]
    owned = heads_all // lax.axis_size("head")
    offset = lax.axis_index("head") * owned
    key_part = lax.dynamic_slice_in_dim(keys, offset, owned, 1)
    value_part = lax.dynamic_slice_in_dim(values, offset, owned, 1)
    both = head_exchange(jnp.stack([queries, dout]), owned)
    query_part, grad_part = both[0], both[1]
    key_one, key_two = sketch_parts(key_part, projector, "thd,df->htf")
    key_feat = tri_features(key_one, key_two, take_a, take_b)
    key_wfeat = key_feat * weight
    value_heads = value_part.transpose(1, 0, 2)
    block_state = jnp.einsum("htf,htd->hfd", key_feat, value_heads, preferred_element_type=f32)
    block_total = jnp.sum(key_feat, 1, dtype=f32)
    state_in, total_in = ctx_scan(block_state, block_total, False)

    query_one, query_two = sketch_parts(query_part, projector, "tmhd,df->hmtf")
    query_feat = tri_features(query_one, query_two, take_a, take_b)
    query_wfeat = query_feat * weight
    grad_heads = grad_part.transpose(2, 1, 0, 3).astype(f32)
    length = key_feat.shape[1]
    causal = lax.broadcasted_iota(jnp.int32, (length, length), 0) >= lax.broadcasted_iota(
        jnp.int32, (length, length), 1
    )
    scores = jnp.where(
        causal,
        jnp.einsum("hmif,hjf->hmij", query_wfeat, key_feat, preferred_element_type=f32),
        0.0,
    )
    weights = scores.astype(bf16)
    numerator = jnp.einsum(
        "hmij,hjd->hmid", weights, value_heads, preferred_element_type=f32
    ) + dot_split("hmif,hfd->hmid", query_wfeat, state_in)
    denominator = 1.0 + jnp.sum(scores, -1) + dot_split("hmif,hf->hmi", query_wfeat, total_in)
    output_rows = numerator / denominator[..., None]
    grad_rows = grad_heads / denominator[..., None]
    grad_low = grad_rows.astype(bf16)
    correction = -jnp.sum(grad_rows * output_rows, -1)
    suffix_part = jnp.einsum("hmif,hmid->hfd", query_feat, grad_low, preferred_element_type=f32)
    suffix_sum = dot_split("hmif,hmi->hf", query_feat, correction)
    merged_state, merged_total = ctx_scan(suffix_part, suffix_sum, True)

    dscores = jnp.where(
        causal,
        jnp.einsum("hmid,hjd->hmij", grad_low, value_heads, preferred_element_type=f32)
        + correction[..., None],
        0.0,
    ).astype(bf16)
    grad_qfeat = (
        jnp.einsum("hmij,hjf->hmif", dscores, key_feat, preferred_element_type=f32)
        + dot_split3("hmid,hfd->hmif", grad_rows, state_in)
        + correction[..., None] * total_in[:, None, None, :]
    )
    query_grad = tri_feature_back(
        grad_qfeat, query_one, query_two, proj_wide, take_a, take_b, off
    )
    query_low = query_grad.transpose(2, 1, 0, 3).astype(bf16)
    query_out = head_return(query_low, heads_all)

    grad_kfeat = jnp.einsum("hmij,hmif->hjf", dscores, query_feat, preferred_element_type=f32)
    grad_value = jnp.einsum("hmij,hmid->hjd", weights, grad_low, preferred_element_type=f32)
    kfeat_total = (
        grad_kfeat
        + dot_split("htd,hfd->htf", value_heads, merged_state)
        + merged_total[:, None, :]
    )
    value_total = grad_value + dot_split("htf,hfd->htd", key_wfeat, merged_state)
    key_sum = tri_feature_back(kfeat_total, key_one, key_two, proj_wide, take_a, take_b, off)
    key_out = key_sum.transpose(1, 0, 2).astype(bf16)
    value_out = value_total.transpose(1, 0, 2).astype(bf16)
    return (query_out, key_out, value_out)


def solution(mesh):
    in_specs = (
        P("ctx", "head", None, None),
        P("ctx", None, None),
        P("ctx", None, None),
        P("ctx", "head", None, None),
        P(),
    )
    out_specs = (P("ctx", "head", None, None), P("ctx", "head", None), P("ctx", "head", None))
    return jax.shard_map(body, mesh=mesh, in_specs=in_specs, out_specs=out_specs, check_vma=False)
```

```python
import jax
import jax.numpy as jnp
import numpy as np
from jax import lax
from jax.sharding import PartitionSpec as P

highest = lax.Precision.HIGHEST
f32 = jnp.float32
bf16 = jnp.bfloat16


def half_blocks(width):
    half, quarter = width // 2, width // 4
    blocks = [((0, half), (half, width), 2.0)]
    blocks += [((lo, lo + quarter), (lo + quarter, lo + half), 2.0) for lo in (0, half)]
    blocks += [((lo, lo + quarter), (lo, lo + quarter), 1.0) for lo in range(0, width, quarter)]
    return blocks


def split_parts(x, count):
    parts = []
    rest = x
    for _ in range(count - 1):
        hi = lax.reduce_precision(rest, exponent_bits=8, mantissa_bits=7)
        parts.append(hi.astype(bf16))
        rest = rest - hi
    parts.append(rest.astype(bf16))
    return parts


def dot_parts(pattern, wide, other, count, wide_first=True):
    total = None
    for part in split_parts(wide, count):
        args = (part, other) if wide_first else (other, part)
        term = jnp.einsum(pattern, *args, preferred_element_type=f32)
        total = term if total is None else total + term
    return total


def dot_split(pattern, exact, wide):
    return dot_parts(pattern, wide, exact, 2, wide_first=False)


def dot_split3(pattern, first, second):
    fh, fl = split_parts(first, 2)
    sh, sl = split_parts(second, 2)
    return (
        jnp.einsum(pattern, fh, sh, preferred_element_type=f32)
        + jnp.einsum(pattern, fh, sl, preferred_element_type=f32)
        + jnp.einsum(pattern, fl, sh, preferred_element_type=f32)
    )


def ctx_scan(state, total, reverse):
    n = lax.axis_size("ctx")
    heads, feat, width = state.shape
    total_rows = -(-feat // width)
    flat = jnp.concatenate(
        [
            state.reshape(heads * feat, width),
            jnp.pad(total, ((0, 0), (0, total_rows * width - feat))).reshape(
                heads * total_rows, width
            ),
        ],
        axis=0,
    )
    rows = flat.shape[0]
    per = -(-rows // (n * 8)) * 8
    flat = jnp.pad(flat, ((0, n * per - rows), (0, 0)))
    got = lax.all_to_all(flat.reshape(n, per, width), "ctx", 0, 0, tiled=True)
    src = lax.broadcasted_iota(jnp.int32, (n, n), 1)
    dst = lax.broadcasted_iota(jnp.int32, (n, n), 0)
    mask = (src > dst if reverse else src < dst).astype(f32)
    summed = jnp.einsum("ij,jrc->irc", mask, got, precision=highest)
    back = lax.all_to_all(summed, "ctx", 0, 0, tiled=True).reshape(n * per, width)
    state_out = back[: heads * feat].reshape(heads, feat, width)
    total_out = back[heads * feat : heads * (feat + total_rows)].reshape(heads, total_rows * width)
    return state_out, total_out[:, :feat]


def head_exchange(stacked, owned):
    count = lax.axis_size("head")
    me = lax.axis_index("head")
    pieces = []
    for k in range(count):
        target = (me + k) % count
        piece = lax.dynamic_slice_in_dim(stacked, target * owned, owned, axis=3)
        if k:
            piece = lax.ppermute(piece, "head", [(j, (j + k) % count) for j in range(count)])
        pieces.append(piece)
    return jnp.concatenate(pieces, axis=2)


def head_return(grads, heads_all):
    count = lax.axis_size("head")
    me = lax.axis_index("head")
    owned = grads.shape[2]
    out = jnp.zeros((grads.shape[0], 1, heads_all, grads.shape[3]), grads.dtype)
    for k in range(count):
        piece = grads[:, k : k + 1]
        if k:
            piece = lax.ppermute(piece, "head", [(j, (j - k) % count) for j in range(count)])
        out = lax.dynamic_update_slice_in_dim(out, piece, ((me + k) % count) * owned, axis=2)
    return out


def sketch_parts(tokens, projector, pattern):
    inverse = tokens.shape[-1] ** (-0.5)
    sketch_one = jnp.einsum(pattern, tokens, projector[0], preferred_element_type=f32) * inverse
    sketch_two = jnp.einsum(pattern, tokens, projector[1], preferred_element_type=f32) * inverse
    return (sketch_one, sketch_two)


def half_features(sketch_one, sketch_two):
    width = sketch_one.shape[-1]
    sketch = sketch_one * sketch_two
    pieces = []
    for (r0, r1), (c0, c1), _ in half_blocks(width):
        outer = sketch[..., r0:r1, None] * sketch[..., None, c0:c1] * (1.0 / width)
        pieces.append(outer.reshape(sketch.shape[:-1] + ((r1 - r0) * (c1 - c0),)))
    return jnp.concatenate(pieces, axis=-1).astype(bf16)


def half_weight(width):
    parts = [np.full((r1 - r0) * (c1 - c0), w, np.float32) for (r0, r1), (c0, c1), w in half_blocks(width)]
    return np.concatenate(parts)


def half_feature_back(cotangent, sketch_one, sketch_two, proj_wide):
    width = sketch_one.shape[-1]
    sketch = sketch_one * sketch_two
    quarter = width // 4
    segments = [[] for _ in range(4)]
    place = 0
    for (r0, r1), (c0, c1), w in half_blocks(width):
        size = (r1 - r0) * (c1 - c0)
        block = cotangent[..., place : place + size].reshape(
            cotangent.shape[:-1] + (r1 - r0, c1 - c0)
        )
        place += size
        rows_part = jnp.einsum("...rc,...c->...r", block, sketch[..., c0:c1], precision=highest)
        for k in range(r0 // quarter, r1 // quarter):
            lo = k * quarter - r0
            segments[k].append(rows_part[..., lo : lo + quarter])
        if w != 1.0:
            cols_part = jnp.einsum("...rc,...r->...c", block, sketch[..., r0:r1], precision=highest)
            for k in range(c0 // quarter, c1 // quarter):
                lo = k * quarter - c0
                segments[k].append(cols_part[..., lo : lo + quarter])
    dsketch = jnp.concatenate([sum(parts[1:], parts[0]) for parts in segments], axis=-1)
    dsketch = dsketch * (2.0 / width)
    back_one = jnp.einsum("...f,df->...d", dsketch * sketch_two, proj_wide[0], precision=highest)
    back_two = jnp.einsum("...f,df->...d", dsketch * sketch_one, proj_wide[1], precision=highest)
    return (back_one + back_two) * proj_wide.shape[1] ** (-0.5)


def body(queries, keys, values, dout, signs):
    projector = (2 * signs - 1).astype(bf16)
    proj_wide = projector.astype(f32)
    width = signs.shape[-1]
    weight = jnp.asarray(half_weight(width), bf16)
    heads_all = keys.shape[1]
    owned = heads_all // lax.axis_size("head")
    offset = lax.axis_index("head") * owned
    key_part = lax.dynamic_slice_in_dim(keys, offset, owned, 1)
    value_part = lax.dynamic_slice_in_dim(values, offset, owned, 1)
    both = head_exchange(jnp.stack([queries, dout]), owned)
    query_part, grad_part = both[0], both[1]
    key_one, key_two = sketch_parts(key_part, projector, "thd,df->htf")
    key_feat = half_features(key_one, key_two)
    key_wfeat = key_feat * weight
    value_heads = value_part.transpose(1, 0, 2)
    block_state = jnp.einsum("htf,htd->hfd", key_feat, value_heads, preferred_element_type=f32)
    block_total = jnp.sum(key_feat, 1, dtype=f32)
    state_in, total_in = ctx_scan(block_state, block_total, False)

    query_one, query_two = sketch_parts(query_part, projector, "tmhd,df->hmtf")
    query_feat = half_features(query_one, query_two)
    query_wfeat = query_feat * weight
    grad_heads = grad_part.transpose(2, 1, 0, 3).astype(f32)
    length = key_feat.shape[1]
    causal = lax.broadcasted_iota(jnp.int32, (length, length), 0) >= lax.broadcasted_iota(
        jnp.int32, (length, length), 1
    )
    scores = jnp.where(
        causal,
        jnp.einsum("hmif,hjf->hmij", query_wfeat, key_feat, preferred_element_type=f32),
        0.0,
    )
    weights = scores.astype(bf16)
    numerator = jnp.einsum(
        "hmij,hjd->hmid", weights, value_heads, preferred_element_type=f32
    ) + dot_split("hmif,hfd->hmid", query_wfeat, state_in)
    denominator = 1.0 + jnp.sum(scores, -1) + dot_split("hmif,hf->hmi", query_wfeat, total_in)
    output_rows = numerator / denominator[..., None]
    grad_rows = grad_heads / denominator[..., None]
    grad_low = grad_rows.astype(bf16)
    correction = -jnp.sum(grad_rows * output_rows, -1)
    suffix_part = jnp.einsum("hmif,hmid->hfd", query_feat, grad_low, preferred_element_type=f32)
    suffix_sum = dot_split("hmif,hmi->hf", query_feat, correction)
    merged_state, merged_total = ctx_scan(suffix_part, suffix_sum, True)

    dscores = jnp.where(
        causal,
        jnp.einsum("hmid,hjd->hmij", grad_low, value_heads, preferred_element_type=f32)
        + correction[..., None],
        0.0,
    ).astype(bf16)
    grad_qfeat = (
        jnp.einsum("hmij,hjf->hmif", dscores, key_feat, preferred_element_type=f32)
        + dot_split3("hmid,hfd->hmif", grad_rows, state_in)
        + correction[..., None] * total_in[:, None, None, :]
    )
    query_grad = half_feature_back(grad_qfeat, query_one, query_two, proj_wide)
    query_low = query_grad.transpose(2, 1, 0, 3).astype(bf16)
    query_out = head_return(query_low, heads_all)

    grad_kfeat = jnp.einsum("hmij,hmif->hjf", dscores, query_feat, preferred_element_type=f32)
    grad_value = jnp.einsum("hmij,hmid->hjd", weights, grad_low, preferred_element_type=f32)
    kfeat_total = (
        grad_kfeat
        + dot_split("htd,hfd->htf", value_heads, merged_state)
        + merged_total[:, None, :]
    )
    value_total = grad_value + dot_split("htf,hfd->htd", key_wfeat, merged_state)
    key_sum = half_feature_back(kfeat_total, key_one, key_two, proj_wide)
    key_out = key_sum.transpose(1, 0, 2).astype(bf16)
    value_out = value_total.transpose(1, 0, 2).astype(bf16)
    return (query_out, key_out, value_out)


def solution(mesh):
    in_specs = (
        P("ctx", "head", None, None),
        P("ctx", None, None),
        P("ctx", None, None),
        P("ctx", "head", None, None),
        P(),
    )
    out_specs = (P("ctx", "head", None, None), P("ctx", "head", None), P("ctx", "head", None))
    return jax.shard_map(body, mesh=mesh, in_specs=in_specs, out_specs=out_specs, check_vma=False)
```

```python
import jax
import jax.numpy as jnp
import numpy as np
from jax import lax
from jax.sharding import PartitionSpec as P

highest = lax.Precision.HIGHEST
f32 = jnp.float32
bf16 = jnp.bfloat16


def triangle(width):
    rows, cols = np.triu_indices(width)
    keep = (rows * width + cols).astype(np.int32)
    place = np.zeros((width, width), np.int32)
    place[rows, cols] = np.arange(rows.size)
    place[cols, rows] = np.arange(rows.size)
    return keep, place.reshape(-1)


def split_parts(x, count):
    parts = []
    rest = x
    for _ in range(count - 1):
        hi = lax.reduce_precision(rest, exponent_bits=8, mantissa_bits=7)
        parts.append(hi.astype(bf16))
        rest = rest - hi
    parts.append(rest.astype(bf16))
    return parts


def dot_parts(pattern, wide, other, count, wide_first=True):
    total = None
    for part in split_parts(wide, count):
        args = (part, other) if wide_first else (other, part)
        term = jnp.einsum(pattern, *args, preferred_element_type=f32)
        total = term if total is None else total + term
    return total


def dot_split(pattern, exact, wide):
    return dot_parts(pattern, wide, exact, 2, wide_first=False)


def dot_split3(pattern, first, second):
    fh, fl = split_parts(first, 2)
    sh, sl = split_parts(second, 2)
    return (
        jnp.einsum(pattern, fh, sh, preferred_element_type=f32)
        + jnp.einsum(pattern, fh, sl, preferred_element_type=f32)
        + jnp.einsum(pattern, fl, sh, preferred_element_type=f32)
    )


def ctx_scan(state, total, reverse):
    n = lax.axis_size("ctx")
    heads, feat, width = state.shape
    total_rows = -(-feat // width)
    flat = jnp.concatenate(
        [
            state.reshape(heads * feat, width),
            jnp.pad(total, ((0, 0), (0, total_rows * width - feat))).reshape(
                heads * total_rows, width
            ),
        ],
        axis=0,
    )
    rows = flat.shape[0]
    per = -(-rows // (n * 8)) * 8
    flat = jnp.pad(flat, ((0, n * per - rows), (0, 0)))
    got = lax.all_to_all(flat.reshape(n, per, width), "ctx", 0, 0, tiled=True)
    src = lax.broadcasted_iota(jnp.int32, (n, n), 1)
    dst = lax.broadcasted_iota(jnp.int32, (n, n), 0)
    mask = (src > dst if reverse else src < dst).astype(f32)
    summed = jnp.einsum("ij,jrc->irc", mask, got, precision=highest)
    back = lax.all_to_all(summed, "ctx", 0, 0, tiled=True).reshape(n * per, width)
    state_out = back[: heads * feat].reshape(heads, feat, width)
    total_out = back[heads * feat : heads * (feat + total_rows)].reshape(heads, total_rows * width)
    return state_out, total_out[:, :feat]


def head_exchange(stacked, owned):
    count = lax.axis_size("head")
    me = lax.axis_index("head")
    pieces = []
    for k in range(count):
        target = (me + k) % count
        piece = lax.dynamic_slice_in_dim(stacked, target * owned, owned, axis=3)
        if k:
            piece = lax.ppermute(piece, "head", [(j, (j + k) % count) for j in range(count)])
        pieces.append(piece)
    return jnp.concatenate(pieces, axis=2)


def head_return(grads, heads_all):
    count = lax.axis_size("head")
    me = lax.axis_index("head")
    owned = grads.shape[2]
    out = jnp.zeros((grads.shape[0], 1, heads_all, grads.shape[3]), grads.dtype)
    for k in range(count):
        piece = grads[:, k : k + 1]
        if k:
            piece = lax.ppermute(piece, "head", [(j, (j - k) % count) for j in range(count)])
        out = lax.dynamic_update_slice_in_dim(out, piece, ((me + k) % count) * owned, axis=2)
    return out


def sketch_parts(tokens, projector, pattern):
    inverse = tokens.shape[-1] ** (-0.5)
    sketch_one = jnp.einsum(pattern, tokens, projector[0], preferred_element_type=f32) * inverse
    sketch_two = jnp.einsum(pattern, tokens, projector[1], preferred_element_type=f32) * inverse
    return (sketch_one, sketch_two)


def features(sketch_one, sketch_two):
    width = sketch_one.shape[-1]
    sketch = sketch_one * sketch_two
    outer = sketch[..., :, None] * sketch[..., None, :] * (1.0 / width)
    return outer.reshape(sketch.shape[:-1] + (width * width,)).astype(bf16)


def feature_back(cotangent, sketch_one, sketch_two, proj_wide):
    width = sketch_one.shape[-1]
    sketch = sketch_one * sketch_two
    square = cotangent.reshape(cotangent.shape[:-1] + (width, width))
    dsketch = (
        jnp.einsum("...ab,...b->...a", square, sketch, precision=highest)
        + jnp.einsum("...ab,...a->...b", square, sketch, precision=highest)
    ) * (1.0 / width)
    back_one = jnp.einsum("...f,df->...d", dsketch * sketch_two, proj_wide[0], precision=highest)
    back_two = jnp.einsum("...f,df->...d", dsketch * sketch_one, proj_wide[1], precision=highest)
    return (back_one + back_two) * proj_wide.shape[1] ** (-0.5)


def sym_scan(state, total, keep, place, reverse):
    half_state, half_total = ctx_scan(
        jnp.take(state, keep, axis=1), jnp.take(total, keep, axis=1), reverse
    )
    return jnp.take(half_state, place, axis=1), jnp.take(half_total, place, axis=1)


def body(queries, keys, values, dout, signs):
    projector = (2 * signs - 1).astype(bf16)
    proj_wide = projector.astype(f32)
    width = signs.shape[-1]
    keep_np, place_np = triangle(width)
    keep = jnp.asarray(keep_np)
    place = jnp.asarray(place_np)
    heads_all = keys.shape[1]
    owned = heads_all // lax.axis_size("head")
    offset = lax.axis_index("head") * owned
    key_part = lax.dynamic_slice_in_dim(keys, offset, owned, 1)
    value_part = lax.dynamic_slice_in_dim(values, offset, owned, 1)
    both = head_exchange(jnp.stack([queries, dout]), owned)
    query_part, grad_part = both[0], both[1]
    key_one, key_two = sketch_parts(key_part, projector, "thd,df->htf")
    key_feat = features(key_one, key_two)
    value_heads = value_part.transpose(1, 0, 2)
    block_state = jnp.einsum("htf,htd->hfd", key_feat, value_heads, preferred_element_type=f32)
    block_total = jnp.sum(key_feat, 1, dtype=f32)
    state_in, total_in = sym_scan(block_state, block_total, keep, place, False)

    query_one, query_two = sketch_parts(query_part, projector, "tmhd,df->hmtf")
    query_feat = features(query_one, query_two)
    grad_heads = grad_part.transpose(2, 1, 0, 3).astype(f32)
    length = key_feat.shape[1]
    causal = lax.broadcasted_iota(jnp.int32, (length, length), 0) >= lax.broadcasted_iota(
        jnp.int32, (length, length), 1
    )
    scores = jnp.where(
        causal,
        jnp.einsum("hmif,hjf->hmij", query_feat, key_feat, preferred_element_type=f32),
        0.0,
    )
    weights = scores.astype(bf16)
    numerator = jnp.einsum(
        "hmij,hjd->hmid", weights, value_heads, preferred_element_type=f32
    ) + dot_split("hmif,hfd->hmid", query_feat, state_in)
    denominator = 1.0 + jnp.sum(scores, -1) + dot_split("hmif,hf->hmi", query_feat, total_in)
    output_rows = numerator / denominator[..., None]
    grad_rows = grad_heads / denominator[..., None]
    grad_low = grad_rows.astype(bf16)
    correction = -jnp.sum(grad_rows * output_rows, -1)
    suffix_part = jnp.einsum("hmif,hmid->hfd", query_feat, grad_low, preferred_element_type=f32)
    suffix_sum = dot_split("hmif,hmi->hf", query_feat, correction)
    merged_state, merged_total = sym_scan(suffix_part, suffix_sum, keep, place, True)

    dscores = jnp.where(
        causal,
        jnp.einsum("hmid,hjd->hmij", grad_low, value_heads, preferred_element_type=f32)
        + correction[..., None],
        0.0,
    ).astype(bf16)
    grad_qfeat = (
        jnp.einsum("hmij,hjf->hmif", dscores, key_feat, preferred_element_type=f32)
        + dot_split3("hmid,hfd->hmif", grad_rows, state_in)
        + correction[..., None] * total_in[:, None, None, :]
    )
    query_grad = feature_back(grad_qfeat, query_one, query_two, proj_wide)
    query_low = query_grad.transpose(2, 1, 0, 3).astype(bf16)
    query_out = head_return(query_low, heads_all)

    grad_kfeat = jnp.einsum("hmij,hmif->hjf", dscores, query_feat, preferred_element_type=f32)
    grad_value = jnp.einsum("hmij,hmid->hjd", weights, grad_low, preferred_element_type=f32)
    kfeat_total = (
        grad_kfeat
        + dot_split("htd,hfd->htf", value_heads, merged_state)
        + merged_total[:, None, :]
    )
    value_total = grad_value + dot_split("htf,hfd->htd", key_feat, merged_state)
    key_sum = feature_back(kfeat_total, key_one, key_two, proj_wide)
    key_out = key_sum.transpose(1, 0, 2).astype(bf16)
    value_out = value_total.transpose(1, 0, 2).astype(bf16)
    return (query_out, key_out, value_out)


def solution(mesh):
    in_specs = (
        P("ctx", "head", None, None),
        P("ctx", None, None),
        P("ctx", None, None),
        P("ctx", "head", None, None),
        P(),
    )
    out_specs = (P("ctx", "head", None, None), P("ctx", "head", None), P("ctx", "head", None))
    return jax.shard_map(body, mesh=mesh, in_specs=in_specs, out_specs=out_specs, check_vma=False)
```

```python
import jax
import jax.numpy as jnp
import numpy as np
from jax import lax
from jax.sharding import PartitionSpec as P

highest = lax.Precision.HIGHEST
f32 = jnp.float32
bf16 = jnp.bfloat16


def triangle(width):
    rows, cols = np.triu_indices(width)
    take_a = np.eye(width, dtype=np.float32)[:, rows]
    take_b = np.eye(width, dtype=np.float32)[:, cols]
    weight = np.where(rows == cols, 1.0, 2.0).astype(np.float32)
    off = (rows != cols).astype(np.float32)
    return take_a, take_b, weight, off


def split_parts(x, count):
    parts = []
    rest = x
    for _ in range(count - 1):
        hi = lax.reduce_precision(rest, exponent_bits=8, mantissa_bits=7)
        parts.append(hi.astype(bf16))
        rest = rest - hi
    parts.append(rest.astype(bf16))
    return parts


def dot_parts(pattern, wide, other, count, wide_first=True):
    total = None
    for part in split_parts(wide, count):
        args = (part, other) if wide_first else (other, part)
        term = jnp.einsum(pattern, *args, preferred_element_type=f32)
        total = term if total is None else total + term
    return total


def dot_split(pattern, exact, wide):
    return dot_parts(pattern, wide, exact, 2, wide_first=False)


def take_pair(x, take_a, take_b):
    lhs = jnp.concatenate(split_parts(x, 3), axis=-1)
    both = jnp.concatenate([take_a, take_b], axis=1)
    rhs = jnp.concatenate([both, both, both], axis=0)
    out = jnp.einsum("...k,kn->...n", lhs, rhs, preferred_element_type=f32)
    size = take_a.shape[1]
    return out[..., :size], out[..., size:]


def ctx_scan(state, total, reverse):
    n = lax.axis_size("ctx")
    heads, feat, width = state.shape
    total_rows = -(-feat // width)
    flat = jnp.concatenate(
        [
            state.reshape(heads * feat, width),
            jnp.pad(total, ((0, 0), (0, total_rows * width - feat))).reshape(
                heads * total_rows, width
            ),
        ],
        axis=0,
    )
    rows = flat.shape[0]
    per = -(-rows // (n * 8)) * 8
    flat = jnp.pad(flat, ((0, n * per - rows), (0, 0)))
    got = lax.all_to_all(flat.reshape(n, per, width), "ctx", 0, 0, tiled=True)
    src = lax.broadcasted_iota(jnp.int32, (n, n), 1)
    dst = lax.broadcasted_iota(jnp.int32, (n, n), 0)
    mask = (src > dst if reverse else src < dst).astype(f32)
    summed = jnp.einsum("ij,jrc->irc", mask, got, precision=highest)
    back = lax.all_to_all(summed, "ctx", 0, 0, tiled=True).reshape(n * per, width)
    state_out = back[: heads * feat].reshape(heads, feat, width)
    total_out = back[heads * feat : heads * (feat + total_rows)].reshape(heads, total_rows * width)
    return state_out, total_out[:, :feat]


def head_exchange(stacked, owned):
    count = lax.axis_size("head")
    me = lax.axis_index("head")
    pieces = []
    for k in range(count):
        target = (me + k) % count
        piece = lax.dynamic_slice_in_dim(stacked, target * owned, owned, axis=3)
        if k:
            piece = lax.ppermute(piece, "head", [(j, (j + k) % count) for j in range(count)])
        pieces.append(piece)
    return jnp.concatenate(pieces, axis=2)


def head_return(grads, heads_all):
    count = lax.axis_size("head")
    me = lax.axis_index("head")
    owned = grads.shape[2]
    out = jnp.zeros((grads.shape[0], 1, heads_all, grads.shape[3]), grads.dtype)
    for k in range(count):
        piece = grads[:, k : k + 1]
        if k:
            piece = lax.ppermute(piece, "head", [(j, (j - k) % count) for j in range(count)])
        out = lax.dynamic_update_slice_in_dim(out, piece, ((me + k) % count) * owned, axis=2)
    return out


def sketch_parts(tokens, projector, pattern):
    inverse = tokens.shape[-1] ** (-0.5)
    sketch_one = jnp.einsum(pattern, tokens, projector[0], preferred_element_type=f32) * inverse
    sketch_two = jnp.einsum(pattern, tokens, projector[1], preferred_element_type=f32) * inverse
    return (sketch_one, sketch_two)


def tri_features(sketch_one, sketch_two, take_a, take_b):
    width = sketch_one.shape[-1]
    sketch = sketch_one * sketch_two
    first, second = take_pair(sketch, take_a, take_b)
    return (first * second * (1.0 / width)).astype(bf16)


def tri_feature_back(cotangent, sketch_one, sketch_two, proj_wide, take_a, take_b, off):
    width = sketch_one.shape[-1]
    sketch = sketch_one * sketch_two
    first, second = take_pair(sketch, take_a, take_b)
    spread = jnp.concatenate([cotangent * second, cotangent * first * off], axis=-1)
    gather = jnp.concatenate([take_a.T, take_b.T], axis=0).astype(bf16)
    dsketch = dot_parts("...k,ka->...a", spread, gather, 2) * (2.0 / width)
    back_one = jnp.einsum("...f,df->...d", dsketch * sketch_two, proj_wide[0], precision=highest)
    back_two = jnp.einsum("...f,df->...d", dsketch * sketch_one, proj_wide[1], precision=highest)
    return (back_one + back_two) * proj_wide.shape[1] ** (-0.5)


def body(queries, keys, values, dout, signs):
    projector = (2 * signs - 1).astype(bf16)
    proj_wide = projector.astype(f32)
    width = signs.shape[-1]
    take_a_np, take_b_np, weight_np, off_np = triangle(width)
    take_a = jnp.asarray(take_a_np, bf16)
    take_b = jnp.asarray(take_b_np, bf16)
    weight = jnp.asarray(weight_np, bf16)
    off = jnp.asarray(off_np, f32)
    heads_all = keys.shape[1]
    owned = heads_all // lax.axis_size("head")
    offset = lax.axis_index("head") * owned
    key_part = lax.dynamic_slice_in_dim(keys, offset, owned, 1)
    value_part = lax.dynamic_slice_in_dim(values, offset, owned, 1)
    both = head_exchange(jnp.stack([queries, dout]), owned)
    query_part, grad_part = both[0], both[1]
    key_one, key_two = sketch_parts(key_part, projector, "thd,df->htf")
    key_feat = tri_features(key_one, key_two, take_a, take_b)
    key_wfeat = key_feat * weight
    value_heads = value_part.transpose(1, 0, 2)
    block_state = jnp.einsum("htf,htd->hfd", key_feat, value_heads, preferred_element_type=f32)
    block_total = jnp.sum(key_feat, 1, dtype=f32)
    state_in, total_in = ctx_scan(block_state, block_total, False)

    query_one, query_two = sketch_parts(query_part, projector, "tmhd,df->hmtf")
    query_feat = tri_features(query_one, query_two, take_a, take_b)
    query_wfeat = query_feat * weight
    grad_heads = grad_part.transpose(2, 1, 0, 3).astype(f32)
    length = key_feat.shape[1]
    causal = lax.broadcasted_iota(jnp.int32, (length, length), 0) >= lax.broadcasted_iota(
        jnp.int32, (length, length), 1
    )
    scores = jnp.where(
        causal,
        jnp.einsum("hmif,hjf->hmij", query_wfeat, key_feat, preferred_element_type=f32),
        0.0,
    )
    weights = scores.astype(bf16)
    numerator = jnp.einsum(
        "hmij,hjd->hmid", weights, value_heads, preferred_element_type=f32
    ) + dot_split("hmif,hfd->hmid", query_wfeat, state_in)
    denominator = 1.0 + jnp.sum(scores, -1) + dot_split("hmif,hf->hmi", query_wfeat, total_in)
    output_rows = numerator / denominator[..., None]
    grad_rows = grad_heads / denominator[..., None]
    grad_low = grad_rows.astype(bf16)
    correction = -jnp.sum(grad_rows * output_rows, -1)
    suffix_part = jnp.einsum("hmif,hmid->hfd", query_feat, grad_low, preferred_element_type=f32)
    suffix_sum = dot_split("hmif,hmi->hf", query_feat, correction)
    merged_state, merged_total = ctx_scan(suffix_part, suffix_sum, True)

    dscores = jnp.where(
        causal,
        jnp.einsum("hmid,hjd->hmij", grad_low, value_heads, preferred_element_type=f32)
        + correction[..., None],
        0.0,
    ).astype(bf16)
    grad_hi, grad_lo = split_parts(grad_rows, 2)
    state_hi, state_lo = split_parts(state_in.transpose(0, 2, 1), 2)
    corr_hi, corr_lo = split_parts(correction[..., None], 2)
    total_hi, total_lo = split_parts(total_in[:, None, :], 2)
    grad_qfeat = jnp.einsum(
        "hmik,hkf->hmif",
        jnp.concatenate([dscores, grad_hi, grad_hi, grad_lo, corr_hi, corr_hi, corr_lo], axis=-1),
        jnp.concatenate(
            [key_feat, state_hi, state_lo, state_hi, total_hi, total_lo, total_hi], axis=1
        ),
        preferred_element_type=f32,
    )
    query_grad = tri_feature_back(
        grad_qfeat, query_one, query_two, proj_wide, take_a, take_b, off
    )
    query_low = query_grad.transpose(2, 1, 0, 3).astype(bf16)
    query_out = head_return(query_low, heads_all)

    grad_kfeat = jnp.einsum("hmij,hmif->hjf", dscores, query_feat, preferred_element_type=f32)
    grad_value = jnp.einsum("hmij,hmid->hjd", weights, grad_low, preferred_element_type=f32)
    merged_hi, merged_lo = split_parts(merged_state.transpose(0, 2, 1), 2)
    kfeat_total = (
        grad_kfeat
        + jnp.einsum(
            "htk,hkf->htf",
            jnp.concatenate([value_heads, value_heads], axis=-1),
            jnp.concatenate([merged_hi, merged_lo], axis=1),
            preferred_element_type=f32,
        )
        + merged_total[:, None, :]
    )
    value_total = grad_value + dot_split("htf,hfd->htd", key_wfeat, merged_state)
    key_sum = tri_feature_back(kfeat_total, key_one, key_two, proj_wide, take_a, take_b, off)
    key_out = key_sum.transpose(1, 0, 2).astype(bf16)
    value_out = value_total.transpose(1, 0, 2).astype(bf16)
    return (query_out, key_out, value_out)


def solution(mesh):
    in_specs = (
        P("ctx", "head", None, None),
        P("ctx", None, None),
        P("ctx", None, None),
        P("ctx", "head", None, None),
        P(),
    )
    out_specs = (P("ctx", "head", None, None), P("ctx", "head", None), P("ctx", "head", None))
    return jax.shard_map(body, mesh=mesh, in_specs=in_specs, out_specs=out_specs, check_vma=False)
```

```python
import jax
import jax.numpy as jnp
import numpy as np
from jax import lax
from jax.sharding import PartitionSpec as P

highest = lax.Precision.HIGHEST
f32 = jnp.float32
bf16 = jnp.bfloat16


def triangle(width):
    rows, cols = np.triu_indices(width)
    take_a = np.eye(width, dtype=np.float32)[:, rows]
    take_b = np.eye(width, dtype=np.float32)[:, cols]
    weight = np.where(rows == cols, 1.0, 2.0).astype(np.float32)
    off = (rows != cols).astype(np.float32)
    return take_a, take_b, weight, off


def split_parts(x, count):
    parts = []
    rest = x
    for _ in range(count - 1):
        hi = lax.reduce_precision(rest, exponent_bits=8, mantissa_bits=7)
        parts.append(hi.astype(bf16))
        rest = rest - hi
    parts.append(rest.astype(bf16))
    return parts


def dot_parts(pattern, wide, other, count, wide_first=True):
    total = None
    for part in split_parts(wide, count):
        args = (part, other) if wide_first else (other, part)
        term = jnp.einsum(pattern, *args, preferred_element_type=f32)
        total = term if total is None else total + term
    return total


def dot_split(pattern, exact, wide):
    return dot_parts(pattern, wide, exact, 2, wide_first=False)


def take_pair(x, take_a, take_b):
    lhs = jnp.concatenate(split_parts(x, 3), axis=-1)
    both = jnp.concatenate([take_a, take_b], axis=1)
    rhs = jnp.concatenate([both, both, both], axis=0)
    out = jnp.einsum("...k,kn->...n", lhs, rhs, preferred_element_type=f32)
    size = take_a.shape[1]
    return out[..., :size], out[..., size:]


def ctx_scan(state, total, reverse):
    n = lax.axis_size("ctx")
    heads, feat, width = state.shape
    total_rows = -(-feat // width)
    flat = jnp.concatenate(
        [
            state.reshape(heads * feat, width),
            jnp.pad(total, ((0, 0), (0, total_rows * width - feat))).reshape(
                heads * total_rows, width
            ),
        ],
        axis=0,
    )
    rows = flat.shape[0]
    per = -(-rows // (n * 8)) * 8
    flat = jnp.pad(flat, ((0, n * per - rows), (0, 0)))
    got = lax.all_to_all(flat.reshape(n, per, width), "ctx", 0, 0, tiled=True)
    src = lax.broadcasted_iota(jnp.int32, (n, n), 1)
    dst = lax.broadcasted_iota(jnp.int32, (n, n), 0)
    mask = (src > dst if reverse else src < dst).astype(f32)
    summed = jnp.einsum("ij,jrc->irc", mask, got, precision=highest)
    back = lax.all_to_all(summed, "ctx", 0, 0, tiled=True).reshape(n * per, width)
    state_out = back[: heads * feat].reshape(heads, feat, width)
    total_out = back[heads * feat : heads * (feat + total_rows)].reshape(heads, total_rows * width)
    return state_out, total_out[:, :feat]


def head_exchange(stacked, owned):
    count = lax.axis_size("head")
    me = lax.axis_index("head")
    pieces = []
    for k in range(count):
        target = (me + k) % count
        piece = lax.dynamic_slice_in_dim(stacked, target * owned, owned, axis=3)
        if k:
            piece = lax.ppermute(piece, "head", [(j, (j + k) % count) for j in range(count)])
        pieces.append(piece)
    return jnp.concatenate(pieces, axis=2)


def head_return(grads, heads_all):
    count = lax.axis_size("head")
    me = lax.axis_index("head")
    owned = grads.shape[2]
    out = jnp.zeros((grads.shape[0], 1, heads_all, grads.shape[3]), grads.dtype)
    for k in range(count):
        piece = grads[:, k : k + 1]
        if k:
            piece = lax.ppermute(piece, "head", [(j, (j - k) % count) for j in range(count)])
        out = lax.dynamic_update_slice_in_dim(out, piece, ((me + k) % count) * owned, axis=2)
    return out


def sketch_parts(tokens, projector, pattern):
    inverse = tokens.shape[-1] ** (-0.5)
    sketch_one = jnp.einsum(pattern, tokens, projector[0], preferred_element_type=f32) * inverse
    sketch_two = jnp.einsum(pattern, tokens, projector[1], preferred_element_type=f32) * inverse
    return (sketch_one, sketch_two)


def tri_features(sketch_one, sketch_two, take_a, take_b):
    width = sketch_one.shape[-1]
    sketch = sketch_one * sketch_two
    first, second = take_pair(sketch, take_a, take_b)
    return (first * second * (1.0 / width)).astype(bf16)


def tri_feature_back(cotangent, sketch_one, sketch_two, proj_wide, take_a, take_b, off):
    width = sketch_one.shape[-1]
    sketch = sketch_one * sketch_two
    first, second = take_pair(sketch, take_a, take_b)
    spread = jnp.concatenate([cotangent * second, cotangent * first * off], axis=-1)
    gather = jnp.concatenate([take_a.T, take_b.T], axis=0).astype(bf16)
    dsketch = dot_parts("...k,ka->...a", spread, gather, 2) * (2.0 / width)
    back_one = jnp.einsum("...f,df->...d", dsketch * sketch_two, proj_wide[0], precision=highest)
    back_two = jnp.einsum("...f,df->...d", dsketch * sketch_one, proj_wide[1], precision=highest)
    return (back_one + back_two) * proj_wide.shape[1] ** (-0.5)


def body(queries, keys, values, dout, signs):
    projector = (2 * signs - 1).astype(bf16)
    proj_wide = projector.astype(f32)
    width = signs.shape[-1]
    take_a_np, take_b_np, weight_np, off_np = triangle(width)
    take_a = jnp.asarray(take_a_np, bf16)
    take_b = jnp.asarray(take_b_np, bf16)
    weight = jnp.asarray(weight_np, bf16)
    off = jnp.asarray(off_np, f32)
    heads_all = keys.shape[1]
    owned = heads_all // lax.axis_size("head")
    offset = lax.axis_index("head") * owned
    key_part = lax.dynamic_slice_in_dim(keys, offset, owned, 1)
    value_part = lax.dynamic_slice_in_dim(values, offset, owned, 1)
    both = head_exchange(jnp.stack([queries, dout]), owned)
    query_part, grad_part = both[0], both[1]
    key_one, key_two = sketch_parts(key_part, projector, "thd,df->htf")
    key_feat = tri_features(key_one, key_two, take_a, take_b)
    key_wfeat = key_feat * weight
    value_heads = value_part.transpose(1, 0, 2)
    block_state = jnp.einsum("htf,htd->hfd", key_feat, value_heads, preferred_element_type=f32)
    block_total = jnp.sum(key_feat, 1, dtype=f32)
    state_in, total_in = ctx_scan(block_state, block_total, False)

    query_one, query_two = sketch_parts(query_part, projector, "tmhd,df->hmtf")
    query_feat = tri_features(query_one, query_two, take_a, take_b)
    query_wfeat = query_feat * weight
    grad_heads = grad_part.transpose(2, 1, 0, 3).astype(f32)
    length = key_feat.shape[1]
    causal = lax.broadcasted_iota(jnp.int32, (length, length), 0) >= lax.broadcasted_iota(
        jnp.int32, (length, length), 1
    )
    scores = jnp.where(
        causal,
        jnp.einsum("hmif,hjf->hmij", query_wfeat, key_feat, preferred_element_type=f32),
        0.0,
    )
    weights = scores.astype(bf16)
    numerator = jnp.einsum(
        "hmij,hjd->hmid", weights, value_heads, preferred_element_type=f32
    ) + dot_split("hmif,hfd->hmid", query_wfeat, state_in)
    denominator = 1.0 + jnp.sum(scores, -1) + dot_split("hmif,hf->hmi", query_wfeat, total_in)
    output_rows = numerator / denominator[..., None]
    grad_rows = grad_heads / denominator[..., None]
    grad_low = grad_rows.astype(bf16)
    correction = -jnp.sum(grad_rows * output_rows, -1)
    suffix_part = jnp.einsum("hmif,hmid->hfd", query_feat, grad_low, preferred_element_type=f32)
    suffix_sum = dot_split("hmif,hmi->hf", query_feat, correction)
    merged_state, merged_total = ctx_scan(suffix_part, suffix_sum, True)

    dscores = jnp.where(
        causal,
        jnp.einsum("hmid,hjd->hmij", grad_low, value_heads, preferred_element_type=f32)
        + correction[..., None],
        0.0,
    ).astype(bf16)
    grad_hi, grad_lo = split_parts(grad_rows, 2)
    state_hi, state_lo = split_parts(state_in.transpose(0, 2, 1), 2)
    grad_qfeat = (
        jnp.einsum(
            "hmik,hkf->hmif",
            jnp.concatenate([dscores, grad_hi, grad_hi, grad_lo], axis=-1),
            jnp.concatenate([key_feat, state_hi, state_lo, state_hi], axis=1),
            preferred_element_type=f32,
        )
        + correction[..., None] * total_in[:, None, None, :]
    )
    query_grad = tri_feature_back(
        grad_qfeat, query_one, query_two, proj_wide, take_a, take_b, off
    )
    query_low = query_grad.transpose(2, 1, 0, 3).astype(bf16)
    query_out = head_return(query_low, heads_all)

    grad_kfeat = jnp.einsum("hmij,hmif->hjf", dscores, query_feat, preferred_element_type=f32)
    grad_value = jnp.einsum("hmij,hmid->hjd", weights, grad_low, preferred_element_type=f32)
    merged_hi, merged_lo = split_parts(merged_state.transpose(0, 2, 1), 2)
    kfeat_total = (
        grad_kfeat
        + jnp.einsum(
            "htk,hkf->htf",
            jnp.concatenate([value_heads, value_heads], axis=-1),
            jnp.concatenate([merged_hi, merged_lo], axis=1),
            preferred_element_type=f32,
        )
        + merged_total[:, None, :]
    )
    value_total = grad_value + dot_split("htf,hfd->htd", key_wfeat, merged_state)
    key_sum = tri_feature_back(kfeat_total, key_one, key_two, proj_wide, take_a, take_b, off)
    key_out = key_sum.transpose(1, 0, 2).astype(bf16)
    value_out = value_total.transpose(1, 0, 2).astype(bf16)
    return (query_out, key_out, value_out)


def solution(mesh):
    in_specs = (
        P("ctx", "head", None, None),
        P("ctx", None, None),
        P("ctx", None, None),
        P("ctx", "head", None, None),
        P(),
    )
    out_specs = (P("ctx", "head", None, None), P("ctx", "head", None), P("ctx", "head", None))
    return jax.shard_map(body, mesh=mesh, in_specs=in_specs, out_specs=out_specs, check_vma=False)
```

```python
import jax
import jax.numpy as jnp
import numpy as np
from jax import lax
from jax.sharding import PartitionSpec as P

highest = lax.Precision.HIGHEST
f32 = jnp.float32
bf16 = jnp.bfloat16


def triangle(width):
    rows, cols = np.triu_indices(width)
    take_a = np.eye(width, dtype=np.float32)[:, rows]
    take_b = np.eye(width, dtype=np.float32)[:, cols]
    weight = np.where(rows == cols, 1.0, 2.0).astype(np.float32)
    off = (rows != cols).astype(np.float32)
    return take_a, take_b, weight, off


def split_parts(x, count):
    parts = []
    rest = x
    for _ in range(count - 1):
        hi = lax.reduce_precision(rest, exponent_bits=8, mantissa_bits=7)
        parts.append(hi.astype(bf16))
        rest = rest - hi
    parts.append(rest.astype(bf16))
    return parts


def dot_parts(pattern, wide, other, count, wide_first=True):
    total = None
    for part in split_parts(wide, count):
        args = (part, other) if wide_first else (other, part)
        term = jnp.einsum(pattern, *args, preferred_element_type=f32)
        total = term if total is None else total + term
    return total


def dot_split(pattern, exact, wide):
    return dot_parts(pattern, wide, exact, 2, wide_first=False)


def take_pair(x, take_a, take_b):
    lhs = jnp.concatenate(split_parts(x, 3), axis=-1)
    both = jnp.concatenate([take_a, take_b], axis=1)
    rhs = jnp.concatenate([both, both, both], axis=0)
    out = jnp.einsum("...k,kn->...n", lhs, rhs, preferred_element_type=f32)
    size = take_a.shape[1]
    return out[..., :size], out[..., size:]


def scan_send(state, total):
    n = lax.axis_size("ctx")
    heads, feat, width = state.shape
    total_rows = -(-feat // width)
    flat = jnp.concatenate(
        [
            state.reshape(heads * feat, width),
            jnp.pad(total, ((0, 0), (0, total_rows * width - feat))).reshape(
                heads * total_rows, width
            ),
        ],
        axis=0,
    )
    rows = flat.shape[0]
    per = -(-rows // (n * 8)) * 8
    flat = jnp.pad(flat, ((0, n * per - rows), (0, 0)))
    return lax.all_to_all(flat.reshape(n, per, width), "ctx", 0, 0, tiled=True)


def scan_sum(got, reverse):
    n = got.shape[0]
    src = lax.broadcasted_iota(jnp.int32, (n, n), 1)
    dst = lax.broadcasted_iota(jnp.int32, (n, n), 0)
    mask = (src > dst if reverse else src < dst).astype(bf16)
    return jnp.einsum(
        "ij,jrc->irc",
        jnp.concatenate([mask, mask, mask], axis=1),
        jnp.concatenate(split_parts(got, 3), axis=0),
        preferred_element_type=f32,
    )


def scan_return(summed, heads, feat):
    n, per, width = summed.shape
    total_rows = -(-feat // width)
    back = lax.all_to_all(summed, "ctx", 0, 0, tiled=True).reshape(n * per, width)
    state_out = back[: heads * feat].reshape(heads, feat, width)
    total_out = back[heads * feat : heads * (feat + total_rows)].reshape(heads, total_rows * width)
    return state_out, total_out[:, :feat]


def ctx_scan(state, total, reverse):
    summed = scan_sum(scan_send(state, total), reverse)
    return scan_return(summed, state.shape[0], state.shape[1])


def head_exchange(stacked, owned):
    count = lax.axis_size("head")
    me = lax.axis_index("head")
    pieces = []
    for k in range(count):
        target = (me + k) % count
        piece = lax.dynamic_slice_in_dim(stacked, target * owned, owned, axis=3)
        if k:
            piece = lax.ppermute(piece, "head", [(j, (j + k) % count) for j in range(count)])
        pieces.append(piece)
    return jnp.concatenate(pieces, axis=2)


def head_return(grads, heads_all):
    count = lax.axis_size("head")
    me = lax.axis_index("head")
    owned = grads.shape[2]
    out = jnp.zeros((grads.shape[0], 1, heads_all, grads.shape[3]), grads.dtype)
    for k in range(count):
        piece = grads[:, k : k + 1]
        if k:
            piece = lax.ppermute(piece, "head", [(j, (j - k) % count) for j in range(count)])
        out = lax.dynamic_update_slice_in_dim(out, piece, ((me + k) % count) * owned, axis=2)
    return out


def sketch_parts(tokens, projector, pattern):
    inverse = tokens.shape[-1] ** (-0.5)
    sketch_one = jnp.einsum(pattern, tokens, projector[0], preferred_element_type=f32) * inverse
    sketch_two = jnp.einsum(pattern, tokens, projector[1], preferred_element_type=f32) * inverse
    return (sketch_one, sketch_two)


def tri_features(sketch_one, sketch_two, take_a, take_b):
    width = sketch_one.shape[-1]
    sketch = sketch_one * sketch_two
    first, second = take_pair(sketch, take_a, take_b)
    return (first * second * (1.0 / width)).astype(bf16)


def tri_feature_back(cotangent, sketch_one, sketch_two, proj_wide, take_a, take_b, off):
    width = sketch_one.shape[-1]
    sketch = sketch_one * sketch_two
    first, second = take_pair(sketch, take_a, take_b)
    spread = jnp.concatenate([cotangent * second, cotangent * first * off], axis=-1)
    gather = jnp.concatenate([take_a.T, take_b.T], axis=0).astype(bf16)
    dsketch = dot_parts("...k,ka->...a", spread, gather, 2) * (2.0 / width)
    back_one = jnp.einsum("...f,df->...d", dsketch * sketch_two, proj_wide[0], precision=highest)
    back_two = jnp.einsum("...f,df->...d", dsketch * sketch_one, proj_wide[1], precision=highest)
    return (back_one + back_two) * proj_wide.shape[1] ** (-0.5)


def body(queries, keys, values, dout, signs):
    projector = (2 * signs - 1).astype(bf16)
    proj_wide = projector.astype(f32)
    width = signs.shape[-1]
    take_a_np, take_b_np, weight_np, off_np = triangle(width)
    take_a = jnp.asarray(take_a_np, bf16)
    take_b = jnp.asarray(take_b_np, bf16)
    weight = jnp.asarray(weight_np, bf16)
    off = jnp.asarray(off_np, f32)
    heads_all = keys.shape[1]
    owned = heads_all // lax.axis_size("head")
    offset = lax.axis_index("head") * owned
    key_part = lax.dynamic_slice_in_dim(keys, offset, owned, 1)
    value_part = lax.dynamic_slice_in_dim(values, offset, owned, 1)
    both = head_exchange(jnp.stack([queries, dout]), owned)
    query_part, grad_part = both[0], both[1]
    key_one, key_two = sketch_parts(key_part, projector, "thd,df->htf")
    key_feat = tri_features(key_one, key_two, take_a, take_b)
    key_wfeat = key_feat * weight
    value_heads = value_part.transpose(1, 0, 2)
    block_state = jnp.einsum("htf,htd->hfd", key_feat, value_heads, preferred_element_type=f32)
    block_total = jnp.sum(key_feat, 1, dtype=f32)
    state_in, total_in = ctx_scan(block_state, block_total, False)

    query_one, query_two = sketch_parts(query_part, projector, "tmhd,df->hmtf")
    query_feat = tri_features(query_one, query_two, take_a, take_b)
    query_wfeat = query_feat * weight
    grad_heads = grad_part.transpose(2, 1, 0, 3).astype(f32)
    length = key_feat.shape[1]
    causal = lax.broadcasted_iota(jnp.int32, (length, length), 0) >= lax.broadcasted_iota(
        jnp.int32, (length, length), 1
    )
    scores = jnp.where(
        causal,
        jnp.einsum("hmif,hjf->hmij", query_wfeat, key_feat, preferred_element_type=f32),
        0.0,
    )
    weights = scores.astype(bf16)
    numerator = jnp.einsum(
        "hmij,hjd->hmid", weights, value_heads, preferred_element_type=f32
    ) + dot_split("hmif,hfd->hmid", query_wfeat, state_in)
    denominator = 1.0 + jnp.sum(scores, -1) + dot_split("hmif,hf->hmi", query_wfeat, total_in)
    output_rows = numerator / denominator[..., None]
    grad_rows = grad_heads / denominator[..., None]
    grad_low = grad_rows.astype(bf16)
    correction = -jnp.sum(grad_rows * output_rows, -1)
    suffix_part = jnp.einsum("hmif,hmid->hfd", query_feat, grad_low, preferred_element_type=f32)
    suffix_sum = dot_split("hmif,hmi->hf", query_feat, correction)
    suffix_got = scan_send(suffix_part, suffix_sum)

    dscores = jnp.where(
        causal,
        jnp.einsum("hmid,hjd->hmij", grad_low, value_heads, preferred_element_type=f32)
        + correction[..., None],
        0.0,
    ).astype(bf16)
    grad_hi, grad_lo = split_parts(grad_rows, 2)
    state_hi, state_lo = split_parts(state_in.transpose(0, 2, 1), 2)
    grad_qfeat = (
        jnp.einsum(
            "hmik,hkf->hmif",
            jnp.concatenate([dscores, grad_hi, grad_hi, grad_lo], axis=-1),
            jnp.concatenate([key_feat, state_hi, state_lo, state_hi], axis=1),
            preferred_element_type=f32,
        )
        + correction[..., None] * total_in[:, None, None, :]
    )
    grad_kfeat = jnp.einsum("hmij,hmif->hjf", dscores, query_feat, preferred_element_type=f32)
    grad_value = jnp.einsum("hmij,hmid->hjd", weights, grad_low, preferred_element_type=f32)
    suffix_summed = scan_sum(suffix_got, True)
    suffix_summed, grad_qfeat, grad_kfeat, grad_value = lax.optimization_barrier(
        (suffix_summed, grad_qfeat, grad_kfeat, grad_value)
    )
    merged_state, merged_total = scan_return(suffix_summed, suffix_part.shape[0], suffix_part.shape[1])
    query_grad = tri_feature_back(
        grad_qfeat, query_one, query_two, proj_wide, take_a, take_b, off
    )
    query_low = query_grad.transpose(2, 1, 0, 3).astype(bf16)
    query_out = head_return(query_low, heads_all)

    merged_hi, merged_lo = split_parts(merged_state.transpose(0, 2, 1), 2)
    kfeat_total = (
        grad_kfeat
        + jnp.einsum(
            "htk,hkf->htf",
            jnp.concatenate([value_heads, value_heads], axis=-1),
            jnp.concatenate([merged_hi, merged_lo], axis=1),
            preferred_element_type=f32,
        )
        + merged_total[:, None, :]
    )
    value_total = grad_value + dot_split("htf,hfd->htd", key_wfeat, merged_state)
    key_sum = tri_feature_back(kfeat_total, key_one, key_two, proj_wide, take_a, take_b, off)
    key_out = key_sum.transpose(1, 0, 2).astype(bf16)
    value_out = value_total.transpose(1, 0, 2).astype(bf16)
    return (query_out, key_out, value_out)


def solution(mesh):
    in_specs = (
        P("ctx", "head", None, None),
        P("ctx", None, None),
        P("ctx", None, None),
        P("ctx", "head", None, None),
        P(),
    )
    out_specs = (P("ctx", "head", None, None), P("ctx", "head", None), P("ctx", "head", None))
    return jax.shard_map(body, mesh=mesh, in_specs=in_specs, out_specs=out_specs, check_vma=False)
```

```python
import jax
import jax.numpy as jnp
import numpy as np
from jax import lax
from jax.sharding import PartitionSpec as P

highest = lax.Precision.HIGHEST
f32 = jnp.float32
bf16 = jnp.bfloat16


def triangle(width):
    rows, cols = np.triu_indices(width)
    take_a = np.eye(width, dtype=np.float32)[:, rows]
    take_b = np.eye(width, dtype=np.float32)[:, cols]
    weight = np.where(rows == cols, 1.0, 2.0).astype(np.float32)
    off = (rows != cols).astype(np.float32)
    return take_a, take_b, weight, off


def split_parts(x, count):
    parts = []
    rest = x
    for _ in range(count - 1):
        hi = lax.reduce_precision(rest, exponent_bits=8, mantissa_bits=7)
        parts.append(hi.astype(bf16))
        rest = rest - hi
    parts.append(rest.astype(bf16))
    return parts


def dot_parts(pattern, wide, other, count, wide_first=True):
    total = None
    for part in split_parts(wide, count):
        args = (part, other) if wide_first else (other, part)
        term = jnp.einsum(pattern, *args, preferred_element_type=f32)
        total = term if total is None else total + term
    return total


def dot_split(pattern, exact, wide):
    return dot_parts(pattern, wide, exact, 2, wide_first=False)


def take_pair(x, take_a, take_b):
    lhs = jnp.concatenate(split_parts(x, 3), axis=-1)
    both = jnp.concatenate([take_a, take_b], axis=1)
    rhs = jnp.concatenate([both, both, both], axis=0)
    out = jnp.einsum("...k,kn->...n", lhs, rhs, preferred_element_type=f32)
    size = take_a.shape[1]
    return out[..., :size], out[..., size:]


def ctx_scan(state, total, reverse):
    n = lax.axis_size("ctx")
    heads, feat, width = state.shape
    total_rows = -(-feat // width)
    flat = jnp.concatenate(
        [
            state.reshape(heads * feat, width),
            jnp.pad(total, ((0, 0), (0, total_rows * width - feat))).reshape(
                heads * total_rows, width
            ),
        ],
        axis=0,
    )
    rows = flat.shape[0]
    per = -(-rows // (n * 8)) * 8
    flat = jnp.pad(flat, ((0, n * per - rows), (0, 0)))
    got = lax.all_to_all(flat.reshape(n, per, width), "ctx", 0, 0, tiled=True)
    src = lax.broadcasted_iota(jnp.int32, (n, n), 1)
    dst = lax.broadcasted_iota(jnp.int32, (n, n), 0)
    mask = (src > dst if reverse else src < dst).astype(bf16)
    summed = jnp.einsum(
        "ij,jrc->irc",
        jnp.concatenate([mask, mask, mask], axis=1),
        jnp.concatenate(split_parts(got, 3), axis=0),
        preferred_element_type=f32,
    )
    back = lax.all_to_all(summed, "ctx", 0, 0, tiled=True).reshape(n * per, width)
    state_out = back[: heads * feat].reshape(heads, feat, width)
    total_out = back[heads * feat : heads * (feat + total_rows)].reshape(heads, total_rows * width)
    return state_out, total_out[:, :feat]


def head_exchange(stacked, owned):
    count = lax.axis_size("head")
    me = lax.axis_index("head")
    pieces = []
    for k in range(count):
        target = (me + k) % count
        piece = lax.dynamic_slice_in_dim(stacked, target * owned, owned, axis=3)
        if k:
            piece = lax.ppermute(piece, "head", [(j, (j + k) % count) for j in range(count)])
        pieces.append(piece)
    return jnp.concatenate(pieces, axis=2)


def head_return(grads, heads_all):
    count = lax.axis_size("head")
    me = lax.axis_index("head")
    owned = grads.shape[2]
    out = jnp.zeros((grads.shape[0], 1, heads_all, grads.shape[3]), grads.dtype)
    for k in range(count):
        piece = grads[:, k : k + 1]
        if k:
            piece = lax.ppermute(piece, "head", [(j, (j - k) % count) for j in range(count)])
        out = lax.dynamic_update_slice_in_dim(out, piece, ((me + k) % count) * owned, axis=2)
    return out


def sketch_parts(tokens, projector, pattern):
    inverse = tokens.shape[-1] ** (-0.5)
    sketch_one = jnp.einsum(pattern, tokens, projector[0], preferred_element_type=f32) * inverse
    sketch_two = jnp.einsum(pattern, tokens, projector[1], preferred_element_type=f32) * inverse
    return (sketch_one, sketch_two)


def tri_features(sketch_one, sketch_two, take_a, take_b):
    width = sketch_one.shape[-1]
    sketch = sketch_one * sketch_two
    first, second = take_pair(sketch, take_a, take_b)
    return (first * second * (1.0 / width)).astype(bf16)


def tri_feature_back(cotangent, sketch_one, sketch_two, proj_wide, take_a, take_b, off):
    width = sketch_one.shape[-1]
    sketch = sketch_one * sketch_two
    first, second = take_pair(sketch, take_a, take_b)
    spread = jnp.concatenate([cotangent * second, cotangent * first * off], axis=-1)
    gather = jnp.concatenate([take_a.T, take_b.T], axis=0).astype(bf16)
    dsketch = dot_parts("...k,ka->...a", spread, gather, 2) * (2.0 / width)
    back_one = jnp.einsum("...f,df->...d", dsketch * sketch_two, proj_wide[0], precision=highest)
    back_two = jnp.einsum("...f,df->...d", dsketch * sketch_one, proj_wide[1], precision=highest)
    return (back_one + back_two) * proj_wide.shape[1] ** (-0.5)


def body(queries, keys, values, dout, signs):
    projector = (2 * signs - 1).astype(bf16)
    proj_wide = projector.astype(f32)
    width = signs.shape[-1]
    take_a_np, take_b_np, weight_np, off_np = triangle(width)
    take_a = jnp.asarray(take_a_np, bf16)
    take_b = jnp.asarray(take_b_np, bf16)
    weight = jnp.asarray(weight_np, bf16)
    off = jnp.asarray(off_np, f32)
    heads_all = keys.shape[1]
    owned = heads_all // lax.axis_size("head")
    offset = lax.axis_index("head") * owned
    key_part = lax.dynamic_slice_in_dim(keys, offset, owned, 1)
    value_part = lax.dynamic_slice_in_dim(values, offset, owned, 1)
    both = head_exchange(jnp.stack([queries, dout]), owned)
    query_part, grad_part = both[0], both[1]
    key_one, key_two = sketch_parts(key_part, projector, "thd,df->htf")
    key_feat = tri_features(key_one, key_two, take_a, take_b)
    key_wfeat = key_feat * weight
    value_heads = value_part.transpose(1, 0, 2)
    block_state = jnp.einsum("htf,htd->hfd", key_feat, value_heads, preferred_element_type=f32)
    block_total = jnp.sum(key_feat, 1, dtype=f32)
    state_in, total_in = ctx_scan(block_state, block_total, False)

    query_one, query_two = sketch_parts(query_part, projector, "tmhd,df->hmtf")
    query_feat = tri_features(query_one, query_two, take_a, take_b)
    query_wfeat = query_feat * weight
    grad_heads = grad_part.transpose(2, 1, 0, 3).astype(f32)
    length = key_feat.shape[1]
    causal = lax.broadcasted_iota(jnp.int32, (length, length), 0) >= lax.broadcasted_iota(
        jnp.int32, (length, length), 1
    )
    scores = jnp.where(
        causal,
        jnp.einsum("hmif,hjf->hmij", query_wfeat, key_feat, preferred_element_type=f32),
        0.0,
    )
    weights = scores.astype(bf16)
    numerator = jnp.einsum(
        "hmij,hjd->hmid", weights, value_heads, preferred_element_type=f32
    ) + dot_split("hmif,hfd->hmid", query_wfeat, state_in)
    denominator = 1.0 + jnp.sum(scores, -1) + dot_split("hmif,hf->hmi", query_wfeat, total_in)
    output_rows = numerator / denominator[..., None]
    grad_rows = grad_heads / denominator[..., None]
    grad_low = grad_rows.astype(bf16)
    correction = -jnp.sum(grad_rows * output_rows, -1)
    suffix_part = jnp.einsum("hmif,hmid->hfd", query_feat, grad_low, preferred_element_type=f32)
    suffix_sum = dot_split("hmif,hmi->hf", query_feat, correction)
    merged_state, merged_total = ctx_scan(suffix_part, suffix_sum, True)

    dscores = jnp.where(
        causal,
        jnp.einsum("hmid,hjd->hmij", grad_low, value_heads, preferred_element_type=f32)
        + correction[..., None],
        0.0,
    ).astype(bf16)
    grad_hi, grad_lo = split_parts(grad_rows, 2)
    state_hi, state_lo = split_parts(state_in.transpose(0, 2, 1), 2)
    grad_qfeat = (
        jnp.einsum(
            "hmik,hkf->hmif",
            jnp.concatenate([dscores, grad_hi, grad_hi, grad_lo], axis=-1),
            jnp.concatenate([key_feat, state_hi, state_lo, state_hi], axis=1),
            preferred_element_type=f32,
        )
        + correction[..., None] * total_in[:, None, None, :]
    )
    query_grad = tri_feature_back(
        grad_qfeat, query_one, query_two, proj_wide, take_a, take_b, off
    )
    query_low = query_grad.transpose(2, 1, 0, 3).astype(bf16)
    query_out = head_return(query_low, heads_all)

    grad_kfeat = jnp.einsum("hmij,hmif->hjf", dscores, query_feat, preferred_element_type=f32)
    grad_value = jnp.einsum("hmij,hmid->hjd", weights, grad_low, preferred_element_type=f32)
    merged_hi, merged_lo = split_parts(merged_state.transpose(0, 2, 1), 2)
    kfeat_total = (
        grad_kfeat
        + jnp.einsum(
            "htk,hkf->htf",
            jnp.concatenate([value_heads, value_heads], axis=-1),
            jnp.concatenate([merged_hi, merged_lo], axis=1),
            preferred_element_type=f32,
        )
        + merged_total[:, None, :]
    )
    value_total = grad_value + dot_split("htf,hfd->htd", key_wfeat, merged_state)
    key_sum = tri_feature_back(kfeat_total, key_one, key_two, proj_wide, take_a, take_b, off)
    key_out = key_sum.transpose(1, 0, 2).astype(bf16)
    value_out = value_total.transpose(1, 0, 2).astype(bf16)
    return (query_out, key_out, value_out)


def solution(mesh):
    in_specs = (
        P("ctx", "head", None, None),
        P("ctx", None, None),
        P("ctx", None, None),
        P("ctx", "head", None, None),
        P(),
    )
    out_specs = (P("ctx", "head", None, None), P("ctx", "head", None), P("ctx", "head", None))
    return jax.shard_map(body, mesh=mesh, in_specs=in_specs, out_specs=out_specs, check_vma=False)
```

```python
import jax
import jax.numpy as jnp
import numpy as np
from jax import lax
from jax.sharding import PartitionSpec as P

highest = lax.Precision.HIGHEST
f32 = jnp.float32
bf16 = jnp.bfloat16


def triangle(width):
    rows, cols = np.triu_indices(width)
    take_a = np.eye(width, dtype=np.float32)[:, rows]
    take_b = np.eye(width, dtype=np.float32)[:, cols]
    weight = np.where(rows == cols, 1.0, 2.0).astype(np.float32)
    off = (rows != cols).astype(np.float32)
    return take_a, take_b, weight, off


def split_parts(x, count):
    parts = []
    rest = x
    for _ in range(count - 1):
        hi = lax.reduce_precision(rest, exponent_bits=8, mantissa_bits=7)
        parts.append(hi.astype(bf16))
        rest = rest - hi
    parts.append(rest.astype(bf16))
    return parts


def dot_parts(pattern, wide, other, count, wide_first=True):
    total = None
    for part in split_parts(wide, count):
        args = (part, other) if wide_first else (other, part)
        term = jnp.einsum(pattern, *args, preferred_element_type=f32)
        total = term if total is None else total + term
    return total


def dot_split(pattern, exact, wide):
    return dot_parts(pattern, wide, exact, 2, wide_first=False)


def take_pair(x, take_a, take_b):
    lhs = jnp.concatenate(split_parts(x, 3), axis=-1)
    both = jnp.concatenate([take_a, take_b], axis=1)
    rhs = jnp.concatenate([both, both, both], axis=0)
    out = jnp.einsum("...k,kn->...n", lhs, rhs, preferred_element_type=f32)
    size = take_a.shape[1]
    return out[..., :size], out[..., size:]


def scan_send(state, total):
    n = lax.axis_size("ctx")
    heads, feat, width = state.shape
    total_rows = -(-feat // width)
    flat = jnp.concatenate(
        [
            state.reshape(heads * feat, width),
            jnp.pad(total, ((0, 0), (0, total_rows * width - feat))).reshape(
                heads * total_rows, width
            ),
        ],
        axis=0,
    )
    rows = flat.shape[0]
    per = -(-rows // (n * 8)) * 8
    flat = jnp.pad(flat, ((0, n * per - rows), (0, 0)))
    return lax.all_to_all(flat.reshape(n, per, width), "ctx", 0, 0, tiled=True)


def scan_sum(got, reverse):
    n = got.shape[0]
    src = lax.broadcasted_iota(jnp.int32, (n, n), 1)
    dst = lax.broadcasted_iota(jnp.int32, (n, n), 0)
    mask = (src > dst if reverse else src < dst).astype(bf16)
    return jnp.einsum(
        "ij,jrc->irc",
        jnp.concatenate([mask, mask, mask], axis=1),
        jnp.concatenate(split_parts(got, 3), axis=0),
        preferred_element_type=f32,
    )


def scan_return(summed, heads, feat):
    n, per, width = summed.shape
    total_rows = -(-feat // width)
    back = lax.all_to_all(summed, "ctx", 0, 0, tiled=True).reshape(n * per, width)
    state_out = back[: heads * feat].reshape(heads, feat, width)
    total_out = back[heads * feat : heads * (feat + total_rows)].reshape(heads, total_rows * width)
    return state_out, total_out[:, :feat]


def head_exchange(stacked, owned):
    count = lax.axis_size("head")
    me = lax.axis_index("head")
    pieces = []
    for k in range(count):
        target = (me + k) % count
        piece = lax.dynamic_slice_in_dim(stacked, target * owned, owned, axis=3)
        if k:
            piece = lax.ppermute(piece, "head", [(j, (j + k) % count) for j in range(count)])
        pieces.append(piece)
    return jnp.concatenate(pieces, axis=2)


def head_return(grads, heads_all):
    count = lax.axis_size("head")
    me = lax.axis_index("head")
    owned = grads.shape[2]
    out = jnp.zeros((grads.shape[0], 1, heads_all, grads.shape[3]), grads.dtype)
    for k in range(count):
        piece = grads[:, k : k + 1]
        if k:
            piece = lax.ppermute(piece, "head", [(j, (j - k) % count) for j in range(count)])
        out = lax.dynamic_update_slice_in_dim(out, piece, ((me + k) % count) * owned, axis=2)
    return out


def sketch_parts(tokens, projector, pattern):
    inverse = tokens.shape[-1] ** (-0.5)
    sketch_one = jnp.einsum(pattern, tokens, projector[0], preferred_element_type=f32) * inverse
    sketch_two = jnp.einsum(pattern, tokens, projector[1], preferred_element_type=f32) * inverse
    return (sketch_one, sketch_two)


def tri_features(sketch_one, sketch_two, take_a, take_b):
    width = sketch_one.shape[-1]
    sketch = sketch_one * sketch_two
    first, second = take_pair(sketch, take_a, take_b)
    return (first * second * (1.0 / width)).astype(bf16)


def tri_feature_back(cotangent, sketch_one, sketch_two, proj_wide, take_a, take_b, off):
    width = sketch_one.shape[-1]
    sketch = sketch_one * sketch_two
    first, second = take_pair(sketch, take_a, take_b)
    spread = jnp.concatenate([cotangent * second, cotangent * first * off], axis=-1)
    gather = jnp.concatenate([take_a.T, take_b.T], axis=0).astype(bf16)
    dsketch = dot_parts("...k,ka->...a", spread, gather, 2) * (2.0 / width)
    back_one = jnp.einsum("...f,df->...d", dsketch * sketch_two, proj_wide[0], precision=highest)
    back_two = jnp.einsum("...f,df->...d", dsketch * sketch_one, proj_wide[1], precision=highest)
    return (back_one + back_two) * proj_wide.shape[1] ** (-0.5)


def body(queries, keys, values, dout, signs):
    projector = (2 * signs - 1).astype(bf16)
    proj_wide = projector.astype(f32)
    width = signs.shape[-1]
    take_a_np, take_b_np, weight_np, off_np = triangle(width)
    take_a = jnp.asarray(take_a_np, bf16)
    take_b = jnp.asarray(take_b_np, bf16)
    weight = jnp.asarray(weight_np, bf16)
    off = jnp.asarray(off_np, f32)
    heads_all = keys.shape[1]
    owned = heads_all // lax.axis_size("head")
    offset = lax.axis_index("head") * owned
    key_part = lax.dynamic_slice_in_dim(keys, offset, owned, 1)
    value_part = lax.dynamic_slice_in_dim(values, offset, owned, 1)
    both = head_exchange(jnp.stack([queries, dout]), owned)
    query_part, grad_part = both[0], both[1]
    key_one, key_two = sketch_parts(key_part, projector, "thd,df->htf")
    key_feat = tri_features(key_one, key_two, take_a, take_b)
    key_wfeat = key_feat * weight
    value_heads = value_part.transpose(1, 0, 2)
    block_state = jnp.einsum("htf,htd->hfd", key_feat, value_heads, preferred_element_type=f32)
    block_total = jnp.sum(key_feat, 1, dtype=f32)
    block_state, block_total, query_part, grad_part = lax.optimization_barrier(
        (block_state, block_total, query_part, grad_part)
    )
    state_in, total_in = scan_return(
        scan_sum(scan_send(block_state, block_total), False), block_state.shape[0], block_state.shape[1]
    )

    query_one, query_two = sketch_parts(query_part, projector, "tmhd,df->hmtf")
    query_feat = tri_features(query_one, query_two, take_a, take_b)
    query_wfeat = query_feat * weight
    grad_heads = grad_part.transpose(2, 1, 0, 3).astype(f32)
    length = key_feat.shape[1]
    causal = lax.broadcasted_iota(jnp.int32, (length, length), 0) >= lax.broadcasted_iota(
        jnp.int32, (length, length), 1
    )
    scores = jnp.where(
        causal,
        jnp.einsum("hmif,hjf->hmij", query_wfeat, key_feat, preferred_element_type=f32),
        0.0,
    )
    weights = scores.astype(bf16)
    numerator = jnp.einsum(
        "hmij,hjd->hmid", weights, value_heads, preferred_element_type=f32
    ) + dot_split("hmif,hfd->hmid", query_wfeat, state_in)
    denominator = 1.0 + jnp.sum(scores, -1) + dot_split("hmif,hf->hmi", query_wfeat, total_in)
    output_rows = numerator / denominator[..., None]
    grad_rows = grad_heads / denominator[..., None]
    grad_low = grad_rows.astype(bf16)
    correction = -jnp.sum(grad_rows * output_rows, -1)
    suffix_part = jnp.einsum("hmif,hmid->hfd", query_feat, grad_low, preferred_element_type=f32)
    suffix_sum = dot_split("hmif,hmi->hf", query_feat, correction)
    suffix_got = scan_send(suffix_part, suffix_sum)

    dscores = jnp.where(
        causal,
        jnp.einsum("hmid,hjd->hmij", grad_low, value_heads, preferred_element_type=f32)
        + correction[..., None],
        0.0,
    ).astype(bf16)
    grad_hi, grad_lo = split_parts(grad_rows, 2)
    state_hi, state_lo = split_parts(state_in.transpose(0, 2, 1), 2)
    grad_qfeat = (
        jnp.einsum(
            "hmik,hkf->hmif",
            jnp.concatenate([dscores, grad_hi, grad_hi, grad_lo], axis=-1),
            jnp.concatenate([key_feat, state_hi, state_lo, state_hi], axis=1),
            preferred_element_type=f32,
        )
        + correction[..., None] * total_in[:, None, None, :]
    )
    grad_kfeat = jnp.einsum("hmij,hmif->hjf", dscores, query_feat, preferred_element_type=f32)
    grad_value = jnp.einsum("hmij,hmid->hjd", weights, grad_low, preferred_element_type=f32)
    suffix_summed = scan_sum(suffix_got, True)
    suffix_summed, grad_qfeat, grad_kfeat, grad_value = lax.optimization_barrier(
        (suffix_summed, grad_qfeat, grad_kfeat, grad_value)
    )
    merged_state, merged_total = scan_return(suffix_summed, suffix_part.shape[0], suffix_part.shape[1])
    query_grad = tri_feature_back(
        grad_qfeat, query_one, query_two, proj_wide, take_a, take_b, off
    )
    query_low = query_grad.transpose(2, 1, 0, 3).astype(bf16)
    query_out = head_return(query_low, heads_all)

    merged_hi, merged_lo = split_parts(merged_state.transpose(0, 2, 1), 2)
    kfeat_total = (
        grad_kfeat
        + jnp.einsum(
            "htk,hkf->htf",
            jnp.concatenate([value_heads, value_heads], axis=-1),
            jnp.concatenate([merged_hi, merged_lo], axis=1),
            preferred_element_type=f32,
        )
        + merged_total[:, None, :]
    )
    value_total = grad_value + dot_split("htf,hfd->htd", key_wfeat, merged_state)
    key_sum = tri_feature_back(kfeat_total, key_one, key_two, proj_wide, take_a, take_b, off)
    key_out = key_sum.transpose(1, 0, 2).astype(bf16)
    value_out = value_total.transpose(1, 0, 2).astype(bf16)
    return (query_out, key_out, value_out)


def solution(mesh):
    in_specs = (
        P("ctx", "head", None, None),
        P("ctx", None, None),
        P("ctx", None, None),
        P("ctx", "head", None, None),
        P(),
    )
    out_specs = (P("ctx", "head", None, None), P("ctx", "head", None), P("ctx", "head", None))
    return jax.shard_map(body, mesh=mesh, in_specs=in_specs, out_specs=out_specs, check_vma=False)
```

```python
import jax
import jax.numpy as jnp
import numpy as np
from jax import lax
from jax.sharding import PartitionSpec as P

highest = lax.Precision.HIGHEST
f32 = jnp.float32
bf16 = jnp.bfloat16


def triangle(width):
    rows, cols = np.triu_indices(width)
    take_a = np.eye(width, dtype=np.float32)[:, rows]
    take_b = np.eye(width, dtype=np.float32)[:, cols]
    weight = np.where(rows == cols, 1.0, 2.0).astype(np.float32)
    off = (rows != cols).astype(np.float32)
    return take_a, take_b, weight, off


def split_parts(x, count):
    parts = []
    rest = x
    for _ in range(count - 1):
        hi = lax.reduce_precision(rest, exponent_bits=8, mantissa_bits=7)
        parts.append(hi.astype(bf16))
        rest = rest - hi
    parts.append(rest.astype(bf16))
    return parts


def dot_parts(pattern, wide, other, count, wide_first=True):
    total = None
    for part in split_parts(wide, count):
        args = (part, other) if wide_first else (other, part)
        term = jnp.einsum(pattern, *args, preferred_element_type=f32)
        total = term if total is None else total + term
    return total


def dot_split(pattern, exact, wide):
    return dot_parts(pattern, wide, exact, 2, wide_first=False)


def take_pair(x, take_a, take_b):
    lhs = jnp.concatenate(split_parts(x, 3), axis=-1)
    both = jnp.concatenate([take_a, take_b], axis=1)
    rhs = jnp.concatenate([both, both, both], axis=0)
    out = jnp.einsum("...k,kn->...n", lhs, rhs, preferred_element_type=f32)
    size = take_a.shape[1]
    return out[..., :size], out[..., size:]


def scan_send(state, total):
    n = lax.axis_size("ctx")
    heads, feat, width = state.shape
    total_rows = -(-feat // width)
    flat = jnp.concatenate(
        [
            state.reshape(heads * feat, width),
            jnp.pad(total, ((0, 0), (0, total_rows * width - feat))).reshape(
                heads * total_rows, width
            ),
        ],
        axis=0,
    )
    rows = flat.shape[0]
    per = -(-rows // (n * 8)) * 8
    flat = jnp.pad(flat, ((0, n * per - rows), (0, 0)))
    return lax.all_to_all(flat.reshape(n, per, width), "ctx", 0, 0, tiled=True)


def scan_sum(got, reverse):
    n = got.shape[0]
    src = lax.broadcasted_iota(jnp.int32, (n, n), 1)
    dst = lax.broadcasted_iota(jnp.int32, (n, n), 0)
    mask = (src > dst if reverse else src < dst).astype(f32)
    return jnp.einsum("ij,jrc->irc", mask, got, precision=highest)


def scan_return(summed, heads, feat):
    n, per, width = summed.shape
    total_rows = -(-feat // width)
    back = lax.all_to_all(summed, "ctx", 0, 0, tiled=True).reshape(n * per, width)
    state_out = back[: heads * feat].reshape(heads, feat, width)
    total_out = back[heads * feat : heads * (feat + total_rows)].reshape(heads, total_rows * width)
    return state_out, total_out[:, :feat]


def ctx_scan(state, total, reverse):
    summed = scan_sum(scan_send(state, total), reverse)
    return scan_return(summed, state.shape[0], state.shape[1])


def head_exchange(stacked, owned):
    count = lax.axis_size("head")
    me = lax.axis_index("head")
    pieces = []
    for k in range(count):
        target = (me + k) % count
        piece = lax.dynamic_slice_in_dim(stacked, target * owned, owned, axis=3)
        if k:
            piece = lax.ppermute(piece, "head", [(j, (j + k) % count) for j in range(count)])
        pieces.append(piece)
    return jnp.concatenate(pieces, axis=2)


def head_return(grads, heads_all):
    count = lax.axis_size("head")
    me = lax.axis_index("head")
    pieces = []
    for k in range(count):
        piece = grads[:, k]
        if k:
            piece = lax.ppermute(piece, "head", [(j, (j - k) % count) for j in range(count)])
        pieces.append(piece)
    ordered = jnp.roll(jnp.stack(pieces), me, axis=0)
    tokens, owned, width = grads.shape[0], grads.shape[2], grads.shape[3]
    return ordered.transpose(1, 0, 2, 3).reshape(tokens, 1, heads_all, width)


def sketch_parts(tokens, projector, pattern):
    inverse = tokens.shape[-1] ** (-0.5)
    sketch_one = jnp.einsum(pattern, tokens, projector[0], preferred_element_type=f32) * inverse
    sketch_two = jnp.einsum(pattern, tokens, projector[1], preferred_element_type=f32) * inverse
    return (sketch_one, sketch_two)


def tri_features(sketch_one, sketch_two, take_a, take_b):
    width = sketch_one.shape[-1]
    sketch = sketch_one * sketch_two
    first, second = take_pair(sketch, take_a, take_b)
    return (first * second * (1.0 / width)).astype(bf16)


def tri_feature_back(cotangent, sketch_one, sketch_two, proj_wide, take_a, take_b, off):
    width = sketch_one.shape[-1]
    sketch = sketch_one * sketch_two
    first, second = take_pair(sketch, take_a, take_b)
    spread = jnp.concatenate([cotangent * second, cotangent * first * off], axis=-1)
    gather = jnp.concatenate([take_a.T, take_b.T], axis=0).astype(bf16)
    dsketch = dot_parts("...k,ka->...a", spread, gather, 2) * (2.0 / width)
    back_one = jnp.einsum("...f,df->...d", dsketch * sketch_two, proj_wide[0], precision=highest)
    back_two = jnp.einsum("...f,df->...d", dsketch * sketch_one, proj_wide[1], precision=highest)
    return (back_one + back_two) * proj_wide.shape[1] ** (-0.5)


def body(queries, keys, values, dout, signs):
    projector = (2 * signs - 1).astype(bf16)
    proj_wide = projector.astype(f32)
    width = signs.shape[-1]
    take_a_np, take_b_np, weight_np, off_np = triangle(width)
    take_a = jnp.asarray(take_a_np, bf16)
    take_b = jnp.asarray(take_b_np, bf16)
    weight = jnp.asarray(weight_np, bf16)
    off = jnp.asarray(off_np, f32)
    heads_all = keys.shape[1]
    owned = heads_all // lax.axis_size("head")
    offset = lax.axis_index("head") * owned
    key_part = lax.dynamic_slice_in_dim(keys, offset, owned, 1)
    value_part = lax.dynamic_slice_in_dim(values, offset, owned, 1)
    both = head_exchange(jnp.stack([queries, dout]), owned)
    query_part, grad_part = both[0], both[1]
    key_one, key_two = sketch_parts(key_part, projector, "thd,df->htf")
    key_feat = tri_features(key_one, key_two, take_a, take_b)
    key_wfeat = key_feat * weight
    value_heads = value_part.transpose(1, 0, 2)
    block_state = jnp.einsum("htf,htd->hfd", key_feat, value_heads, preferred_element_type=f32)
    block_total = jnp.sum(key_feat, 1, dtype=f32)
    state_in, total_in = ctx_scan(block_state, block_total, False)

    query_one, query_two = sketch_parts(query_part, projector, "tmhd,df->hmtf")
    query_feat = tri_features(query_one, query_two, take_a, take_b)
    query_wfeat = query_feat * weight
    grad_heads = grad_part.transpose(2, 1, 0, 3).astype(f32)
    length = key_feat.shape[1]
    causal = lax.broadcasted_iota(jnp.int32, (length, length), 0) >= lax.broadcasted_iota(
        jnp.int32, (length, length), 1
    )
    scores = jnp.where(
        causal,
        jnp.einsum("hmif,hjf->hmij", query_wfeat, key_feat, preferred_element_type=f32),
        0.0,
    )
    weights = scores.astype(bf16)
    width_v = value_heads.shape[-1]
    carried = dot_split(
        "hmif,hfd->hmid", query_wfeat, jnp.concatenate([state_in, total_in[..., None]], axis=-1)
    )
    numerator = (
        jnp.einsum("hmij,hjd->hmid", weights, value_heads, preferred_element_type=f32)
        + carried[..., :width_v]
    )
    denominator = 1.0 + jnp.sum(scores, -1) + carried[..., width_v]
    output_rows = numerator / denominator[..., None]
    grad_rows = grad_heads / denominator[..., None]
    grad_low = grad_rows.astype(bf16)
    correction = -jnp.sum(grad_rows * output_rows, -1)
    corr_hi, corr_lo = split_parts(correction[..., None], 2)
    suffix_both = jnp.einsum(
        "hmif,hmid->hfd",
        query_feat,
        jnp.concatenate([grad_low, corr_hi, corr_lo], axis=-1),
        preferred_element_type=f32,
    )
    suffix_part = suffix_both[..., :width_v]
    suffix_sum = suffix_both[..., width_v] + suffix_both[..., width_v + 1]
    suffix_got = scan_send(suffix_part, suffix_sum)

    dscores = jnp.where(
        causal,
        jnp.einsum("hmid,hjd->hmij", grad_low, value_heads, preferred_element_type=f32)
        + correction[..., None],
        0.0,
    ).astype(bf16)
    grad_hi, grad_lo = split_parts(grad_rows, 2)
    state_hi, state_lo = split_parts(state_in.transpose(0, 2, 1), 2)
    grad_qfeat = (
        jnp.einsum(
            "hmik,hkf->hmif",
            jnp.concatenate([dscores, grad_hi, grad_hi, grad_lo], axis=-1),
            jnp.concatenate([key_feat, state_hi, state_lo, state_hi], axis=1),
            preferred_element_type=f32,
        )
        + correction[..., None] * total_in[:, None, None, :]
    )
    grad_kfeat = jnp.einsum("hmij,hmif->hjf", dscores, query_feat, preferred_element_type=f32)
    grad_value = jnp.einsum("hmij,hmid->hjd", weights, grad_low, preferred_element_type=f32)
    suffix_summed = scan_sum(suffix_got, True)
    suffix_summed, grad_qfeat, grad_kfeat, grad_value = lax.optimization_barrier(
        (suffix_summed, grad_qfeat, grad_kfeat, grad_value)
    )
    merged_state, merged_total = scan_return(suffix_summed, suffix_part.shape[0], suffix_part.shape[1])
    query_grad = tri_feature_back(
        grad_qfeat, query_one, query_two, proj_wide, take_a, take_b, off
    )
    query_low = query_grad.transpose(2, 1, 0, 3).astype(bf16)
    query_low, merged_state, merged_total = lax.optimization_barrier(
        (query_low, merged_state, merged_total)
    )
    query_out = head_return(query_low, heads_all)

    merged_hi, merged_lo = split_parts(merged_state.transpose(0, 2, 1), 2)
    kfeat_total = (
        grad_kfeat
        + jnp.einsum(
            "htk,hkf->htf",
            jnp.concatenate([value_heads, value_heads], axis=-1),
            jnp.concatenate([merged_hi, merged_lo], axis=1),
            preferred_element_type=f32,
        )
        + merged_total[:, None, :]
    )
    value_total = grad_value + dot_split("htf,hfd->htd", key_wfeat, merged_state)
    key_sum = tri_feature_back(kfeat_total, key_one, key_two, proj_wide, take_a, take_b, off)
    key_out = key_sum.transpose(1, 0, 2).astype(bf16)
    value_out = value_total.transpose(1, 0, 2).astype(bf16)
    return (query_out, key_out, value_out)


def solution(mesh):
    in_specs = (
        P("ctx", "head", None, None),
        P("ctx", None, None),
        P("ctx", None, None),
        P("ctx", "head", None, None),
        P(),
    )
    out_specs = (P("ctx", "head", None, None), P("ctx", "head", None), P("ctx", "head", None))
    return jax.shard_map(body, mesh=mesh, in_specs=in_specs, out_specs=out_specs, check_vma=False)
```

```python
import jax
import jax.numpy as jnp
import numpy as np
from jax import lax
from jax.sharding import PartitionSpec as P

highest = lax.Precision.HIGHEST
f32 = jnp.float32
bf16 = jnp.bfloat16


def triangle(width):
    rows, cols = np.triu_indices(width)
    take_a = np.eye(width, dtype=np.float32)[:, rows]
    take_b = np.eye(width, dtype=np.float32)[:, cols]
    weight = np.where(rows == cols, 1.0, 2.0).astype(np.float32)
    off = (rows != cols).astype(np.float32)
    return take_a, take_b, weight, off


def split_parts(x, count):
    parts = []
    rest = x
    for _ in range(count - 1):
        hi = lax.reduce_precision(rest, exponent_bits=8, mantissa_bits=7)
        parts.append(hi.astype(bf16))
        rest = rest - hi
    parts.append(rest.astype(bf16))
    return parts


def dot_parts(pattern, wide, other, count, wide_first=True):
    total = None
    for part in split_parts(wide, count):
        args = (part, other) if wide_first else (other, part)
        term = jnp.einsum(pattern, *args, preferred_element_type=f32)
        total = term if total is None else total + term
    return total


def dot_split(pattern, exact, wide):
    return dot_parts(pattern, wide, exact, 2, wide_first=False)


def take_pair(x, take_a, take_b):
    lhs = jnp.concatenate(split_parts(x, 3), axis=-1)
    both = jnp.concatenate([take_a, take_b], axis=1)
    rhs = jnp.concatenate([both, both, both], axis=0)
    out = jnp.einsum("...k,kn->...n", lhs, rhs, preferred_element_type=f32)
    size = take_a.shape[1]
    return out[..., :size], out[..., size:]


def scan_send(state, total):
    n = lax.axis_size("ctx")
    heads, feat, width = state.shape
    total_rows = -(-feat // width)
    flat = jnp.concatenate(
        [
            state.reshape(heads * feat, width),
            jnp.pad(total, ((0, 0), (0, total_rows * width - feat))).reshape(
                heads * total_rows, width
            ),
        ],
        axis=0,
    )
    rows = flat.shape[0]
    per = -(-rows // (n * 8)) * 8
    flat = jnp.pad(flat, ((0, n * per - rows), (0, 0)))
    return lax.all_to_all(flat.reshape(n, per, width), "ctx", 0, 0, tiled=True)


def scan_sum(got, reverse):
    n = got.shape[0]
    src = lax.broadcasted_iota(jnp.int32, (n, n), 1)
    dst = lax.broadcasted_iota(jnp.int32, (n, n), 0)
    mask = (src > dst if reverse else src < dst).astype(f32)
    return jnp.einsum("ij,jrc->irc", mask, got, precision=highest)


def scan_return(summed, heads, feat):
    n, per, width = summed.shape
    total_rows = -(-feat // width)
    back = lax.all_to_all(summed, "ctx", 0, 0, tiled=True).reshape(n * per, width)
    state_out = back[: heads * feat].reshape(heads, feat, width)
    total_out = back[heads * feat : heads * (feat + total_rows)].reshape(heads, total_rows * width)
    return state_out, total_out[:, :feat]


def ctx_scan(state, total, reverse):
    summed = scan_sum(scan_send(state, total), reverse)
    return scan_return(summed, state.shape[0], state.shape[1])


def head_exchange(stacked, owned):
    count = lax.axis_size("head")
    me = lax.axis_index("head")
    pieces = []
    for k in range(count):
        target = (me + k) % count
        piece = lax.dynamic_slice_in_dim(stacked, target * owned, owned, axis=3)
        if k:
            piece = lax.ppermute(piece, "head", [(j, (j + k) % count) for j in range(count)])
        pieces.append(piece)
    return jnp.concatenate(pieces, axis=2)


def head_return(grads, heads_all):
    count = lax.axis_size("head")
    me = lax.axis_index("head")
    owned = grads.shape[2]
    out = jnp.zeros((grads.shape[0], 1, heads_all, grads.shape[3]), grads.dtype)
    for k in range(count):
        piece = grads[:, k : k + 1]
        if k:
            piece = lax.ppermute(piece, "head", [(j, (j - k) % count) for j in range(count)])
        out = lax.dynamic_update_slice_in_dim(out, piece, ((me + k) % count) * owned, axis=2)
    return out


def sketch_parts(tokens, projector, pattern):
    inverse = tokens.shape[-1] ** (-0.5)
    sketch_one = jnp.einsum(pattern, tokens, projector[0], preferred_element_type=f32) * inverse
    sketch_two = jnp.einsum(pattern, tokens, projector[1], preferred_element_type=f32) * inverse
    return (sketch_one, sketch_two)


def tri_features(sketch_one, sketch_two, take_a, take_b):
    width = sketch_one.shape[-1]
    sketch = sketch_one * sketch_two
    first, second = take_pair(sketch, take_a, take_b)
    return (first * second * (1.0 / width)).astype(bf16)


def tri_feature_back(cotangent, sketch_one, sketch_two, proj_wide, take_a, take_b, off):
    width = sketch_one.shape[-1]
    sketch = sketch_one * sketch_two
    first, second = take_pair(sketch, take_a, take_b)
    spread = jnp.concatenate([cotangent * second, cotangent * first * off], axis=-1)
    gather = jnp.concatenate([take_a.T, take_b.T], axis=0).astype(bf16)
    dsketch = dot_parts("...k,ka->...a", spread, gather, 2) * (2.0 / width)
    back_one = jnp.einsum("...f,df->...d", dsketch * sketch_two, proj_wide[0], precision=highest)
    back_two = jnp.einsum("...f,df->...d", dsketch * sketch_one, proj_wide[1], precision=highest)
    return (back_one + back_two) * proj_wide.shape[1] ** (-0.5)


def body(queries, keys, values, dout, signs):
    projector = (2 * signs - 1).astype(bf16)
    proj_wide = projector.astype(f32)
    width = signs.shape[-1]
    take_a_np, take_b_np, weight_np, off_np = triangle(width)
    take_a = jnp.asarray(take_a_np, bf16)
    take_b = jnp.asarray(take_b_np, bf16)
    weight = jnp.asarray(weight_np, bf16)
    off = jnp.asarray(off_np, f32)
    heads_all = keys.shape[1]
    owned = heads_all // lax.axis_size("head")
    offset = lax.axis_index("head") * owned
    key_part = lax.dynamic_slice_in_dim(keys, offset, owned, 1)
    value_part = lax.dynamic_slice_in_dim(values, offset, owned, 1)
    both = head_exchange(jnp.stack([queries, dout]), owned)
    query_part, grad_part = both[0], both[1]
    key_one, key_two = sketch_parts(key_part, projector, "thd,df->htf")
    key_feat = tri_features(key_one, key_two, take_a, take_b)
    key_wfeat = key_feat * weight
    value_heads = value_part.transpose(1, 0, 2)
    block_state = jnp.einsum("htf,htd->hfd", key_feat, value_heads, preferred_element_type=f32)
    block_total = jnp.sum(key_feat, 1, dtype=f32)
    state_in, total_in = ctx_scan(block_state, block_total, False)

    query_one, query_two = sketch_parts(query_part, projector, "tmhd,df->hmtf")
    query_feat = tri_features(query_one, query_two, take_a, take_b)
    query_wfeat = query_feat * weight
    grad_heads = grad_part.transpose(2, 1, 0, 3).astype(f32)
    length = key_feat.shape[1]
    causal = lax.broadcasted_iota(jnp.int32, (length, length), 0) >= lax.broadcasted_iota(
        jnp.int32, (length, length), 1
    )
    scores = jnp.where(
        causal,
        jnp.einsum("hmif,hjf->hmij", query_wfeat, key_feat, preferred_element_type=f32),
        0.0,
    )
    weights = scores.astype(bf16)
    numerator = jnp.einsum(
        "hmij,hjd->hmid", weights, value_heads, preferred_element_type=f32
    ) + dot_split("hmif,hfd->hmid", query_wfeat, state_in)
    denominator = 1.0 + jnp.sum(scores, -1) + dot_split("hmif,hf->hmi", query_wfeat, total_in)
    output_rows = numerator / denominator[..., None]
    grad_rows = grad_heads / denominator[..., None]
    grad_low = grad_rows.astype(bf16)
    correction = -jnp.sum(grad_rows * output_rows, -1)
    suffix_part = jnp.einsum("hmif,hmid->hfd", query_feat, grad_low, preferred_element_type=f32)
    suffix_sum = dot_split("hmif,hmi->hf", query_feat, correction)
    suffix_got = scan_send(suffix_part, suffix_sum)

    dscores = jnp.where(
        causal,
        jnp.einsum("hmid,hjd->hmij", grad_low, value_heads, preferred_element_type=f32)
        + correction[..., None],
        0.0,
    ).astype(bf16)
    grad_hi, grad_lo = split_parts(grad_rows, 2)
    state_hi, state_lo = split_parts(state_in.transpose(0, 2, 1), 2)
    grad_qfeat = (
        jnp.einsum(
            "hmik,hkf->hmif",
            jnp.concatenate([dscores, grad_hi, grad_hi, grad_lo], axis=-1),
            jnp.concatenate([key_feat, state_hi, state_lo, state_hi], axis=1),
            preferred_element_type=f32,
        )
        + correction[..., None] * total_in[:, None, None, :]
    )
    grad_kfeat = jnp.einsum("hmij,hmif->hjf", dscores, query_feat, preferred_element_type=f32)
    grad_value = jnp.einsum("hmij,hmid->hjd", weights, grad_low, preferred_element_type=f32)
    suffix_summed = scan_sum(suffix_got, True)
    suffix_summed, grad_qfeat, grad_kfeat, grad_value = lax.optimization_barrier(
        (suffix_summed, grad_qfeat, grad_kfeat, grad_value)
    )
    merged_state, merged_total = scan_return(suffix_summed, suffix_part.shape[0], suffix_part.shape[1])
    query_grad = tri_feature_back(
        grad_qfeat, query_one, query_two, proj_wide, take_a, take_b, off
    )
    query_low = query_grad.transpose(2, 1, 0, 3).astype(bf16)
    query_low, merged_state, merged_total = lax.optimization_barrier(
        (query_low, merged_state, merged_total)
    )
    query_out = head_return(query_low, heads_all)

    merged_hi, merged_lo = split_parts(merged_state.transpose(0, 2, 1), 2)
    kfeat_total = (
        grad_kfeat
        + jnp.einsum(
            "htk,hkf->htf",
            jnp.concatenate([value_heads, value_heads], axis=-1),
            jnp.concatenate([merged_hi, merged_lo], axis=1),
            preferred_element_type=f32,
        )
        + merged_total[:, None, :]
    )
    value_total = grad_value + dot_split("htf,hfd->htd", key_wfeat, merged_state)
    key_sum = tri_feature_back(kfeat_total, key_one, key_two, proj_wide, take_a, take_b, off)
    key_out = key_sum.transpose(1, 0, 2).astype(bf16)
    value_out = value_total.transpose(1, 0, 2).astype(bf16)
    return (query_out, key_out, value_out)


def solution(mesh):
    in_specs = (
        P("ctx", "head", None, None),
        P("ctx", None, None),
        P("ctx", None, None),
        P("ctx", "head", None, None),
        P(),
    )
    out_specs = (P("ctx", "head", None, None), P("ctx", "head", None), P("ctx", "head", None))
    return jax.shard_map(body, mesh=mesh, in_specs=in_specs, out_specs=out_specs, check_vma=False)
```

```python
import jax
import jax.numpy as jnp
import numpy as np
from jax import lax
from jax.sharding import PartitionSpec as P

highest = lax.Precision.HIGHEST
f32 = jnp.float32
bf16 = jnp.bfloat16


def triangle(width):
    rows, cols = np.triu_indices(width)
    take_a = np.eye(width, dtype=np.float32)[:, rows]
    take_b = np.eye(width, dtype=np.float32)[:, cols]
    weight = np.where(rows == cols, 1.0, 2.0).astype(np.float32)
    off = (rows != cols).astype(np.float32)
    return take_a, take_b, weight, off


def split_parts(x, count):
    parts = []
    rest = x
    for _ in range(count - 1):
        hi = lax.reduce_precision(rest, exponent_bits=8, mantissa_bits=7)
        parts.append(hi.astype(bf16))
        rest = rest - hi
    parts.append(rest.astype(bf16))
    return parts


def dot_parts(pattern, wide, other, count, wide_first=True):
    total = None
    for part in split_parts(wide, count):
        args = (part, other) if wide_first else (other, part)
        term = jnp.einsum(pattern, *args, preferred_element_type=f32)
        total = term if total is None else total + term
    return total


def dot_split(pattern, exact, wide):
    return dot_parts(pattern, wide, exact, 2, wide_first=False)


def take_pair(x, take_a, take_b):
    lhs = jnp.concatenate(split_parts(x, 3), axis=-1)
    both = jnp.concatenate([take_a, take_b], axis=1)
    rhs = jnp.concatenate([both, both, both], axis=0)
    out = jnp.einsum("...k,kn->...n", lhs, rhs, preferred_element_type=f32)
    size = take_a.shape[1]
    return out[..., :size], out[..., size:]


def scan_send(state, total):
    n = lax.axis_size("ctx")
    heads, feat, width = state.shape
    total_rows = -(-feat // width)
    flat = jnp.concatenate(
        [
            state.reshape(heads * feat, width),
            jnp.pad(total, ((0, 0), (0, total_rows * width - feat))).reshape(
                heads * total_rows, width
            ),
        ],
        axis=0,
    )
    rows = flat.shape[0]
    per = -(-rows // (n * 8)) * 8
    flat = jnp.pad(flat, ((0, n * per - rows), (0, 0)))
    return lax.all_to_all(flat.reshape(n, per, width), "ctx", 0, 0, tiled=True)


def scan_sum(got, reverse):
    n = got.shape[0]
    src = lax.broadcasted_iota(jnp.int32, (n, n), 1)
    dst = lax.broadcasted_iota(jnp.int32, (n, n), 0)
    mask = (src > dst if reverse else src < dst).astype(f32)
    return jnp.einsum("ij,jrc->irc", mask, got, precision=highest)


def scan_return(summed, heads, feat):
    n, per, width = summed.shape
    total_rows = -(-feat // width)
    back = lax.all_to_all(summed, "ctx", 0, 0, tiled=True).reshape(n * per, width)
    state_out = back[: heads * feat].reshape(heads, feat, width)
    total_out = back[heads * feat : heads * (feat + total_rows)].reshape(heads, total_rows * width)
    return state_out, total_out[:, :feat]


def ctx_scan(state, total, reverse):
    summed = scan_sum(scan_send(state, total), reverse)
    return scan_return(summed, state.shape[0], state.shape[1])


def head_exchange(stacked, owned):
    count = lax.axis_size("head")
    me = lax.axis_index("head")
    pieces = []
    for k in range(count):
        target = (me + k) % count
        piece = lax.dynamic_slice_in_dim(stacked, target * owned, owned, axis=3)
        if k:
            piece = lax.ppermute(piece, "head", [(j, (j + k) % count) for j in range(count)])
        pieces.append(piece)
    return jnp.concatenate(pieces, axis=2)


def head_return(grads, heads_all):
    count = lax.axis_size("head")
    me = lax.axis_index("head")
    owned = grads.shape[2]
    out = jnp.zeros((grads.shape[0], 1, heads_all, grads.shape[3]), grads.dtype)
    for k in range(count):
        piece = grads[:, k : k + 1]
        if k:
            piece = lax.ppermute(piece, "head", [(j, (j - k) % count) for j in range(count)])
        out = lax.dynamic_update_slice_in_dim(out, piece, ((me + k) % count) * owned, axis=2)
    return out


def sketch_parts(tokens, projector, pattern):
    inverse = tokens.shape[-1] ** (-0.5)
    sketch_one = jnp.einsum(pattern, tokens, projector[0], preferred_element_type=f32) * inverse
    sketch_two = jnp.einsum(pattern, tokens, projector[1], preferred_element_type=f32) * inverse
    return (sketch_one, sketch_two)


def tri_features(sketch_one, sketch_two, take_a, take_b):
    width = sketch_one.shape[-1]
    sketch = sketch_one * sketch_two
    first, second = take_pair(sketch, take_a, take_b)
    return (first * second * (1.0 / width)).astype(bf16)


def tri_feature_back(cotangent, sketch_one, sketch_two, proj_wide, take_a, take_b, off):
    width = sketch_one.shape[-1]
    sketch = sketch_one * sketch_two
    first, second = take_pair(sketch, take_a, take_b)
    spread = jnp.concatenate([cotangent * second, cotangent * first * off], axis=-1)
    gather = jnp.concatenate([take_a.T, take_b.T], axis=0).astype(bf16)
    dsketch = dot_parts("...k,ka->...a", spread, gather, 2) * (2.0 / width)
    back_one = jnp.einsum("...f,df->...d", dsketch * sketch_two, proj_wide[0], precision=highest)
    back_two = jnp.einsum("...f,df->...d", dsketch * sketch_one, proj_wide[1], precision=highest)
    return (back_one + back_two) * proj_wide.shape[1] ** (-0.5)


def body(queries, keys, values, dout, signs):
    projector = (2 * signs - 1).astype(bf16)
    proj_wide = projector.astype(f32)
    width = signs.shape[-1]
    take_a_np, take_b_np, weight_np, off_np = triangle(width)
    take_a = jnp.asarray(take_a_np, bf16)
    take_b = jnp.asarray(take_b_np, bf16)
    weight = jnp.asarray(weight_np, bf16)
    off = jnp.asarray(off_np, f32)
    heads_all = keys.shape[1]
    owned = heads_all // lax.axis_size("head")
    offset = lax.axis_index("head") * owned
    key_part = lax.dynamic_slice_in_dim(keys, offset, owned, 1)
    value_part = lax.dynamic_slice_in_dim(values, offset, owned, 1)
    both = head_exchange(jnp.stack([queries, dout]), owned)
    query_part, grad_part = both[0], both[1]
    key_one, key_two = sketch_parts(key_part, projector, "thd,df->htf")
    key_feat = tri_features(key_one, key_two, take_a, take_b)
    key_wfeat = key_feat * weight
    value_heads = value_part.transpose(1, 0, 2)
    block_state = jnp.einsum("htf,htd->hfd", key_feat, value_heads, preferred_element_type=f32)
    block_total = jnp.sum(key_feat, 1, dtype=f32)
    state_in, total_in = ctx_scan(block_state, block_total, False)

    query_one, query_two = sketch_parts(query_part, projector, "tmhd,df->hmtf")
    query_feat = tri_features(query_one, query_two, take_a, take_b)
    query_wfeat = query_feat * weight
    grad_heads = grad_part.transpose(2, 1, 0, 3).astype(f32)
    length = key_feat.shape[1]
    causal = lax.broadcasted_iota(jnp.int32, (length, length), 0) >= lax.broadcasted_iota(
        jnp.int32, (length, length), 1
    )
    scores = jnp.where(
        causal,
        jnp.einsum("hmif,hjf->hmij", query_wfeat, key_feat, preferred_element_type=f32),
        0.0,
    )
    weights = scores.astype(bf16)
    numerator = jnp.einsum(
        "hmij,hjd->hmid", weights, value_heads, preferred_element_type=f32
    ) + dot_split("hmif,hfd->hmid", query_wfeat, state_in)
    denominator = 1.0 + jnp.sum(scores, -1) + dot_split("hmif,hf->hmi", query_wfeat, total_in)
    output_rows = numerator / denominator[..., None]
    grad_rows = grad_heads / denominator[..., None]
    grad_low = grad_rows.astype(bf16)
    correction = -jnp.sum(grad_rows * output_rows, -1)
    suffix_part = jnp.einsum("hmif,hmid->hfd", query_feat, grad_low, preferred_element_type=f32)
    suffix_sum = dot_split("hmif,hmi->hf", query_feat, correction)
    suffix_got = scan_send(suffix_part, suffix_sum)

    dscores = jnp.where(
        causal,
        jnp.einsum("hmid,hjd->hmij", grad_low, value_heads, preferred_element_type=f32)
        + correction[..., None],
        0.0,
    ).astype(bf16)
    grad_hi, grad_lo = split_parts(grad_rows, 2)
    state_hi, state_lo = split_parts(state_in.transpose(0, 2, 1), 2)
    grad_qfeat = (
        jnp.einsum(
            "hmik,hkf->hmif",
            jnp.concatenate([dscores, grad_hi, grad_hi, grad_lo], axis=-1),
            jnp.concatenate([key_feat, state_hi, state_lo, state_hi], axis=1),
            preferred_element_type=f32,
        )
        + correction[..., None] * total_in[:, None, None, :]
    )
    query_grad = tri_feature_back(
        grad_qfeat, query_one, query_two, proj_wide, take_a, take_b, off
    )
    query_low = query_grad.transpose(2, 1, 0, 3).astype(bf16)
    query_out = head_return(query_low, heads_all)
    suffix_summed = scan_sum(suffix_got, True)
    suffix_summed, query_out = lax.optimization_barrier((suffix_summed, query_out))
    merged_state, merged_total = scan_return(suffix_summed, suffix_part.shape[0], suffix_part.shape[1])
    grad_kfeat = jnp.einsum("hmij,hmif->hjf", dscores, query_feat, preferred_element_type=f32)
    grad_value = jnp.einsum("hmij,hmid->hjd", weights, grad_low, preferred_element_type=f32)

    merged_hi, merged_lo = split_parts(merged_state.transpose(0, 2, 1), 2)
    kfeat_total = (
        grad_kfeat
        + jnp.einsum(
            "htk,hkf->htf",
            jnp.concatenate([value_heads, value_heads], axis=-1),
            jnp.concatenate([merged_hi, merged_lo], axis=1),
            preferred_element_type=f32,
        )
        + merged_total[:, None, :]
    )
    value_total = grad_value + dot_split("htf,hfd->htd", key_wfeat, merged_state)
    key_sum = tri_feature_back(kfeat_total, key_one, key_two, proj_wide, take_a, take_b, off)
    key_out = key_sum.transpose(1, 0, 2).astype(bf16)
    value_out = value_total.transpose(1, 0, 2).astype(bf16)
    return (query_out, key_out, value_out)


def solution(mesh):
    in_specs = (
        P("ctx", "head", None, None),
        P("ctx", None, None),
        P("ctx", None, None),
        P("ctx", "head", None, None),
        P(),
    )
    out_specs = (P("ctx", "head", None, None), P("ctx", "head", None), P("ctx", "head", None))
    return jax.shard_map(body, mesh=mesh, in_specs=in_specs, out_specs=out_specs, check_vma=False)
```

```python
import jax
import jax.numpy as jnp
import numpy as np
from jax import lax
from jax.sharding import PartitionSpec as P

highest = lax.Precision.HIGHEST
f32 = jnp.float32
bf16 = jnp.bfloat16


def triangle(width):
    rows, cols = np.triu_indices(width)
    take_a = np.eye(width, dtype=np.float32)[:, rows]
    take_b = np.eye(width, dtype=np.float32)[:, cols]
    weight = np.where(rows == cols, 1.0, 2.0).astype(np.float32)
    off = (rows != cols).astype(np.float32)
    return take_a, take_b, weight, off


def split_parts(x, count):
    parts = []
    rest = x
    for _ in range(count - 1):
        hi = lax.reduce_precision(rest, exponent_bits=8, mantissa_bits=7)
        parts.append(hi.astype(bf16))
        rest = rest - hi
    parts.append(rest.astype(bf16))
    return parts


def dot_parts(pattern, wide, other, count, wide_first=True):
    total = None
    for part in split_parts(wide, count):
        args = (part, other) if wide_first else (other, part)
        term = jnp.einsum(pattern, *args, preferred_element_type=f32)
        total = term if total is None else total + term
    return total


def dot_split(pattern, exact, wide):
    return dot_parts(pattern, wide, exact, 2, wide_first=False)


def take_pair(x, take_a, take_b):
    lhs = jnp.concatenate(split_parts(x, 3), axis=-1)
    both = jnp.concatenate([take_a, take_b], axis=1)
    rhs = jnp.concatenate([both, both, both], axis=0)
    out = jnp.einsum("...k,kn->...n", lhs, rhs, preferred_element_type=f32)
    size = take_a.shape[1]
    return out[..., :size], out[..., size:]


def scan_send(state, total):
    n = lax.axis_size("ctx")
    heads, feat, width = state.shape
    total_rows = -(-feat // width)
    flat = jnp.concatenate(
        [
            state.reshape(heads * feat, width),
            jnp.pad(total, ((0, 0), (0, total_rows * width - feat))).reshape(
                heads * total_rows, width
            ),
        ],
        axis=0,
    )
    rows = flat.shape[0]
    per = -(-rows // (n * 8)) * 8
    flat = jnp.pad(flat, ((0, n * per - rows), (0, 0)))
    return lax.all_to_all(flat.reshape(n, per, width), "ctx", 0, 0, tiled=True)


def scan_sum(got, reverse):
    n = got.shape[0]
    src = lax.broadcasted_iota(jnp.int32, (n, n), 1)
    dst = lax.broadcasted_iota(jnp.int32, (n, n), 0)
    mask = (src > dst if reverse else src < dst).astype(f32)
    return jnp.einsum("ij,jrc->irc", mask, got, precision=highest)


def scan_return(summed, heads, feat):
    n, per, width = summed.shape
    total_rows = -(-feat // width)
    back = lax.all_to_all(summed, "ctx", 0, 0, tiled=True).reshape(n * per, width)
    state_out = back[: heads * feat].reshape(heads, feat, width)
    total_out = back[heads * feat : heads * (feat + total_rows)].reshape(heads, total_rows * width)
    return state_out, total_out[:, :feat]


def ctx_scan(state, total, reverse):
    summed = scan_sum(scan_send(state, total), reverse)
    return scan_return(summed, state.shape[0], state.shape[1])


def head_exchange(stacked, owned):
    count = lax.axis_size("head")
    me = lax.axis_index("head")
    pieces = []
    for k in range(count):
        target = (me + k) % count
        piece = lax.dynamic_slice_in_dim(stacked, target * owned, owned, axis=3)
        if k:
            piece = lax.ppermute(piece, "head", [(j, (j + k) % count) for j in range(count)])
        pieces.append(piece)
    return jnp.concatenate(pieces, axis=2)


def head_return(grads, heads_all):
    count = lax.axis_size("head")
    me = lax.axis_index("head")
    owned = grads.shape[2]
    out = jnp.zeros((grads.shape[0], 1, heads_all, grads.shape[3]), grads.dtype)
    for k in range(count):
        piece = grads[:, k : k + 1]
        if k:
            piece = lax.ppermute(piece, "head", [(j, (j - k) % count) for j in range(count)])
        out = lax.dynamic_update_slice_in_dim(out, piece, ((me + k) % count) * owned, axis=2)
    return out


def sketch_parts(tokens, projector, pattern):
    inverse = tokens.shape[-1] ** (-0.5)
    sketch_one = jnp.einsum(pattern, tokens, projector[0], preferred_element_type=f32) * inverse
    sketch_two = jnp.einsum(pattern, tokens, projector[1], preferred_element_type=f32) * inverse
    return (sketch_one, sketch_two)


def tri_features(sketch_one, sketch_two, take_a, take_b):
    width = sketch_one.shape[-1]
    sketch = sketch_one * sketch_two
    first, second = take_pair(sketch, take_a, take_b)
    return (first * second * (1.0 / width)).astype(bf16)


def tri_feature_back(cotangent, sketch_one, sketch_two, proj_wide, take_a, take_b, off):
    width = sketch_one.shape[-1]
    sketch = sketch_one * sketch_two
    first, second = take_pair(sketch, take_a, take_b)
    spread = jnp.concatenate([cotangent * second, cotangent * first * off], axis=-1)
    gather = jnp.concatenate([take_a.T, take_b.T], axis=0).astype(bf16)
    dsketch = dot_parts("...k,ka->...a", spread, gather, 2) * (2.0 / width)
    one_hi, one_lo = split_parts(dsketch * sketch_two, 2)
    two_hi, two_lo = split_parts(dsketch * sketch_one, 2)
    proj = proj_wide.astype(bf16)
    back = jnp.einsum(
        "...k,dk->...d",
        jnp.concatenate([one_hi, one_lo, two_hi, two_lo], axis=-1),
        jnp.concatenate([proj[0], proj[0], proj[1], proj[1]], axis=-1),
        preferred_element_type=f32,
    )
    return back * proj_wide.shape[1] ** (-0.5)


def body(queries, keys, values, dout, signs):
    projector = (2 * signs - 1).astype(bf16)
    proj_wide = projector.astype(f32)
    width = signs.shape[-1]
    take_a_np, take_b_np, weight_np, off_np = triangle(width)
    take_a = jnp.asarray(take_a_np, bf16)
    take_b = jnp.asarray(take_b_np, bf16)
    weight = jnp.asarray(weight_np, bf16)
    off = jnp.asarray(off_np, f32)
    heads_all = keys.shape[1]
    owned = heads_all // lax.axis_size("head")
    offset = lax.axis_index("head") * owned
    key_part = lax.dynamic_slice_in_dim(keys, offset, owned, 1)
    value_part = lax.dynamic_slice_in_dim(values, offset, owned, 1)
    both = head_exchange(jnp.stack([queries, dout]), owned)
    query_part, grad_part = both[0], both[1]
    key_one, key_two = sketch_parts(key_part, projector, "thd,df->htf")
    key_feat = tri_features(key_one, key_two, take_a, take_b)
    key_wfeat = key_feat * weight
    value_heads = value_part.transpose(1, 0, 2)
    block_state = jnp.einsum("htf,htd->hfd", key_feat, value_heads, preferred_element_type=f32)
    block_total = jnp.sum(key_feat, 1, dtype=f32)
    state_in, total_in = ctx_scan(block_state, block_total, False)

    query_one, query_two = sketch_parts(query_part, projector, "tmhd,df->hmtf")
    query_feat = tri_features(query_one, query_two, take_a, take_b)
    query_wfeat = query_feat * weight
    grad_heads = grad_part.transpose(2, 1, 0, 3).astype(f32)
    length = key_feat.shape[1]
    causal = lax.broadcasted_iota(jnp.int32, (length, length), 0) >= lax.broadcasted_iota(
        jnp.int32, (length, length), 1
    )
    scores = jnp.where(
        causal,
        jnp.einsum("hmif,hjf->hmij", query_wfeat, key_feat, preferred_element_type=f32),
        0.0,
    )
    weights = scores.astype(bf16)
    numerator = jnp.einsum(
        "hmij,hjd->hmid", weights, value_heads, preferred_element_type=f32
    ) + dot_split("hmif,hfd->hmid", query_wfeat, state_in)
    denominator = 1.0 + jnp.sum(scores, -1) + dot_split("hmif,hf->hmi", query_wfeat, total_in)
    output_rows = numerator / denominator[..., None]
    grad_rows = grad_heads / denominator[..., None]
    grad_low = grad_rows.astype(bf16)
    correction = -jnp.sum(grad_rows * output_rows, -1)
    suffix_part = jnp.einsum("hmif,hmid->hfd", query_feat, grad_low, preferred_element_type=f32)
    suffix_sum = dot_split("hmif,hmi->hf", query_feat, correction)
    suffix_got = scan_send(suffix_part, suffix_sum)

    dscores = jnp.where(
        causal,
        jnp.einsum("hmid,hjd->hmij", grad_low, value_heads, preferred_element_type=f32)
        + correction[..., None],
        0.0,
    ).astype(bf16)
    grad_hi, grad_lo = split_parts(grad_rows, 2)
    state_hi, state_lo = split_parts(state_in.transpose(0, 2, 1), 2)
    grad_qfeat = (
        jnp.einsum(
            "hmik,hkf->hmif",
            jnp.concatenate([dscores, grad_hi, grad_hi, grad_lo], axis=-1),
            jnp.concatenate([key_feat, state_hi, state_lo, state_hi], axis=1),
            preferred_element_type=f32,
        )
        + correction[..., None] * total_in[:, None, None, :]
    )
    grad_kfeat = jnp.einsum("hmij,hmif->hjf", dscores, query_feat, preferred_element_type=f32)
    grad_value = jnp.einsum("hmij,hmid->hjd", weights, grad_low, preferred_element_type=f32)
    suffix_summed = scan_sum(suffix_got, True)
    suffix_summed, grad_qfeat, grad_kfeat, grad_value = lax.optimization_barrier(
        (suffix_summed, grad_qfeat, grad_kfeat, grad_value)
    )
    merged_state, merged_total = scan_return(suffix_summed, suffix_part.shape[0], suffix_part.shape[1])
    query_grad = tri_feature_back(
        grad_qfeat, query_one, query_two, proj_wide, take_a, take_b, off
    )
    query_low = query_grad.transpose(2, 1, 0, 3).astype(bf16)
    query_low, merged_state, merged_total = lax.optimization_barrier(
        (query_low, merged_state, merged_total)
    )
    query_out = head_return(query_low, heads_all)

    merged_hi, merged_lo = split_parts(merged_state.transpose(0, 2, 1), 2)
    kfeat_total = (
        grad_kfeat
        + jnp.einsum(
            "htk,hkf->htf",
            jnp.concatenate([value_heads, value_heads], axis=-1),
            jnp.concatenate([merged_hi, merged_lo], axis=1),
            preferred_element_type=f32,
        )
        + merged_total[:, None, :]
    )
    value_total = grad_value + dot_split("htf,hfd->htd", key_wfeat, merged_state)
    key_sum = tri_feature_back(kfeat_total, key_one, key_two, proj_wide, take_a, take_b, off)
    key_out = key_sum.transpose(1, 0, 2).astype(bf16)
    value_out = value_total.transpose(1, 0, 2).astype(bf16)
    return (query_out, key_out, value_out)


def solution(mesh):
    in_specs = (
        P("ctx", "head", None, None),
        P("ctx", None, None),
        P("ctx", None, None),
        P("ctx", "head", None, None),
        P(),
    )
    out_specs = (P("ctx", "head", None, None), P("ctx", "head", None), P("ctx", "head", None))
    return jax.shard_map(body, mesh=mesh, in_specs=in_specs, out_specs=out_specs, check_vma=False)
```

```python
import jax
import jax.numpy as jnp
import numpy as np
from jax import lax
from jax.sharding import PartitionSpec as P

highest = lax.Precision.HIGHEST
f32 = jnp.float32
bf16 = jnp.bfloat16


def triangle(width):
    rows, cols = np.triu_indices(width)
    take_a = np.eye(width, dtype=np.float32)[:, rows]
    take_b = np.eye(width, dtype=np.float32)[:, cols]
    weight = np.where(rows == cols, 1.0, 2.0).astype(np.float32)
    off = (rows != cols).astype(np.float32)
    return take_a, take_b, weight, off


def split_parts(x, count):
    parts = []
    rest = x
    for _ in range(count - 1):
        hi = lax.reduce_precision(rest, exponent_bits=8, mantissa_bits=7)
        parts.append(hi.astype(bf16))
        rest = rest - hi
    parts.append(rest.astype(bf16))
    return parts


def dot_parts(pattern, wide, other, count, wide_first=True):
    total = None
    for part in split_parts(wide, count):
        args = (part, other) if wide_first else (other, part)
        term = jnp.einsum(pattern, *args, preferred_element_type=f32)
        total = term if total is None else total + term
    return total


def dot_split(pattern, exact, wide):
    return dot_parts(pattern, wide, exact, 2, wide_first=False)


def take_pair(x, take_a, take_b):
    lhs = jnp.concatenate(split_parts(x, 3), axis=-1)
    both = jnp.concatenate([take_a, take_b], axis=1)
    rhs = jnp.concatenate([both, both, both], axis=0)
    out = jnp.einsum("...k,kn->...n", lhs, rhs, preferred_element_type=f32)
    size = take_a.shape[1]
    return out[..., :size], out[..., size:]


def scan_send(state, total):
    n = lax.axis_size("ctx")
    heads, feat, width = state.shape
    total_rows = -(-feat // width)
    flat = jnp.concatenate(
        [
            state.reshape(heads * feat, width),
            jnp.pad(total, ((0, 0), (0, total_rows * width - feat))).reshape(
                heads * total_rows, width
            ),
        ],
        axis=0,
    )
    rows = flat.shape[0]
    per = -(-rows // (n * 8)) * 8
    flat = jnp.pad(flat, ((0, n * per - rows), (0, 0)))
    return lax.all_to_all(flat.reshape(n, per, width), "ctx", 0, 0, tiled=True)


def scan_sum(got, reverse):
    n = got.shape[0]
    src = lax.broadcasted_iota(jnp.int32, (n, n), 1)
    dst = lax.broadcasted_iota(jnp.int32, (n, n), 0)
    mask = (src > dst if reverse else src < dst).astype(f32)
    return jnp.einsum("ij,jrc->irc", mask, got, precision=highest)


def scan_return(summed, heads, feat):
    n, per, width = summed.shape
    total_rows = -(-feat // width)
    back = lax.all_to_all(summed, "ctx", 0, 0, tiled=True).reshape(n * per, width)
    state_out = back[: heads * feat].reshape(heads, feat, width)
    total_out = back[heads * feat : heads * (feat + total_rows)].reshape(heads, total_rows * width)
    return state_out, total_out[:, :feat]


def ctx_scan(state, total, reverse):
    summed = scan_sum(scan_send(state, total), reverse)
    return scan_return(summed, state.shape[0], state.shape[1])


def head_exchange(stacked, owned):
    count = lax.axis_size("head")
    me = lax.axis_index("head")
    pieces = []
    for k in range(count):
        target = (me + k) % count
        piece = lax.dynamic_slice_in_dim(stacked, target * owned, owned, axis=3)
        if k:
            piece = lax.ppermute(piece, "head", [(j, (j + k) % count) for j in range(count)])
        pieces.append(piece)
    return jnp.concatenate(pieces, axis=2)


def head_return(grads, heads_all):
    count = lax.axis_size("head")
    me = lax.axis_index("head")
    owned = grads.shape[2]
    out = jnp.zeros((grads.shape[0], 1, heads_all, grads.shape[3]), grads.dtype)
    for k in range(count):
        piece = grads[:, k : k + 1]
        if k:
            piece = lax.ppermute(piece, "head", [(j, (j - k) % count) for j in range(count)])
        out = lax.dynamic_update_slice_in_dim(out, piece, ((me + k) % count) * owned, axis=2)
    return out


def sketch_parts(tokens, projector, pattern):
    inverse = tokens.shape[-1] ** (-0.5)
    sketch_one = jnp.einsum(pattern, tokens, projector[0], preferred_element_type=f32) * inverse
    sketch_two = jnp.einsum(pattern, tokens, projector[1], preferred_element_type=f32) * inverse
    return (sketch_one, sketch_two)


def tri_features(sketch_one, sketch_two, take_a, take_b):
    width = sketch_one.shape[-1]
    sketch = sketch_one * sketch_two
    first, second = take_pair(sketch, take_a, take_b)
    return (first * second * (1.0 / width)).astype(bf16)


def tri_feature_back(cotangent, sketch_one, sketch_two, proj_wide, take_a, take_b, off):
    width = sketch_one.shape[-1]
    sketch = sketch_one * sketch_two
    first, second = take_pair(sketch, take_a, take_b)
    spread = jnp.concatenate([cotangent * second, cotangent * first * off], axis=-1)
    gather = jnp.concatenate([take_a.T, take_b.T], axis=0).astype(bf16)
    dsketch = dot_parts("...k,ka->...a", spread, gather, 2) * (2.0 / width)
    one_hi, one_lo = split_parts(dsketch * sketch_two, 2)
    two_hi, two_lo = split_parts(dsketch * sketch_one, 2)
    proj = proj_wide.astype(bf16)
    back = jnp.einsum(
        "...k,dk->...d",
        jnp.concatenate([one_hi, one_lo, two_hi, two_lo], axis=-1),
        jnp.concatenate([proj[0], proj[0], proj[1], proj[1]], axis=-1),
        preferred_element_type=f32,
    )
    return back * proj_wide.shape[1] ** (-0.5)


def body(queries, keys, values, dout, signs):
    projector = (2 * signs - 1).astype(bf16)
    proj_wide = projector.astype(f32)
    width = signs.shape[-1]
    take_a_np, take_b_np, weight_np, off_np = triangle(width)
    take_a = jnp.asarray(take_a_np, bf16)
    take_b = jnp.asarray(take_b_np, bf16)
    weight = jnp.asarray(weight_np, bf16)
    off = jnp.asarray(off_np, f32)
    heads_all = keys.shape[1]
    owned = heads_all // lax.axis_size("head")
    offset = lax.axis_index("head") * owned
    key_part = lax.dynamic_slice_in_dim(keys, offset, owned, 1)
    value_part = lax.dynamic_slice_in_dim(values, offset, owned, 1)
    both = head_exchange(jnp.stack([queries, dout]), owned)
    query_part, grad_part = both[0], both[1]
    key_one, key_two = sketch_parts(key_part, projector, "thd,df->htf")
    key_feat = tri_features(key_one, key_two, take_a, take_b)
    key_wfeat = key_feat * weight
    value_heads = value_part.transpose(1, 0, 2)
    block_state = jnp.einsum("htf,htd->hfd", key_feat, value_heads, preferred_element_type=f32)
    block_total = jnp.sum(key_feat, 1, dtype=f32)
    state_in, total_in = ctx_scan(block_state, block_total, False)

    query_one, query_two = sketch_parts(query_part, projector, "tmhd,df->hmtf")
    query_feat = tri_features(query_one, query_two, take_a, take_b)
    query_wfeat = query_feat * weight
    grad_heads = grad_part.transpose(2, 1, 0, 3).astype(f32)
    length = key_feat.shape[1]
    causal = lax.broadcasted_iota(jnp.int32, (length, length), 0) >= lax.broadcasted_iota(
        jnp.int32, (length, length), 1
    )
    scores = jnp.where(
        causal,
        jnp.einsum("hmif,hjf->hmij", query_wfeat, key_feat, preferred_element_type=f32),
        0.0,
    )
    weights = scores.astype(bf16)
    numerator = jnp.einsum(
        "hmij,hjd->hmid", weights, value_heads, preferred_element_type=f32
    ) + dot_split("hmif,hfd->hmid", query_wfeat, state_in)
    denominator = 1.0 + jnp.sum(scores, -1) + dot_split("hmif,hf->hmi", query_wfeat, total_in)
    output_rows = numerator / denominator[..., None]
    grad_rows = grad_heads / denominator[..., None]
    grad_low = grad_rows.astype(bf16)
    correction = -jnp.sum(grad_rows * output_rows, -1)
    width_v = value_heads.shape[-1]
    corr_hi, corr_lo = split_parts(correction[..., None], 2)
    suffix_both = jnp.einsum(
        "hmif,hmid->hfd",
        query_feat,
        jnp.concatenate([grad_low, corr_hi, corr_lo], axis=-1),
        preferred_element_type=f32,
    )
    suffix_part = suffix_both[..., :width_v]
    suffix_sum = suffix_both[..., width_v] + suffix_both[..., width_v + 1]
    suffix_got = scan_send(suffix_part, suffix_sum)

    dscores = jnp.where(
        causal,
        jnp.einsum("hmid,hjd->hmij", grad_low, value_heads, preferred_element_type=f32)
        + correction[..., None],
        0.0,
    ).astype(bf16)
    grad_hi, grad_lo = split_parts(grad_rows, 2)
    state_hi, state_lo = split_parts(state_in.transpose(0, 2, 1), 2)
    grad_qfeat = (
        jnp.einsum(
            "hmik,hkf->hmif",
            jnp.concatenate([dscores, grad_hi, grad_hi, grad_lo], axis=-1),
            jnp.concatenate([key_feat, state_hi, state_lo, state_hi], axis=1),
            preferred_element_type=f32,
        )
        + correction[..., None] * total_in[:, None, None, :]
    )
    grad_kfeat = jnp.einsum("hmij,hmif->hjf", dscores, query_feat, preferred_element_type=f32)
    grad_value = jnp.einsum("hmij,hmid->hjd", weights, grad_low, preferred_element_type=f32)
    suffix_summed = scan_sum(suffix_got, True)
    suffix_summed, grad_qfeat, grad_kfeat, grad_value = lax.optimization_barrier(
        (suffix_summed, grad_qfeat, grad_kfeat, grad_value)
    )
    merged_state, merged_total = scan_return(suffix_summed, suffix_part.shape[0], suffix_part.shape[1])
    query_grad = tri_feature_back(
        grad_qfeat, query_one, query_two, proj_wide, take_a, take_b, off
    )
    query_low = query_grad.transpose(2, 1, 0, 3).astype(bf16)
    query_low, merged_state, merged_total = lax.optimization_barrier(
        (query_low, merged_state, merged_total)
    )
    query_out = head_return(query_low, heads_all)

    merged_hi, merged_lo = split_parts(merged_state.transpose(0, 2, 1), 2)
    kfeat_total = (
        grad_kfeat
        + jnp.einsum(
            "htk,hkf->htf",
            jnp.concatenate([value_heads, value_heads], axis=-1),
            jnp.concatenate([merged_hi, merged_lo], axis=1),
            preferred_element_type=f32,
        )
        + merged_total[:, None, :]
    )
    value_total = grad_value + dot_split("htf,hfd->htd", key_wfeat, merged_state)
    key_sum = tri_feature_back(kfeat_total, key_one, key_two, proj_wide, take_a, take_b, off)
    key_out = key_sum.transpose(1, 0, 2).astype(bf16)
    value_out = value_total.transpose(1, 0, 2).astype(bf16)
    return (query_out, key_out, value_out)


def solution(mesh):
    in_specs = (
        P("ctx", "head", None, None),
        P("ctx", None, None),
        P("ctx", None, None),
        P("ctx", "head", None, None),
        P(),
    )
    out_specs = (P("ctx", "head", None, None), P("ctx", "head", None), P("ctx", "head", None))
    return jax.shard_map(body, mesh=mesh, in_specs=in_specs, out_specs=out_specs, check_vma=False)
```

```python
import jax
import jax.numpy as jnp
import numpy as np
from jax import lax
from jax.sharding import PartitionSpec as P

highest = lax.Precision.HIGHEST
f32 = jnp.float32
bf16 = jnp.bfloat16


def triangle(width):
    rows, cols = np.triu_indices(width)
    take_a = np.eye(width, dtype=np.float32)[:, rows]
    take_b = np.eye(width, dtype=np.float32)[:, cols]
    weight = np.where(rows == cols, 1.0, 2.0).astype(np.float32)
    off = (rows != cols).astype(np.float32)
    return take_a, take_b, weight, off


def split_parts(x, count):
    parts = []
    rest = x
    for _ in range(count - 1):
        hi = lax.reduce_precision(rest, exponent_bits=8, mantissa_bits=7)
        parts.append(hi.astype(bf16))
        rest = rest - hi
    parts.append(rest.astype(bf16))
    return parts


def dot_parts(pattern, wide, other, count, wide_first=True):
    total = None
    for part in split_parts(wide, count):
        args = (part, other) if wide_first else (other, part)
        term = jnp.einsum(pattern, *args, preferred_element_type=f32)
        total = term if total is None else total + term
    return total


def dot_split(pattern, exact, wide):
    return dot_parts(pattern, wide, exact, 2, wide_first=False)


def take_pair(x, take_a, take_b):
    lhs = jnp.concatenate(split_parts(x, 3), axis=-1)
    both = jnp.concatenate([take_a, take_b], axis=1)
    rhs = jnp.concatenate([both, both, both], axis=0)
    out = jnp.einsum("...k,kn->...n", lhs, rhs, preferred_element_type=f32)
    size = take_a.shape[1]
    return out[..., :size], out[..., size:]


def scan_send(state, total):
    n = lax.axis_size("ctx")
    heads, feat, width = state.shape
    total_rows = -(-feat // width)
    flat = jnp.concatenate(
        [
            state.reshape(heads * feat, width),
            jnp.pad(total, ((0, 0), (0, total_rows * width - feat))).reshape(
                heads * total_rows, width
            ),
        ],
        axis=0,
    )
    rows = flat.shape[0]
    per = -(-rows // (n * 8)) * 8
    flat = jnp.pad(flat, ((0, n * per - rows), (0, 0)))
    return lax.all_to_all(flat.reshape(n, per, width), "ctx", 0, 0, tiled=True)


def scan_sum(got, reverse):
    n = got.shape[0]
    src = lax.broadcasted_iota(jnp.int32, (n, n), 1)
    dst = lax.broadcasted_iota(jnp.int32, (n, n), 0)
    mask = (src > dst if reverse else src < dst).astype(f32)
    return jnp.einsum("ij,jrc->irc", mask, got, precision=highest)


def scan_return(summed, heads, feat):
    n, per, width = summed.shape
    total_rows = -(-feat // width)
    back = lax.all_to_all(summed, "ctx", 0, 0, tiled=True).reshape(n * per, width)
    state_out = back[: heads * feat].reshape(heads, feat, width)
    total_out = back[heads * feat : heads * (feat + total_rows)].reshape(heads, total_rows * width)
    return state_out, total_out[:, :feat]


def ctx_scan(state, total, reverse):
    summed = scan_sum(scan_send(state, total), reverse)
    return scan_return(summed, state.shape[0], state.shape[1])


def head_exchange(stacked, owned):
    count = lax.axis_size("head")
    me = lax.axis_index("head")
    pieces = []
    for k in range(count):
        target = (me + k) % count
        piece = lax.dynamic_slice_in_dim(stacked, target * owned, owned, axis=3)
        if k:
            piece = lax.ppermute(piece, "head", [(j, (j + k) % count) for j in range(count)])
        pieces.append(piece)
    return jnp.concatenate(pieces, axis=2)


def head_return(grads, heads_all):
    count = lax.axis_size("head")
    me = lax.axis_index("head")
    pieces = []
    for k in range(count):
        piece = grads[:, k : k + 1]
        if k:
            piece = lax.ppermute(piece, "head", [(j, (j - k) % count) for j in range(count)])
        pieces.append(piece)
    blocks = [lax.select_n((b - me) % count, *pieces) for b in range(count)]
    return jnp.concatenate(blocks, axis=2)


def sketch_parts(tokens, projector, pattern):
    inverse = tokens.shape[-1] ** (-0.5)
    sketch_one = jnp.einsum(pattern, tokens, projector[0], preferred_element_type=f32) * inverse
    sketch_two = jnp.einsum(pattern, tokens, projector[1], preferred_element_type=f32) * inverse
    return (sketch_one, sketch_two)


def tri_features(sketch_one, sketch_two, take_a, take_b):
    width = sketch_one.shape[-1]
    sketch = sketch_one * sketch_two
    first, second = take_pair(sketch, take_a, take_b)
    return (first * second * (1.0 / width)).astype(bf16)


def tri_feature_back(cotangent, sketch_one, sketch_two, proj_wide, take_a, take_b, off):
    width = sketch_one.shape[-1]
    sketch = sketch_one * sketch_two
    first, second = take_pair(sketch, take_a, take_b)
    spread = jnp.concatenate([cotangent * second, cotangent * first * off], axis=-1)
    gather = jnp.concatenate([take_a.T, take_b.T], axis=0).astype(bf16)
    dsketch = dot_parts("...k,ka->...a", spread, gather, 2) * (2.0 / width)
    one_hi, one_lo = split_parts(dsketch * sketch_two, 2)
    two_hi, two_lo = split_parts(dsketch * sketch_one, 2)
    proj = proj_wide.astype(bf16)
    back = jnp.einsum(
        "...k,dk->...d",
        jnp.concatenate([one_hi, one_lo, two_hi, two_lo], axis=-1),
        jnp.concatenate([proj[0], proj[0], proj[1], proj[1]], axis=-1),
        preferred_element_type=f32,
    )
    return back * proj_wide.shape[1] ** (-0.5)


def body(queries, keys, values, dout, signs):
    projector = (2 * signs - 1).astype(bf16)
    proj_wide = projector.astype(f32)
    width = signs.shape[-1]
    take_a_np, take_b_np, weight_np, off_np = triangle(width)
    take_a = jnp.asarray(take_a_np, bf16)
    take_b = jnp.asarray(take_b_np, bf16)
    weight = jnp.asarray(weight_np, bf16)
    off = jnp.asarray(off_np, f32)
    heads_all = keys.shape[1]
    owned = heads_all // lax.axis_size("head")
    offset = lax.axis_index("head") * owned
    key_part = lax.dynamic_slice_in_dim(keys, offset, owned, 1)
    value_part = lax.dynamic_slice_in_dim(values, offset, owned, 1)
    both = head_exchange(jnp.stack([queries, dout]), owned)
    query_part, grad_part = both[0], both[1]
    key_one, key_two = sketch_parts(key_part, projector, "thd,df->htf")
    key_feat = tri_features(key_one, key_two, take_a, take_b)
    key_wfeat = key_feat * weight
    value_heads = value_part.transpose(1, 0, 2)
    block_state = jnp.einsum("htf,htd->hfd", key_feat, value_heads, preferred_element_type=f32)
    block_total = jnp.sum(key_feat, 1, dtype=f32)
    state_in, total_in = ctx_scan(block_state, block_total, False)

    query_one, query_two = sketch_parts(query_part, projector, "tmhd,df->hmtf")
    query_feat = tri_features(query_one, query_two, take_a, take_b)
    query_wfeat = query_feat * weight
    grad_heads = grad_part.transpose(2, 1, 0, 3).astype(f32)
    length = key_feat.shape[1]
    causal = lax.broadcasted_iota(jnp.int32, (length, length), 0) >= lax.broadcasted_iota(
        jnp.int32, (length, length), 1
    )
    scores = jnp.where(
        causal,
        jnp.einsum("hmif,hjf->hmij", query_wfeat, key_feat, preferred_element_type=f32),
        0.0,
    )
    weights = scores.astype(bf16)
    numerator = jnp.einsum(
        "hmij,hjd->hmid", weights, value_heads, preferred_element_type=f32
    ) + dot_split("hmif,hfd->hmid", query_wfeat, state_in)
    denominator = 1.0 + jnp.sum(scores, -1) + dot_split("hmif,hf->hmi", query_wfeat, total_in)
    output_rows = numerator / denominator[..., None]
    grad_rows = grad_heads / denominator[..., None]
    grad_low = grad_rows.astype(bf16)
    correction = -jnp.sum(grad_rows * output_rows, -1)
    suffix_part = jnp.einsum("hmif,hmid->hfd", query_feat, grad_low, preferred_element_type=f32)
    suffix_sum = dot_split("hmif,hmi->hf", query_feat, correction)
    suffix_got = scan_send(suffix_part, suffix_sum)

    dscores = jnp.where(
        causal,
        jnp.einsum("hmid,hjd->hmij", grad_low, value_heads, preferred_element_type=f32)
        + correction[..., None],
        0.0,
    ).astype(bf16)
    grad_hi, grad_lo = split_parts(grad_rows, 2)
    state_hi, state_lo = split_parts(state_in.transpose(0, 2, 1), 2)
    grad_qfeat = (
        jnp.einsum(
            "hmik,hkf->hmif",
            jnp.concatenate([dscores, grad_hi, grad_hi, grad_lo], axis=-1),
            jnp.concatenate([key_feat, state_hi, state_lo, state_hi], axis=1),
            preferred_element_type=f32,
        )
        + correction[..., None] * total_in[:, None, None, :]
    )
    grad_kfeat = jnp.einsum("hmij,hmif->hjf", dscores, query_feat, preferred_element_type=f32)
    grad_value = jnp.einsum("hmij,hmid->hjd", weights, grad_low, preferred_element_type=f32)
    suffix_summed = scan_sum(suffix_got, True)
    suffix_summed, grad_qfeat, grad_kfeat, grad_value = lax.optimization_barrier(
        (suffix_summed, grad_qfeat, grad_kfeat, grad_value)
    )
    merged_state, merged_total = scan_return(suffix_summed, suffix_part.shape[0], suffix_part.shape[1])
    query_grad = tri_feature_back(
        grad_qfeat, query_one, query_two, proj_wide, take_a, take_b, off
    )
    query_low = query_grad.transpose(2, 1, 0, 3).astype(bf16)
    query_low, merged_state, merged_total = lax.optimization_barrier(
        (query_low, merged_state, merged_total)
    )
    query_out = head_return(query_low, heads_all)

    merged_hi, merged_lo = split_parts(merged_state.transpose(0, 2, 1), 2)
    kfeat_total = (
        grad_kfeat
        + jnp.einsum(
            "htk,hkf->htf",
            jnp.concatenate([value_heads, value_heads], axis=-1),
            jnp.concatenate([merged_hi, merged_lo], axis=1),
            preferred_element_type=f32,
        )
        + merged_total[:, None, :]
    )
    value_total = grad_value + dot_split("htf,hfd->htd", key_wfeat, merged_state)
    key_sum = tri_feature_back(kfeat_total, key_one, key_two, proj_wide, take_a, take_b, off)
    key_out = key_sum.transpose(1, 0, 2).astype(bf16)
    value_out = value_total.transpose(1, 0, 2).astype(bf16)
    return (query_out, key_out, value_out)


def solution(mesh):
    in_specs = (
        P("ctx", "head", None, None),
        P("ctx", None, None),
        P("ctx", None, None),
        P("ctx", "head", None, None),
        P(),
    )
    out_specs = (P("ctx", "head", None, None), P("ctx", "head", None), P("ctx", "head", None))
    return jax.shard_map(body, mesh=mesh, in_specs=in_specs, out_specs=out_specs, check_vma=False)
```

```python
import jax
import jax.numpy as jnp
import numpy as np
from jax import lax
from jax.sharding import PartitionSpec as P

highest = lax.Precision.HIGHEST
f32 = jnp.float32
bf16 = jnp.bfloat16


def triangle(width):
    rows, cols = np.triu_indices(width)
    take_a = np.eye(width, dtype=np.float32)[:, rows]
    take_b = np.eye(width, dtype=np.float32)[:, cols]
    weight = np.where(rows == cols, 1.0, 2.0).astype(np.float32)
    off = (rows != cols).astype(np.float32)
    return take_a, take_b, weight, off


def split_parts(x, count):
    parts = []
    rest = x
    for _ in range(count - 1):
        hi = lax.reduce_precision(rest, exponent_bits=8, mantissa_bits=7)
        parts.append(hi.astype(bf16))
        rest = rest - hi
    parts.append(rest.astype(bf16))
    return parts


def dot_parts(pattern, wide, other, count, wide_first=True):
    total = None
    for part in split_parts(wide, count):
        args = (part, other) if wide_first else (other, part)
        term = jnp.einsum(pattern, *args, preferred_element_type=f32)
        total = term if total is None else total + term
    return total


def dot_split(pattern, exact, wide):
    return dot_parts(pattern, wide, exact, 2, wide_first=False)


def take_pair(x, take_a, take_b):
    lhs = jnp.concatenate(split_parts(x, 3), axis=-1)
    both = jnp.concatenate([take_a, take_b], axis=1)
    rhs = jnp.concatenate([both, both, both], axis=0)
    out = jnp.einsum("...k,kn->...n", lhs, rhs, preferred_element_type=f32)
    size = take_a.shape[1]
    return out[..., :size], out[..., size:]


def scan_send(state, total):
    n = lax.axis_size("ctx")
    heads, feat, width = state.shape
    total_rows = -(-feat // width)
    flat = jnp.concatenate(
        [
            state.reshape(heads * feat, width),
            jnp.pad(total, ((0, 0), (0, total_rows * width - feat))).reshape(
                heads * total_rows, width
            ),
        ],
        axis=0,
    )
    rows = flat.shape[0]
    per = -(-rows // (n * 8)) * 8
    flat = jnp.pad(flat, ((0, n * per - rows), (0, 0)))
    return lax.all_to_all(flat.reshape(n, per, width), "ctx", 0, 0, tiled=True)


def scan_sum(got, reverse):
    n = got.shape[0]
    src = lax.broadcasted_iota(jnp.int32, (n, n), 1)
    dst = lax.broadcasted_iota(jnp.int32, (n, n), 0)
    mask = (src > dst if reverse else src < dst).astype(f32)
    return jnp.einsum("ij,jrc->irc", mask, got, precision=highest)


def scan_return(summed, heads, feat):
    n, per, width = summed.shape
    total_rows = -(-feat // width)
    back = lax.all_to_all(summed, "ctx", 0, 0, tiled=True).reshape(n * per, width)
    state_out = back[: heads * feat].reshape(heads, feat, width)
    total_out = back[heads * feat : heads * (feat + total_rows)].reshape(heads, total_rows * width)
    return state_out, total_out[:, :feat]


def ctx_scan(state, total, reverse):
    summed = scan_sum(scan_send(state, total), reverse)
    return scan_return(summed, state.shape[0], state.shape[1])


def head_exchange(stacked, owned):
    count = lax.axis_size("head")
    me = lax.axis_index("head")
    pieces = []
    for k in range(count):
        blocks = [stacked[:, :, :, b * owned : (b + 1) * owned] for b in range(count)]
        piece = lax.select_n((me + k) % count, *blocks)
        if k:
            piece = lax.ppermute(piece, "head", [(j, (j + k) % count) for j in range(count)])
        pieces.append(piece)
    return jnp.concatenate(pieces, axis=2)


def head_return(grads, heads_all):
    count = lax.axis_size("head")
    me = lax.axis_index("head")
    pieces = []
    for k in range(count):
        piece = grads[:, k : k + 1]
        if k:
            piece = lax.ppermute(piece, "head", [(j, (j - k) % count) for j in range(count)])
        pieces.append(piece)
    blocks = [lax.select_n((b - me) % count, *pieces) for b in range(count)]
    return jnp.concatenate(blocks, axis=2)


def sketch_parts(tokens, projector, pattern):
    inverse = tokens.shape[-1] ** (-0.5)
    sketch_one = jnp.einsum(pattern, tokens, projector[0], preferred_element_type=f32) * inverse
    sketch_two = jnp.einsum(pattern, tokens, projector[1], preferred_element_type=f32) * inverse
    return (sketch_one, sketch_two)


def tri_features(sketch_one, sketch_two, take_a, take_b):
    width = sketch_one.shape[-1]
    sketch = sketch_one * sketch_two
    first, second = take_pair(sketch, take_a, take_b)
    return (first * second * (1.0 / width)).astype(bf16)


def tri_feature_back(cotangent, sketch_one, sketch_two, proj_wide, take_a, take_b, off):
    width = sketch_one.shape[-1]
    sketch = sketch_one * sketch_two
    first, second = take_pair(sketch, take_a, take_b)
    spread = jnp.concatenate([cotangent * second, cotangent * first * off], axis=-1)
    gather = jnp.concatenate([take_a.T, take_b.T], axis=0).astype(bf16)
    dsketch = dot_parts("...k,ka->...a", spread, gather, 2) * (2.0 / width)
    one_hi, one_lo = split_parts(dsketch * sketch_two, 2)
    two_hi, two_lo = split_parts(dsketch * sketch_one, 2)
    proj = proj_wide.astype(bf16)
    back = jnp.einsum(
        "...k,dk->...d",
        jnp.concatenate([one_hi, one_lo, two_hi, two_lo], axis=-1),
        jnp.concatenate([proj[0], proj[0], proj[1], proj[1]], axis=-1),
        preferred_element_type=f32,
    )
    return back * proj_wide.shape[1] ** (-0.5)


def body(queries, keys, values, dout, signs):
    projector = (2 * signs - 1).astype(bf16)
    proj_wide = projector.astype(f32)
    width = signs.shape[-1]
    take_a_np, take_b_np, weight_np, off_np = triangle(width)
    take_a = jnp.asarray(take_a_np, bf16)
    take_b = jnp.asarray(take_b_np, bf16)
    weight = jnp.asarray(weight_np, bf16)
    off = jnp.asarray(off_np, f32)
    heads_all = keys.shape[1]
    owned = heads_all // lax.axis_size("head")
    offset = lax.axis_index("head") * owned
    key_part = lax.dynamic_slice_in_dim(keys, offset, owned, 1)
    value_part = lax.dynamic_slice_in_dim(values, offset, owned, 1)
    both = head_exchange(jnp.stack([queries, dout]), owned)
    query_part, grad_part = both[0], both[1]
    key_one, key_two = sketch_parts(key_part, projector, "thd,df->htf")
    key_feat = tri_features(key_one, key_two, take_a, take_b)
    key_wfeat = key_feat * weight
    value_heads = value_part.transpose(1, 0, 2)
    block_state = jnp.einsum("htf,htd->hfd", key_feat, value_heads, preferred_element_type=f32)
    block_total = jnp.sum(key_feat, 1, dtype=f32)
    state_in, total_in = ctx_scan(block_state, block_total, False)

    query_one, query_two = sketch_parts(query_part, projector, "tmhd,df->hmtf")
    query_feat = tri_features(query_one, query_two, take_a, take_b)
    query_wfeat = query_feat * weight
    grad_heads = grad_part.transpose(2, 1, 0, 3).astype(f32)
    length = key_feat.shape[1]
    causal = lax.broadcasted_iota(jnp.int32, (length, length), 0) >= lax.broadcasted_iota(
        jnp.int32, (length, length), 1
    )
    scores = jnp.where(
        causal,
        jnp.einsum("hmif,hjf->hmij", query_wfeat, key_feat, preferred_element_type=f32),
        0.0,
    )
    weights = scores.astype(bf16)
    numerator = jnp.einsum(
        "hmij,hjd->hmid", weights, value_heads, preferred_element_type=f32
    ) + dot_split("hmif,hfd->hmid", query_wfeat, state_in)
    denominator = 1.0 + jnp.sum(scores, -1) + dot_split("hmif,hf->hmi", query_wfeat, total_in)
    output_rows = numerator / denominator[..., None]
    grad_rows = grad_heads / denominator[..., None]
    grad_low = grad_rows.astype(bf16)
    correction = -jnp.sum(grad_rows * output_rows, -1)
    suffix_part = jnp.einsum("hmif,hmid->hfd", query_feat, grad_low, preferred_element_type=f32)
    suffix_sum = dot_split("hmif,hmi->hf", query_feat, correction)
    suffix_got = scan_send(suffix_part, suffix_sum)

    dscores = jnp.where(
        causal,
        jnp.einsum("hmid,hjd->hmij", grad_low, value_heads, preferred_element_type=f32)
        + correction[..., None],
        0.0,
    ).astype(bf16)
    grad_hi, grad_lo = split_parts(grad_rows, 2)
    state_hi, state_lo = split_parts(state_in.transpose(0, 2, 1), 2)
    grad_qfeat = (
        jnp.einsum(
            "hmik,hkf->hmif",
            jnp.concatenate([dscores, grad_hi, grad_hi, grad_lo], axis=-1),
            jnp.concatenate([key_feat, state_hi, state_lo, state_hi], axis=1),
            preferred_element_type=f32,
        )
        + correction[..., None] * total_in[:, None, None, :]
    )
    grad_kfeat = jnp.einsum("hmij,hmif->hjf", dscores, query_feat, preferred_element_type=f32)
    grad_value = jnp.einsum("hmij,hmid->hjd", weights, grad_low, preferred_element_type=f32)
    suffix_summed = scan_sum(suffix_got, True)
    suffix_summed, grad_qfeat, grad_kfeat, grad_value = lax.optimization_barrier(
        (suffix_summed, grad_qfeat, grad_kfeat, grad_value)
    )
    merged_state, merged_total = scan_return(suffix_summed, suffix_part.shape[0], suffix_part.shape[1])
    query_grad = tri_feature_back(
        grad_qfeat, query_one, query_two, proj_wide, take_a, take_b, off
    )
    query_low = query_grad.transpose(2, 1, 0, 3).astype(bf16)
    query_low, merged_state, merged_total = lax.optimization_barrier(
        (query_low, merged_state, merged_total)
    )
    query_out = head_return(query_low, heads_all)

    merged_hi, merged_lo = split_parts(merged_state.transpose(0, 2, 1), 2)
    kfeat_total = (
        grad_kfeat
        + jnp.einsum(
            "htk,hkf->htf",
            jnp.concatenate([value_heads, value_heads], axis=-1),
            jnp.concatenate([merged_hi, merged_lo], axis=1),
            preferred_element_type=f32,
        )
        + merged_total[:, None, :]
    )
    value_total = grad_value + dot_split("htf,hfd->htd", key_wfeat, merged_state)
    key_sum = tri_feature_back(kfeat_total, key_one, key_two, proj_wide, take_a, take_b, off)
    key_out = key_sum.transpose(1, 0, 2).astype(bf16)
    value_out = value_total.transpose(1, 0, 2).astype(bf16)
    return (query_out, key_out, value_out)


def solution(mesh):
    in_specs = (
        P("ctx", "head", None, None),
        P("ctx", None, None),
        P("ctx", None, None),
        P("ctx", "head", None, None),
        P(),
    )
    out_specs = (P("ctx", "head", None, None), P("ctx", "head", None), P("ctx", "head", None))
    return jax.shard_map(body, mesh=mesh, in_specs=in_specs, out_specs=out_specs, check_vma=False)
```

```python
import jax
import jax.numpy as jnp
import numpy as np
from jax import lax
from jax.sharding import PartitionSpec as P

highest = lax.Precision.HIGHEST
f32 = jnp.float32
bf16 = jnp.bfloat16


def triangle(width):
    rows, cols = np.triu_indices(width)
    take_a = np.eye(width, dtype=np.float32)[:, rows]
    take_b = np.eye(width, dtype=np.float32)[:, cols]
    weight = np.where(rows == cols, 1.0, 2.0).astype(np.float32)
    off = (rows != cols).astype(np.float32)
    return take_a, take_b, weight, off


def split_parts(x, count):
    parts = []
    rest = x
    for _ in range(count - 1):
        hi = lax.reduce_precision(rest, exponent_bits=8, mantissa_bits=7)
        parts.append(hi.astype(bf16))
        rest = rest - hi
    parts.append(rest.astype(bf16))
    return parts


def dot_parts(pattern, wide, other, count, wide_first=True):
    total = None
    for part in split_parts(wide, count):
        args = (part, other) if wide_first else (other, part)
        term = jnp.einsum(pattern, *args, preferred_element_type=f32)
        total = term if total is None else total + term
    return total


def dot_split(pattern, exact, wide):
    return dot_parts(pattern, wide, exact, 2, wide_first=False)


def take_pair(x, take_a, take_b):
    lhs = jnp.concatenate(split_parts(x, 3), axis=-1)
    both = jnp.concatenate([take_a, take_b], axis=1)
    rhs = jnp.concatenate([both, both, both], axis=0)
    out = jnp.einsum("...k,kn->...n", lhs, rhs, preferred_element_type=f32)
    size = take_a.shape[1]
    return out[..., :size], out[..., size:]


def scan_send(state, total):
    n = lax.axis_size("ctx")
    heads, feat, width = state.shape
    total_rows = -(-feat // width)
    flat = jnp.concatenate(
        [
            state.reshape(heads * feat, width),
            jnp.pad(total, ((0, 0), (0, total_rows * width - feat))).reshape(
                heads * total_rows, width
            ),
        ],
        axis=0,
    )
    rows = flat.shape[0]
    per = -(-rows // (n * 8)) * 8
    flat = jnp.pad(flat, ((0, n * per - rows), (0, 0)))
    return lax.all_to_all(flat.reshape(n, per, width), "ctx", 0, 0, tiled=True)


def scan_sum(got, reverse):
    n = got.shape[0]
    src = lax.broadcasted_iota(jnp.int32, (n, n), 1)
    dst = lax.broadcasted_iota(jnp.int32, (n, n), 0)
    mask = (src > dst if reverse else src < dst).astype(bf16)
    return jnp.einsum(
        "ij,jrc->irc",
        jnp.concatenate([mask, mask, mask], axis=1),
        jnp.concatenate(split_parts(got, 3), axis=0),
        preferred_element_type=f32,
    )


def scan_return(summed, heads, feat):
    n, per, width = summed.shape
    total_rows = -(-feat // width)
    back = lax.all_to_all(summed, "ctx", 0, 0, tiled=True).reshape(n * per, width)
    state_out = back[: heads * feat].reshape(heads, feat, width)
    total_out = back[heads * feat : heads * (feat + total_rows)].reshape(heads, total_rows * width)
    return state_out, total_out[:, :feat]


def ctx_scan(state, total, reverse):
    summed = scan_sum(scan_send(state, total), reverse)
    return scan_return(summed, state.shape[0], state.shape[1])


def head_exchange(stacked, owned):
    count = lax.axis_size("head")
    me = lax.axis_index("head")
    pieces = []
    for k in range(count):
        blocks = [stacked[:, :, :, b * owned : (b + 1) * owned] for b in range(count)]
        piece = lax.select_n((me + k) % count, *blocks)
        if k:
            piece = lax.ppermute(piece, "head", [(j, (j + k) % count) for j in range(count)])
        pieces.append(piece)
    return jnp.concatenate(pieces, axis=2)


def head_return(grads, heads_all):
    count = lax.axis_size("head")
    me = lax.axis_index("head")
    pieces = []
    for k in range(count):
        piece = grads[:, k : k + 1]
        if k:
            piece = lax.ppermute(piece, "head", [(j, (j - k) % count) for j in range(count)])
        pieces.append(piece)
    blocks = [lax.select_n((b - me) % count, *pieces) for b in range(count)]
    return jnp.concatenate(blocks, axis=2)


def sketch_parts(tokens, projector, pattern):
    inverse = tokens.shape[-1] ** (-0.5)
    sketch_one = jnp.einsum(pattern, tokens, projector[0], preferred_element_type=f32) * inverse
    sketch_two = jnp.einsum(pattern, tokens, projector[1], preferred_element_type=f32) * inverse
    return (sketch_one, sketch_two)


def tri_features(sketch_one, sketch_two, take_a, take_b):
    width = sketch_one.shape[-1]
    sketch = sketch_one * sketch_two
    first, second = take_pair(sketch, take_a, take_b)
    return (first * second * (1.0 / width)).astype(bf16)


def tri_feature_back(cotangent, sketch_one, sketch_two, proj_wide, take_a, take_b, off):
    width = sketch_one.shape[-1]
    sketch = sketch_one * sketch_two
    first, second = take_pair(sketch, take_a, take_b)
    spread = jnp.concatenate([cotangent * second, cotangent * first * off], axis=-1)
    gather = jnp.concatenate([take_a.T, take_b.T], axis=0).astype(bf16)
    dsketch = dot_parts("...k,ka->...a", spread, gather, 2) * (2.0 / width)
    one_hi, one_lo = split_parts(dsketch * sketch_two, 2)
    two_hi, two_lo = split_parts(dsketch * sketch_one, 2)
    proj = proj_wide.astype(bf16)
    back = jnp.einsum(
        "...k,dk->...d",
        jnp.concatenate([one_hi, one_lo, two_hi, two_lo], axis=-1),
        jnp.concatenate([proj[0], proj[0], proj[1], proj[1]], axis=-1),
        preferred_element_type=f32,
    )
    return back * proj_wide.shape[1] ** (-0.5)


def body(queries, keys, values, dout, signs):
    projector = (2 * signs - 1).astype(bf16)
    proj_wide = projector.astype(f32)
    width = signs.shape[-1]
    take_a_np, take_b_np, weight_np, off_np = triangle(width)
    take_a = jnp.asarray(take_a_np, bf16)
    take_b = jnp.asarray(take_b_np, bf16)
    weight = jnp.asarray(weight_np, bf16)
    off = jnp.asarray(off_np, f32)
    heads_all = keys.shape[1]
    owned = heads_all // lax.axis_size("head")
    offset = lax.axis_index("head") * owned
    key_part = lax.dynamic_slice_in_dim(keys, offset, owned, 1)
    value_part = lax.dynamic_slice_in_dim(values, offset, owned, 1)
    both = head_exchange(jnp.stack([queries, dout]), owned)
    query_part, grad_part = both[0], both[1]
    key_one, key_two = sketch_parts(key_part, projector, "thd,df->htf")
    key_feat = tri_features(key_one, key_two, take_a, take_b)
    key_wfeat = key_feat * weight
    value_heads = value_part.transpose(1, 0, 2)
    block_state = jnp.einsum("htf,htd->hfd", key_feat, value_heads, preferred_element_type=f32)
    block_total = jnp.sum(key_feat, 1, dtype=f32)
    state_in, total_in = ctx_scan(block_state, block_total, False)

    query_one, query_two = sketch_parts(query_part, projector, "tmhd,df->hmtf")
    query_feat = tri_features(query_one, query_two, take_a, take_b)
    query_wfeat = query_feat * weight
    grad_heads = grad_part.transpose(2, 1, 0, 3).astype(f32)
    length = key_feat.shape[1]
    causal = lax.broadcasted_iota(jnp.int32, (length, length), 0) >= lax.broadcasted_iota(
        jnp.int32, (length, length), 1
    )
    scores = jnp.where(
        causal,
        jnp.einsum("hmif,hjf->hmij", query_wfeat, key_feat, preferred_element_type=f32),
        0.0,
    )
    weights = scores.astype(bf16)
    numerator = jnp.einsum(
        "hmij,hjd->hmid", weights, value_heads, preferred_element_type=f32
    ) + dot_split("hmif,hfd->hmid", query_wfeat, state_in)
    denominator = 1.0 + jnp.sum(scores, -1) + dot_split("hmif,hf->hmi", query_wfeat, total_in)
    output_rows = numerator / denominator[..., None]
    grad_rows = grad_heads / denominator[..., None]
    grad_low = grad_rows.astype(bf16)
    correction = -jnp.sum(grad_rows * output_rows, -1)
    suffix_part = jnp.einsum("hmif,hmid->hfd", query_feat, grad_low, preferred_element_type=f32)
    suffix_sum = dot_split("hmif,hmi->hf", query_feat, correction)
    suffix_got = scan_send(suffix_part, suffix_sum)

    dscores = jnp.where(
        causal,
        jnp.einsum("hmid,hjd->hmij", grad_low, value_heads, preferred_element_type=f32)
        + correction[..., None],
        0.0,
    ).astype(bf16)
    grad_hi, grad_lo = split_parts(grad_rows, 2)
    state_hi, state_lo = split_parts(state_in.transpose(0, 2, 1), 2)
    grad_qfeat = (
        jnp.einsum(
            "hmik,hkf->hmif",
            jnp.concatenate([dscores, grad_hi, grad_hi, grad_lo], axis=-1),
            jnp.concatenate([key_feat, state_hi, state_lo, state_hi], axis=1),
            preferred_element_type=f32,
        )
        + correction[..., None] * total_in[:, None, None, :]
    )
    grad_kfeat = jnp.einsum("hmij,hmif->hjf", dscores, query_feat, preferred_element_type=f32)
    grad_value = jnp.einsum("hmij,hmid->hjd", weights, grad_low, preferred_element_type=f32)
    suffix_summed = scan_sum(suffix_got, True)
    suffix_summed, grad_qfeat, grad_kfeat, grad_value = lax.optimization_barrier(
        (suffix_summed, grad_qfeat, grad_kfeat, grad_value)
    )
    merged_state, merged_total = scan_return(suffix_summed, suffix_part.shape[0], suffix_part.shape[1])
    query_grad = tri_feature_back(
        grad_qfeat, query_one, query_two, proj_wide, take_a, take_b, off
    )
    query_low = query_grad.transpose(2, 1, 0, 3).astype(bf16)
    query_low, merged_state, merged_total = lax.optimization_barrier(
        (query_low, merged_state, merged_total)
    )
    query_out = head_return(query_low, heads_all)

    merged_hi, merged_lo = split_parts(merged_state.transpose(0, 2, 1), 2)
    kfeat_total = (
        grad_kfeat
        + jnp.einsum(
            "htk,hkf->htf",
            jnp.concatenate([value_heads, value_heads], axis=-1),
            jnp.concatenate([merged_hi, merged_lo], axis=1),
            preferred_element_type=f32,
        )
        + merged_total[:, None, :]
    )
    value_total = grad_value + dot_split("htf,hfd->htd", key_wfeat, merged_state)
    key_sum = tri_feature_back(kfeat_total, key_one, key_two, proj_wide, take_a, take_b, off)
    key_out = key_sum.transpose(1, 0, 2).astype(bf16)
    value_out = value_total.transpose(1, 0, 2).astype(bf16)
    return (query_out, key_out, value_out)


def solution(mesh):
    in_specs = (
        P("ctx", "head", None, None),
        P("ctx", None, None),
        P("ctx", None, None),
        P("ctx", "head", None, None),
        P(),
    )
    out_specs = (P("ctx", "head", None, None), P("ctx", "head", None), P("ctx", "head", None))
    return jax.shard_map(body, mesh=mesh, in_specs=in_specs, out_specs=out_specs, check_vma=False)
```

```python
import jax
import jax.numpy as jnp
import numpy as np
from jax import lax
from jax.sharding import PartitionSpec as P

highest = lax.Precision.HIGHEST
f32 = jnp.float32
bf16 = jnp.bfloat16


def triangle(width):
    rows, cols = np.triu_indices(width)
    take_a = np.eye(width, dtype=np.float32)[:, rows]
    take_b = np.eye(width, dtype=np.float32)[:, cols]
    weight = np.where(rows == cols, 1.0, 2.0).astype(np.float32)
    off = (rows != cols).astype(np.float32)
    return take_a, take_b, weight, off


def split_parts(x, count):
    parts = []
    rest = x
    for _ in range(count - 1):
        hi = lax.reduce_precision(rest, exponent_bits=8, mantissa_bits=7)
        parts.append(hi.astype(bf16))
        rest = rest - hi
    parts.append(rest.astype(bf16))
    return parts


def dot_parts(pattern, wide, other, count, wide_first=True):
    total = None
    for part in split_parts(wide, count):
        args = (part, other) if wide_first else (other, part)
        term = jnp.einsum(pattern, *args, preferred_element_type=f32)
        total = term if total is None else total + term
    return total


def dot_split(pattern, exact, wide):
    return dot_parts(pattern, wide, exact, 2, wide_first=False)


def take_pair(x, take_a, take_b):
    lhs = jnp.concatenate(split_parts(x, 3), axis=-1)
    both = jnp.concatenate([take_a, take_b], axis=1)
    rhs = jnp.concatenate([both, both, both], axis=0)
    out = jnp.einsum("...k,kn->...n", lhs, rhs, preferred_element_type=f32)
    size = take_a.shape[1]
    return out[..., :size], out[..., size:]


def scan_send(state, total):
    n = lax.axis_size("ctx")
    heads, feat, width = state.shape
    total_rows = -(-feat // width)
    flat = jnp.concatenate(
        [
            state.reshape(heads * feat, width),
            jnp.pad(total, ((0, 0), (0, total_rows * width - feat))).reshape(
                heads * total_rows, width
            ),
        ],
        axis=0,
    )
    rows = flat.shape[0]
    per = -(-rows // (n * 8)) * 8
    flat = jnp.pad(flat, ((0, n * per - rows), (0, 0)))
    return lax.all_to_all(flat.reshape(n, per, width), "ctx", 0, 0, tiled=True)


def scan_sum(got, reverse):
    n = got.shape[0]
    src = lax.broadcasted_iota(jnp.int32, (n, n), 1)
    dst = lax.broadcasted_iota(jnp.int32, (n, n), 0)
    mask = (src > dst if reverse else src < dst).astype(f32)
    return jnp.einsum("ij,jrc->irc", mask, got, precision=highest)


def scan_return(summed, heads, feat):
    n, per, width = summed.shape
    total_rows = -(-feat // width)
    back = lax.all_to_all(summed, "ctx", 0, 0, tiled=True).reshape(n * per, width)
    state_out = back[: heads * feat].reshape(heads, feat, width)
    total_out = back[heads * feat : heads * (feat + total_rows)].reshape(heads, total_rows * width)
    return state_out, total_out[:, :feat]


def ctx_scan(state, total, reverse):
    summed = scan_sum(scan_send(state, total), reverse)
    return scan_return(summed, state.shape[0], state.shape[1])


def head_exchange(stacked, owned):
    count = lax.axis_size("head")
    me = lax.axis_index("head")
    pieces = []
    for k in range(count):
        blocks = [stacked[:, :, :, b * owned : (b + 1) * owned] for b in range(count)]
        piece = lax.select_n((me + k) % count, *blocks)
        if k:
            piece = lax.ppermute(piece, "head", [(j, (j + k) % count) for j in range(count)])
        pieces.append(piece)
    return jnp.concatenate(pieces, axis=2)


def head_return(grads, heads_all):
    count = lax.axis_size("head")
    me = lax.axis_index("head")
    pieces = []
    for k in range(count):
        piece = grads[:, k : k + 1]
        if k:
            piece = lax.ppermute(piece, "head", [(j, (j - k) % count) for j in range(count)])
        pieces.append(piece)
    blocks = [lax.select_n((b - me) % count, *pieces) for b in range(count)]
    return jnp.concatenate(blocks, axis=2)


def sketch_parts(tokens, projector, pattern):
    inverse = tokens.shape[-1] ** (-0.5)
    sketch_one = jnp.einsum(pattern, tokens, projector[0], preferred_element_type=f32) * inverse
    sketch_two = jnp.einsum(pattern, tokens, projector[1], preferred_element_type=f32) * inverse
    return (sketch_one, sketch_two)


def tri_features(sketch_one, sketch_two, take_a, take_b):
    width = sketch_one.shape[-1]
    sketch = sketch_one * sketch_two
    first, second = take_pair(sketch, take_a, take_b)
    return (first * second * (1.0 / width)).astype(bf16)


def tri_feature_back(cotangent, sketch_one, sketch_two, proj_wide, take_a, take_b, off):
    width = sketch_one.shape[-1]
    sketch = sketch_one * sketch_two
    first, second = take_pair(sketch, take_a, take_b)
    spread = jnp.concatenate([cotangent * second, cotangent * first * off], axis=-1)
    gather = jnp.concatenate([take_a.T, take_b.T], axis=0).astype(bf16)
    dsketch = dot_parts("...k,ka->...a", spread, gather, 2) * (2.0 / width)
    one_hi, one_lo = split_parts(dsketch * sketch_two, 2)
    two_hi, two_lo = split_parts(dsketch * sketch_one, 2)
    proj = proj_wide.astype(bf16)
    back = jnp.einsum(
        "...k,dk->...d",
        jnp.concatenate([one_hi, one_lo, two_hi, two_lo], axis=-1),
        jnp.concatenate([proj[0], proj[0], proj[1], proj[1]], axis=-1),
        preferred_element_type=f32,
    )
    return back * proj_wide.shape[1] ** (-0.5)


def body(queries, keys, values, dout, signs):
    projector = (2 * signs - 1).astype(bf16)
    proj_wide = projector.astype(f32)
    width = signs.shape[-1]
    take_a_np, take_b_np, weight_np, off_np = triangle(width)
    take_a = jnp.asarray(take_a_np, bf16)
    take_b = jnp.asarray(take_b_np, bf16)
    weight = jnp.asarray(weight_np, bf16)
    off = jnp.asarray(off_np, f32)
    heads_all = keys.shape[1]
    owned = heads_all // lax.axis_size("head")
    offset = lax.axis_index("head") * owned
    groups = heads_all // owned
    me_head = lax.axis_index("head")
    key_part = lax.select_n(me_head, *[keys[:, b * owned : (b + 1) * owned] for b in range(groups)])
    value_part = lax.select_n(
        me_head, *[values[:, b * owned : (b + 1) * owned] for b in range(groups)]
    )
    both = head_exchange(jnp.stack([queries, dout]), owned)
    query_part, grad_part = both[0], both[1]
    key_one, key_two = sketch_parts(key_part, projector, "thd,df->htf")
    key_feat = tri_features(key_one, key_two, take_a, take_b)
    key_wfeat = key_feat * weight
    value_heads = value_part.transpose(1, 0, 2)
    block_state = jnp.einsum("htf,htd->hfd", key_feat, value_heads, preferred_element_type=f32)
    block_total = jnp.sum(key_feat, 1, dtype=f32)
    state_in, total_in = ctx_scan(block_state, block_total, False)

    query_one, query_two = sketch_parts(query_part, projector, "tmhd,df->hmtf")
    query_feat = tri_features(query_one, query_two, take_a, take_b)
    query_wfeat = query_feat * weight
    grad_heads = grad_part.transpose(2, 1, 0, 3).astype(f32)
    length = key_feat.shape[1]
    causal = lax.broadcasted_iota(jnp.int32, (length, length), 0) >= lax.broadcasted_iota(
        jnp.int32, (length, length), 1
    )
    scores = jnp.where(
        causal,
        jnp.einsum("hmif,hjf->hmij", query_wfeat, key_feat, preferred_element_type=f32),
        0.0,
    )
    weights = scores.astype(bf16)
    numerator = jnp.einsum(
        "hmij,hjd->hmid", weights, value_heads, preferred_element_type=f32
    ) + dot_split("hmif,hfd->hmid", query_wfeat, state_in)
    denominator = 1.0 + jnp.sum(scores, -1) + dot_split("hmif,hf->hmi", query_wfeat, total_in)
    output_rows = numerator / denominator[..., None]
    grad_rows = grad_heads / denominator[..., None]
    grad_low = grad_rows.astype(bf16)
    correction = -jnp.sum(grad_rows * output_rows, -1)
    suffix_part = jnp.einsum("hmif,hmid->hfd", query_feat, grad_low, preferred_element_type=f32)
    suffix_sum = dot_split("hmif,hmi->hf", query_feat, correction)
    suffix_got = scan_send(suffix_part, suffix_sum)

    dscores = jnp.where(
        causal,
        jnp.einsum("hmid,hjd->hmij", grad_low, value_heads, preferred_element_type=f32)
        + correction[..., None],
        0.0,
    ).astype(bf16)
    grad_hi, grad_lo = split_parts(grad_rows, 2)
    state_hi, state_lo = split_parts(state_in.transpose(0, 2, 1), 2)
    grad_qfeat = (
        jnp.einsum(
            "hmik,hkf->hmif",
            jnp.concatenate([dscores, grad_hi, grad_hi, grad_lo], axis=-1),
            jnp.concatenate([key_feat, state_hi, state_lo, state_hi], axis=1),
            preferred_element_type=f32,
        )
        + correction[..., None] * total_in[:, None, None, :]
    )
    grad_kfeat = jnp.einsum("hmij,hmif->hjf", dscores, query_feat, preferred_element_type=f32)
    grad_value = jnp.einsum("hmij,hmid->hjd", weights, grad_low, preferred_element_type=f32)
    suffix_summed = scan_sum(suffix_got, True)
    suffix_summed, grad_qfeat, grad_kfeat, grad_value = lax.optimization_barrier(
        (suffix_summed, grad_qfeat, grad_kfeat, grad_value)
    )
    merged_state, merged_total = scan_return(suffix_summed, suffix_part.shape[0], suffix_part.shape[1])
    query_grad = tri_feature_back(
        grad_qfeat, query_one, query_two, proj_wide, take_a, take_b, off
    )
    query_low = query_grad.transpose(2, 1, 0, 3).astype(bf16)
    query_low, merged_state, merged_total = lax.optimization_barrier(
        (query_low, merged_state, merged_total)
    )
    query_out = head_return(query_low, heads_all)

    merged_hi, merged_lo = split_parts(merged_state.transpose(0, 2, 1), 2)
    kfeat_total = (
        grad_kfeat
        + jnp.einsum(
            "htk,hkf->htf",
            jnp.concatenate([value_heads, value_heads], axis=-1),
            jnp.concatenate([merged_hi, merged_lo], axis=1),
            preferred_element_type=f32,
        )
        + merged_total[:, None, :]
    )
    value_total = grad_value + dot_split("htf,hfd->htd", key_wfeat, merged_state)
    key_sum = tri_feature_back(kfeat_total, key_one, key_two, proj_wide, take_a, take_b, off)
    key_out = key_sum.transpose(1, 0, 2).astype(bf16)
    value_out = value_total.transpose(1, 0, 2).astype(bf16)
    return (query_out, key_out, value_out)


def solution(mesh):
    in_specs = (
        P("ctx", "head", None, None),
        P("ctx", None, None),
        P("ctx", None, None),
        P("ctx", "head", None, None),
        P(),
    )
    out_specs = (P("ctx", "head", None, None), P("ctx", "head", None), P("ctx", "head", None))
    return jax.shard_map(body, mesh=mesh, in_specs=in_specs, out_specs=out_specs, check_vma=False)
```

```python
import jax
import jax.numpy as jnp
import numpy as np
from jax import lax
from jax.sharding import PartitionSpec as P

highest = lax.Precision.HIGHEST
f32 = jnp.float32
bf16 = jnp.bfloat16


def triangle(width):
    rows, cols = np.triu_indices(width)
    take_a = np.eye(width, dtype=np.float32)[:, rows]
    take_b = np.eye(width, dtype=np.float32)[:, cols]
    weight = np.where(rows == cols, 1.0, 2.0).astype(np.float32)
    off = (rows != cols).astype(np.float32)
    return take_a, take_b, weight, off


def split_parts(x, count):
    parts = []
    rest = x
    for _ in range(count - 1):
        hi = lax.reduce_precision(rest, exponent_bits=8, mantissa_bits=7)
        parts.append(hi.astype(bf16))
        rest = rest - hi
    parts.append(rest.astype(bf16))
    return parts


def dot_parts(pattern, wide, other, count, wide_first=True):
    total = None
    for part in split_parts(wide, count):
        args = (part, other) if wide_first else (other, part)
        term = jnp.einsum(pattern, *args, preferred_element_type=f32)
        total = term if total is None else total + term
    return total


def dot_split(pattern, exact, wide):
    return dot_parts(pattern, wide, exact, 2, wide_first=False)


def take_pair(x, take_a, take_b):
    lhs = jnp.concatenate(split_parts(x, 3), axis=-1)
    both = jnp.concatenate([take_a, take_b], axis=1)
    rhs = jnp.concatenate([both, both, both], axis=0)
    out = jnp.einsum("...k,kn->...n", lhs, rhs, preferred_element_type=f32)
    size = take_a.shape[1]
    return out[..., :size], out[..., size:]


def scan_send(state, total):
    n = lax.axis_size("ctx")
    heads, feat, width = state.shape
    total_rows = -(-feat // width)
    flat = jnp.concatenate(
        [
            state.reshape(heads * feat, width),
            jnp.pad(total, ((0, 0), (0, total_rows * width - feat))).reshape(
                heads * total_rows, width
            ),
        ],
        axis=0,
    )
    rows = flat.shape[0]
    per = -(-rows // (n * 8)) * 8
    flat = jnp.pad(flat, ((0, n * per - rows), (0, 0)))
    return lax.all_to_all(flat.reshape(n, per, width), "ctx", 0, 0, tiled=True)


def scan_sum(got, reverse):
    n = got.shape[0]
    src = lax.broadcasted_iota(jnp.int32, (n, n), 1)
    dst = lax.broadcasted_iota(jnp.int32, (n, n), 0)
    mask = (src > dst if reverse else src < dst).astype(f32)
    return jnp.einsum("ij,jrc->irc", mask, got, precision=highest)


def scan_return(summed, heads, feat):
    n, per, width = summed.shape
    total_rows = -(-feat // width)
    back = lax.all_to_all(summed, "ctx", 0, 0, tiled=True).reshape(n * per, width)
    state_out = back[: heads * feat].reshape(heads, feat, width)
    total_out = back[heads * feat : heads * (feat + total_rows)].reshape(heads, total_rows * width)
    return state_out, total_out[:, :feat]


def ctx_scan(state, total, reverse):
    summed = scan_sum(scan_send(state, total), reverse)
    return scan_return(summed, state.shape[0], state.shape[1])


def head_exchange(stacked, owned):
    count = lax.axis_size("head")
    me = lax.axis_index("head")
    pieces = []
    for k in range(count):
        blocks = [stacked[:, :, :, b * owned : (b + 1) * owned] for b in range(count)]
        piece = lax.select_n((me + k) % count, *blocks)
        if k:
            piece = lax.ppermute(piece, "head", [(j, (j + k) % count) for j in range(count)])
        pieces.append(piece)
    return jnp.concatenate(pieces, axis=2)


def head_return(grads, heads_all):
    count = lax.axis_size("head")
    me = lax.axis_index("head")
    pieces = []
    for k in range(count):
        piece = grads[:, k : k + 1]
        if k:
            piece = lax.ppermute(piece, "head", [(j, (j - k) % count) for j in range(count)])
        pieces.append(piece)
    blocks = [lax.select_n((b - me) % count, *pieces) for b in range(count)]
    return jnp.concatenate(blocks, axis=2)


def sketch_parts(tokens, projector, pattern):
    inverse = tokens.shape[-1] ** (-0.5)
    sketch_one = jnp.einsum(pattern, tokens, projector[0], preferred_element_type=f32) * inverse
    sketch_two = jnp.einsum(pattern, tokens, projector[1], preferred_element_type=f32) * inverse
    return (sketch_one, sketch_two)


def tri_features(sketch_one, sketch_two, take_a, take_b):
    width = sketch_one.shape[-1]
    sketch = sketch_one * sketch_two
    first, second = take_pair(sketch, take_a, take_b)
    return (first * second * (1.0 / width)).astype(bf16)


def tri_feature_back(cotangent, sketch_one, sketch_two, proj_wide, take_a, take_b, off):
    width = sketch_one.shape[-1]
    sketch = sketch_one * sketch_two
    first, second = take_pair(sketch, take_a, take_b)
    spread = jnp.concatenate([cotangent * second, cotangent * first * off], axis=-1)
    gather = jnp.concatenate([take_a.T, take_b.T], axis=0).astype(bf16)
    dsketch = dot_parts("...k,ka->...a", spread, gather, 2) * (2.0 / width)
    one_hi, one_lo = split_parts(dsketch * sketch_two, 2)
    two_hi, two_lo = split_parts(dsketch * sketch_one, 2)
    proj = proj_wide.astype(bf16)
    back = jnp.einsum(
        "...k,dk->...d",
        jnp.concatenate([one_hi, one_lo, two_hi, two_lo], axis=-1),
        jnp.concatenate([proj[0], proj[0], proj[1], proj[1]], axis=-1),
        preferred_element_type=f32,
    )
    return back * proj_wide.shape[1] ** (-0.5)


def body(queries, keys, values, dout, signs):
    projector = (2 * signs - 1).astype(bf16)
    proj_wide = projector.astype(f32)
    width = signs.shape[-1]
    take_a_np, take_b_np, weight_np, off_np = triangle(width)
    take_a = jnp.asarray(take_a_np, bf16)
    take_b = jnp.asarray(take_b_np, bf16)
    weight = jnp.asarray(weight_np, bf16)
    off = jnp.asarray(off_np, f32)
    heads_all = keys.shape[1]
    owned = heads_all // lax.axis_size("head")
    offset = lax.axis_index("head") * owned
    groups = heads_all // owned
    me_head = lax.axis_index("head")
    key_part = lax.select_n(me_head, *[keys[:, b * owned : (b + 1) * owned] for b in range(groups)])
    value_part = lax.select_n(
        me_head, *[values[:, b * owned : (b + 1) * owned] for b in range(groups)]
    )
    both = head_exchange(jnp.stack([queries, dout]), owned)
    query_part, grad_part = both[0], both[1]
    key_one, key_two = sketch_parts(key_part, projector, "thd,df->htf")
    key_feat = tri_features(key_one, key_two, take_a, take_b)
    key_wfeat = key_feat * weight
    value_heads = value_part.transpose(1, 0, 2)
    block_state = jnp.einsum("htf,htd->hfd", key_feat, value_heads, preferred_element_type=f32)
    block_total = jnp.sum(key_feat, 1, dtype=f32)
    state_in, total_in = ctx_scan(block_state, block_total, False)

    query_one, query_two = sketch_parts(query_part, projector, "tmhd,df->hmtf")
    query_feat = tri_features(query_one, query_two, take_a, take_b)
    grad_heads = grad_part.transpose(2, 1, 0, 3).astype(f32)
    length = key_feat.shape[1]
    causal = lax.broadcasted_iota(jnp.int32, (length, length), 0) >= lax.broadcasted_iota(
        jnp.int32, (length, length), 1
    )
    scores = jnp.where(
        causal,
        jnp.einsum("hmif,hjf->hmij", query_feat, key_wfeat, preferred_element_type=f32),
        0.0,
    )
    weights = scores.astype(bf16)
    numerator = jnp.einsum(
        "hmij,hjd->hmid", weights, value_heads, preferred_element_type=f32
    ) + dot_split("hmif,hfd->hmid", query_feat, state_in * weight.astype(f32)[None, :, None])
    denominator = 1.0 + jnp.sum(scores, -1) + dot_split("hmif,hf->hmi", query_feat, total_in * weight.astype(f32)[None, :])
    output_rows = numerator / denominator[..., None]
    grad_rows = grad_heads / denominator[..., None]
    grad_low = grad_rows.astype(bf16)
    correction = -jnp.sum(grad_rows * output_rows, -1)
    suffix_part = jnp.einsum("hmif,hmid->hfd", query_feat, grad_low, preferred_element_type=f32)
    suffix_sum = dot_split("hmif,hmi->hf", query_feat, correction)
    suffix_got = scan_send(suffix_part, suffix_sum)

    dscores = jnp.where(
        causal,
        jnp.einsum("hmid,hjd->hmij", grad_low, value_heads, preferred_element_type=f32)
        + correction[..., None],
        0.0,
    ).astype(bf16)
    grad_hi, grad_lo = split_parts(grad_rows, 2)
    state_hi, state_lo = split_parts(state_in.transpose(0, 2, 1), 2)
    grad_qfeat = (
        jnp.einsum(
            "hmik,hkf->hmif",
            jnp.concatenate([dscores, grad_hi, grad_hi, grad_lo], axis=-1),
            jnp.concatenate([key_feat, state_hi, state_lo, state_hi], axis=1),
            preferred_element_type=f32,
        )
        + correction[..., None] * total_in[:, None, None, :]
    )
    grad_kfeat = jnp.einsum("hmij,hmif->hjf", dscores, query_feat, preferred_element_type=f32)
    grad_value = jnp.einsum("hmij,hmid->hjd", weights, grad_low, preferred_element_type=f32)
    suffix_summed = scan_sum(suffix_got, True)
    suffix_summed, grad_qfeat, grad_kfeat, grad_value = lax.optimization_barrier(
        (suffix_summed, grad_qfeat, grad_kfeat, grad_value)
    )
    merged_state, merged_total = scan_return(suffix_summed, suffix_part.shape[0], suffix_part.shape[1])
    query_grad = tri_feature_back(
        grad_qfeat, query_one, query_two, proj_wide, take_a, take_b, off
    )
    query_low = query_grad.transpose(2, 1, 0, 3).astype(bf16)
    query_low, merged_state, merged_total = lax.optimization_barrier(
        (query_low, merged_state, merged_total)
    )
    query_out = head_return(query_low, heads_all)

    merged_hi, merged_lo = split_parts(merged_state.transpose(0, 2, 1), 2)
    kfeat_total = (
        grad_kfeat
        + jnp.einsum(
            "htk,hkf->htf",
            jnp.concatenate([value_heads, value_heads], axis=-1),
            jnp.concatenate([merged_hi, merged_lo], axis=1),
            preferred_element_type=f32,
        )
        + merged_total[:, None, :]
    )
    value_total = grad_value + dot_split("htf,hfd->htd", key_wfeat, merged_state)
    key_sum = tri_feature_back(kfeat_total, key_one, key_two, proj_wide, take_a, take_b, off)
    key_out = key_sum.transpose(1, 0, 2).astype(bf16)
    value_out = value_total.transpose(1, 0, 2).astype(bf16)
    return (query_out, key_out, value_out)


def solution(mesh):
    in_specs = (
        P("ctx", "head", None, None),
        P("ctx", None, None),
        P("ctx", None, None),
        P("ctx", "head", None, None),
        P(),
    )
    out_specs = (P("ctx", "head", None, None), P("ctx", "head", None), P("ctx", "head", None))
    return jax.shard_map(body, mesh=mesh, in_specs=in_specs, out_specs=out_specs, check_vma=False)
```
